32 devices in a mesh: inv: 2 (over y), tracer: 4 (over z), band: 4 (over x, core).
Axes of the slice: x: 2, y: 2, z: 4, core: 2. Of those that a mesh axis runs over, the one named last changes fastest.
Arguments:
- tracer_state: float32 [32, 32, 48, 512], P(('inv', 'tracer'), 'band'), parts along dimension 0, may hold values from -6 to 6
- control: float32 [32, 32, 512], P(('inv', 'tracer'), 'band'), parts along dimension 0, may hold values from -6 to 6
- prior_tiles: float32 [8, 8, 8], replicated, may hold values from -1 to 1
- tile_index: int32 [4, 4], replicated, may hold values from 0 to 7, as said below
- region_map: int32 [32, 512], P('band'), may hold values from 0 to 21
- region_sigma: float32 [16, 22], P('tracer'), may hold values from 0.3 to 3
- zonal_courant: float32 [64, 48, 512], P(('inv', 'band'), None, 'tracer'), parts along dimension 0, may hold values from -0.3 to 0.3
- meridional_courant: float32 [64, 48, 512], P(('inv', 'band'), None, 'tracer'), parts along dimension 0, may hold values from -0.3 to 0.3
- vertical_diffusion: float32 [64, 48, 512], P(('inv', 'band'), None, 'tracer'), parts along dimension 0, may hold values from 0.02 to 0.2
Outputs:
- final_state: float32 [32, 32, 48, 512], P(('inv', 'tracer'), 'band'), parts along dimension 0
- emission: float32 [32, 32, 512], P(('inv', 'tracer'), 'band'), parts along dimension 0
The draws below stay inside these ranges and needn't reach their ends.
There are 2 independent parts, one for each index of `inv`. The reference program is written for one: setup_inputs(seed, part) draws one part's arguments, and reference() takes and returns one part's arrays. A program takes and returns all parts, laid end to end along the dimension named above; an argument that names none is the same for every part. Nothing has to cross between parts.
Inputs may be any that keep to these rules, and one draw needn't show every extreme that they name: `tile_index`: each entry names one of the 8 tiles; 0 and 7 both occur.
All inputs are finite; a program needn't handle non-finite values.
Results may differ from the reference program's by a relative error of at most 0.000071.
Values sent between devices are 32-bit elements; how exact they have to be, the bound alone decides.
No kernel may reach another device: no remote copies, remote signals or barrier semaphores. Data moves between devices by JAX's collectives and lax.ppermute only.
A program may use at most 128 MiB of HBM per device.

```python
import math
import jax
import jax.numpy as jnp
from jax import lax

NTR = 16
LAT_DEV = 8
NLAT = 32
BANDS = 4
LEV = 48
NLON = 512
NREG = 22
NTILE = 8
STEPS = 2


def draw_tile_index(key, part):
    drawn = jax.random.randint(jax.random.fold_in(key, 11), (BANDS, BANDS), 0, NTILE)
    drawn = drawn.at[0, 0].set(NTILE - 1)
    drawn = drawn.at[BANDS - 1, 0].set(0)
    return drawn.astype(jnp.int32)


def with_ends(values, rng, low, high):
    dims = values.shape
    place = [jax.random.randint(jax.random.fold_in(rng, axis), (), 0, dims[axis]) for axis in range(len(dims))]
    values = values.at[tuple(place)].set(low)
    longest = dims.index(max(dims))
    place[longest] = (place[longest] + 1) % dims[longest]
    return values.at[tuple(place)].set(high)


def block_scale(own_key, shape, shards, least, largest):
    def one(dim, blocks):
        draws = jax.random.uniform(jax.random.fold_in(jax.random.fold_in(own_key, 6), dim), (blocks,), jnp.float32, least / len(shards), largest / len(shards))
        return jnp.repeat(jnp.exp(draws), shape[dim] // blocks).reshape((-1,) + (1,) * (len(shape) - dim - 1))

    factor_of = one(*shards[0])
    for cut in shards[1:]:
        factor_of = factor_of * one(*cut)
    return factor_of


def normal_values(rng, dims, scale, most, pieces=(), kind=jnp.bfloat16):
    values = scale * jax.random.normal(rng, dims, jnp.float32)
    if pieces:
        values = values * block_scale(rng, dims, pieces, -0.22, 0.18)
    return jnp.clip(values, -most, most).astype(kind)


def setup_inputs(seed: int = 0, part: int = 0) -> dict:
    arg_keys = jax.random.split(jax.random.key(seed), 10)
    own_keys = jax.random.split(jax.random.fold_in(arg_keys[9], part), 10)
    return {
        "tracer_state": normal_values(own_keys[0], (NTR, NLAT, LEV, NLON), 1.0, 6.0, ((0, 4), (1, 4)), jnp.float32),
        "control": normal_values(own_keys[1], (NTR, NLAT, NLON), 1.0, 6.0, ((0, 4), (1, 4)), jnp.float32),
        "prior_tiles": normal_values(arg_keys[2], (NTILE, LAT_DEV, LAT_DEV), NLAT ** -0.5, 1.0, (), jnp.float32),
        "tile_index": draw_tile_index(jax.random.fold_in(arg_keys[9], 71), part),
        "region_map": with_ends(jax.random.randint(arg_keys[4], (NLAT, NLON), 0, NREG), jax.random.fold_in(arg_keys[4], 1), 0, NREG - 1).astype(jnp.int32),
        "region_sigma": jnp.clip(jnp.exp(math.log(3.0) - 2.3025851 * jax.random.uniform(arg_keys[5], (NTR, NREG), jnp.float32) ** block_scale(arg_keys[5], (NTR, NREG), ((0, 4),), -0.2, 0.2)), 0.3, 3.0),
        "zonal_courant": jnp.clip(jax.random.uniform(own_keys[6], (NLAT, LEV, NLON), jnp.float32, -0.3, 0.3) * block_scale(own_keys[6], (NLAT, LEV, NLON), ((0, 4), (2, 4)), -0.4, 0.0), -0.3, 0.3),
        "meridional_courant": jnp.clip(jax.random.uniform(own_keys[7], (NLAT, LEV, NLON), jnp.float32, -0.3, 0.3) * block_scale(own_keys[7], (NLAT, LEV, NLON), ((0, 4), (2, 4)), -0.4, 0.0), -0.3, 0.3),
        "vertical_diffusion": jnp.clip(jnp.exp(math.log(0.2) - 2.3025851 * jax.random.uniform(own_keys[8], (NLAT, LEV, NLON), jnp.float32) ** block_scale(own_keys[8], (NLAT, LEV, NLON), ((0, 4), (2, 4)), -0.2, 0.2)), 0.02, 0.2),
    }


exact_dot = lax.Precision.HIGHEST


def vertical_mixing(tracer_now, mixing):
    levels = tracer_now.shape[2]
    upper_level = jnp.concatenate([tracer_now[:, :, 1:], jnp.zeros_like(tracer_now[:, :, :1])], axis=2)
    open_top = (lax.broadcasted_iota(jnp.int32, (levels, 1), 0) < levels - 1).astype(jnp.float32)
    flux_up = mixing * (tracer_now - upper_level) * open_top
    flux_down = jnp.concatenate([jnp.zeros_like(flux_up[:, :, :1]), flux_up[:, :, :-1]], axis=2)
    return flux_up - flux_down


def advance(tracer_now, zonal, meridional, mixing, source, north_open):
    east_side = jnp.roll(tracer_now, -1, axis=3)
    flux_east = jnp.maximum(zonal, 0.0) * tracer_now + jnp.minimum(zonal, 0.0) * east_side
    north_side = jnp.concatenate([tracer_now[:, 1:], jnp.zeros_like(tracer_now[:, :1])], axis=1)
    flux_north = (jnp.maximum(meridional, 0.0) * tracer_now + jnp.minimum(meridional, 0.0) * north_side) * north_open
    flux_south = jnp.concatenate([jnp.zeros_like(flux_north[:, :1]), flux_north[:, :-1]], axis=1)
    result = tracer_now - (flux_east - jnp.roll(flux_east, 1, axis=3)) - (flux_north - flux_south) - vertical_mixing(tracer_now, mixing)
    return result.at[:, :, 0, :].add(source)


def reference(tracer_state, control, prior_tiles, tile_index, region_map, region_sigma, zonal_courant, meridional_courant, vertical_diffusion):
    blocks = prior_tiles[tile_index]
    root = jnp.transpose(blocks, (0, 2, 1, 3)).reshape(NLAT, NLAT)
    prior_field = jnp.einsum("ab,kbn->kan", root, control, precision=exact_dot)
    emission = region_sigma[:, region_map] * prior_field
    north_open = (lax.broadcasted_iota(jnp.int32, (NLAT, 1, 1), 0) < NLAT - 1).astype(jnp.float32)
    groups = NTR // 8
    state_groups = tracer_state.reshape(8, groups, NLAT, LEV, NLON)
    source_groups = emission.reshape(8, groups, NLAT, NLON)

    def run_group(pair):
        tracer_now, source = pair
        for substep in range(STEPS):
            tracer_now = advance(tracer_now, zonal_courant, meridional_courant, vertical_diffusion, source, north_open)
        return tracer_now

    final_state = lax.map(run_group, (state_groups, source_groups)).reshape(NTR, NLAT, LEV, NLON)
    return final_state, emission
```

```python
import functools

import jax
import jax.numpy as jnp
from jax import lax
from jax.experimental import pallas as pl
from jax.experimental.pallas import tpu as pltpu
from jax.sharding import PartitionSpec as P

STEPS = 2

exact_dot = lax.Precision.HIGHEST


def passed_along(value, axis, by):
    count = lax.axis_size(axis)
    pairs = [(i, i + by) for i in range(count) if 0 <= i + by < count]
    return lax.ppermute(value, axis, pairs)


def step_kernel(north_ref, q_ref, qs_ref, qn_ref, u_ref, v_ref, vs_ref, w_ref, src_ref, o_ref):
    lat_rows = q_ref.shape[1]
    levels, lon = q_ref.shape[2], q_ref.shape[3]
    level = lax.broadcasted_iota(jnp.int32, (levels, lon), 0)
    not_top = level < levels - 1
    not_bottom = level > 0
    bottom = level == 0
    for a in range(lat_rows):
        qa = q_ref[0, a]
        qm = qs_ref[0] if a == 0 else q_ref[0, a - 1]
        qp = qn_ref[0] if a == lat_rows - 1 else q_ref[0, a + 1]
        u = u_ref[a]
        v = v_ref[a]
        vm = vs_ref[...] if a == 0 else v_ref[a - 1]
        w = w_ref[a]
        east = pltpu.roll(qa, lon - 1, 1)
        west = pltpu.roll(qa, 1, 1)
        uw = pltpu.roll(u, 1, 1)
        flux_east = jnp.maximum(u, 0.0) * qa + jnp.minimum(u, 0.0) * east
        flux_west = jnp.maximum(uw, 0.0) * west + jnp.minimum(uw, 0.0) * qa
        flux_north = (jnp.maximum(v, 0.0) * qa + jnp.minimum(v, 0.0) * qp) * north_ref[a]
        flux_south = jnp.maximum(vm, 0.0) * qm + jnp.minimum(vm, 0.0) * qa
        upper = jnp.where(not_top, pltpu.roll(qa, levels - 1, 0), 0.0)
        flux_up = jnp.where(not_top, w * (qa - upper), 0.0)
        flux_down = jnp.where(not_bottom, pltpu.roll(flux_up, 1, 0), 0.0)
        result = qa - (flux_east - flux_west) - (flux_north - flux_south) - (flux_up - flux_down)
        source = jnp.broadcast_to(src_ref[0, a : a + 1, :], (levels, lon))
        o_ref[0, a] = result + jnp.where(bottom, source, 0.0)


def advance(state, south, north, zonal, merid, merid_south, mixing, emission, north_open):
    tracers, lat_rows, levels, lon = state.shape
    row = pl.BlockSpec((1, lat_rows, levels, lon), lambda k: (k, 0, 0, 0))
    edge = pl.BlockSpec((1, levels, lon), lambda k: (k, 0, 0))
    weather = pl.BlockSpec((lat_rows, levels, lon), lambda k: (0, 0, 0))
    return pl.pallas_call(
        step_kernel,
        grid=(tracers,),
        in_specs=[
            pl.BlockSpec(memory_space=pltpu.SMEM),
            row,
            edge,
            edge,
            weather,
            weather,
            pl.BlockSpec((levels, lon), lambda k: (0, 0)),
            weather,
            pl.BlockSpec((1, lat_rows, lon), lambda k: (k, 0, 0)),
        ],
        out_specs=row,
        out_shape=jax.ShapeDtypeStruct(state.shape, state.dtype),
    )(north_open, state, south, north, zonal, merid, merid_south, mixing, emission)


def on_device(
    tracer_state,
    control,
    prior_tiles,
    tile_index,
    region_map,
    region_sigma,
    zonal_courant,
    meridional_courant,
    vertical_diffusion,
):
    band_count = lax.axis_size("band")
    band_index = lax.axis_index("band")
    tiles_count = prior_tiles.shape[0]
    lat_rows = control.shape[1]

    south_v = passed_along(meridional_courant[-1:], "band", 1)
    q_south = passed_along(tracer_state[:, -1], "band", 1)
    q_north = passed_along(tracer_state[:, 0], "band", -1)
    shifted = [control]
    for s in range(1, band_count):
        pairs = [(i, (i + s) % band_count) for i in range(band_count)]
        shifted.append(lax.ppermute(control, "band", pairs))

    pack = jnp.concatenate([zonal_courant, meridional_courant, vertical_diffusion, south_v], axis=0)
    weather = lax.all_gather(pack, "tracer", axis=2, tiled=True)
    zonal = weather[:lat_rows]
    merid = weather[lat_rows : 2 * lat_rows]
    mixing = weather[2 * lat_rows : 3 * lat_rows]
    merid_south = weather[3 * lat_rows]

    choose = (
        tile_index[:, :, None] == lax.broadcasted_iota(jnp.int32, (1, 1, tiles_count), 2)
    ).astype(jnp.float32)
    own_row = lax.dynamic_slice_in_dim(choose, band_index, 1, 0)[0]
    row_tiles = jnp.einsum("bt,tmn->bmn", own_row, prior_tiles, precision=exact_dot)
    prior_field = None
    for s, part in enumerate(shifted):
        source_band = (band_index - s) % band_count
        tile = lax.dynamic_index_in_dim(row_tiles, source_band, 0, keepdims=False)
        term = jnp.einsum("jm,kmn->kjn", tile, part, precision=exact_dot)
        prior_field = term if prior_field is None else prior_field + term
    regions = region_sigma.shape[1]
    onehot = (region_map[:, :, None] == lax.broadcasted_iota(jnp.int32, (1, 1, regions), 2)).astype(
        jnp.float32
    )
    cell_sigma = jnp.einsum("kr,jnr->kjn", region_sigma, onehot, precision=exact_dot)
    emission = cell_sigma * prior_field

    latitude = band_index * lat_rows + jnp.arange(lat_rows, dtype=jnp.int32)
    north_open = (latitude < band_count * lat_rows - 1).astype(jnp.float32)

    tracer_field = tracer_state
    south, north = q_south, q_north
    for substep in range(STEPS):
        if substep > 0:
            south = passed_along(tracer_field[:, -1], "band", 1)
            north = passed_along(tracer_field[:, 0], "band", -1)
        tracer_field = advance(
            tracer_field, south, north, zonal, merid, merid_south, mixing, emission, north_open
        )
    return (tracer_field, emission)


def solution(mesh):
    in_specs = (
        P(("inv", "tracer"), "band", None, None),
        P(("inv", "tracer"), "band", None),
        P(),
        P(),
        P("band", None),
        P("tracer", None),
        P(("inv", "band"), None, "tracer"),
        P(("inv", "band"), None, "tracer"),
        P(("inv", "band"), None, "tracer"),
    )
    out_specs = (P(("inv", "tracer"), "band", None, None), P(("inv", "tracer"), "band", None))
    return jax.shard_map(
        on_device, mesh=mesh, in_specs=in_specs, out_specs=out_specs, check_vma=False
    )
```

```python
import jax
import jax.numpy as jnp
from jax import lax
from jax.experimental import pallas as pl
from jax.experimental.pallas import tpu as pltpu
from jax.sharding import PartitionSpec as P

exact_dot = lax.Precision.HIGHEST


def passed_along(value, axis, by):
    count = lax.axis_size(axis)
    pairs = [(i, i + by) for i in range(count) if 0 <= i + by < count]
    return lax.ppermute(value, axis, pairs)


def row_blocks(lat_rows):
    edge = max(1, lat_rows // 4)
    outer = sorted(set(range(edge)) | set(range(lat_rows - edge, lat_rows)))
    inner = [r for r in range(lat_rows) if r not in outer]
    return [outer, inner] if inner else [outer]


def merid_schedule(blocks):
    seen = set()
    plan = []
    for rows in blocks:
        fresh = []
        for r in rows:
            for need in (r - 1, r):
                if need not in seen:
                    seen.add(need)
                    fresh.append(need)
        plan.append(sorted(fresh))
    return plan


def step_rows(rows, state_loc, n_state, zonal_loc, merid_loc, mixing_loc, n_met):
    def kernel(*refs):
        north_ref = refs[0]
        state = refs[1 : 1 + n_state]
        met = refs[1 + n_state : 1 + n_state + n_met]
        src_ref = refs[1 + n_state + n_met]
        o_ref = refs[2 + n_state + n_met]

        def q_row(r):
            i, p = state_loc[r]
            return state[i][0, p]

        def met_row(loc, r):
            i, p = loc[r]
            return met[i][p]

        levels, lon = o_ref.shape[2], o_ref.shape[3]
        level = lax.broadcasted_iota(jnp.int32, (levels, lon), 0)
        not_top = level < levels - 1
        not_bottom = level > 0
        bottom = level == 0
        for out_index, a in enumerate(rows):
            qa = q_row(a)
            qm = q_row(a - 1)
            qp = q_row(a + 1)
            u = met_row(zonal_loc, a)
            v = met_row(merid_loc, a)
            vm = met_row(merid_loc, a - 1)
            w = met_row(mixing_loc, a)
            east = pltpu.roll(qa, lon - 1, 1)
            west = pltpu.roll(qa, 1, 1)
            uw = pltpu.roll(u, 1, 1)
            flux_east = jnp.maximum(u, 0.0) * qa + jnp.minimum(u, 0.0) * east
            flux_west = jnp.maximum(uw, 0.0) * west + jnp.minimum(uw, 0.0) * qa
            flux_north = (jnp.maximum(v, 0.0) * qa + jnp.minimum(v, 0.0) * qp) * north_ref[a]
            flux_south = jnp.maximum(vm, 0.0) * qm + jnp.minimum(vm, 0.0) * qa
            upper = jnp.where(not_top, pltpu.roll(qa, levels - 1, 0), 0.0)
            flux_up = jnp.where(not_top, w * (qa - upper), 0.0)
            flux_down = jnp.where(not_bottom, pltpu.roll(flux_up, 1, 0), 0.0)
            result = qa - (flux_east - flux_west) - (flux_north - flux_south) - (flux_up - flux_down)
            source = jnp.broadcast_to(src_ref[0, a : a + 1, :], (levels, lon))
            o_ref[0, out_index] = result + jnp.where(bottom, source, 0.0)

    return kernel


def advance_rows(rows, states, state_loc, mets, zonal_loc, merid_loc, mixing_loc, emission, north_open):
    tracers, lat_rows, lon = emission.shape
    levels = states[0].shape[2]
    kernel = step_rows(rows, state_loc, len(states), zonal_loc, merid_loc, mixing_loc, len(mets))
    in_specs = [pl.BlockSpec(memory_space=pltpu.SMEM)]
    in_specs += [pl.BlockSpec((1,) + s.shape[1:], lambda k: (k, 0, 0, 0)) for s in states]
    in_specs += [pl.BlockSpec(m.shape, lambda k: (0, 0, 0)) for m in mets]
    in_specs += [pl.BlockSpec((1, lat_rows, lon), lambda k: (k, 0, 0))]
    out_shape = (tracers, len(rows), levels, lon)
    return pl.pallas_call(
        kernel,
        grid=(tracers,),
        in_specs=in_specs,
        out_specs=pl.BlockSpec((1,) + out_shape[1:], lambda k: (k, 0, 0, 0)),
        out_shape=jax.ShapeDtypeStruct(out_shape, jnp.float32),
    )(north_open, *states, *mets, emission)


def on_device(
    tracer_state,
    control,
    prior_tiles,
    tile_index,
    region_map,
    region_sigma,
    zonal_courant,
    meridional_courant,
    vertical_diffusion,
):
    band_count = lax.axis_size("band")
    band_index = lax.axis_index("band")
    tiles_count = prior_tiles.shape[0]
    lat_rows = control.shape[1]

    blocks = row_blocks(lat_rows)
    v_plan = merid_schedule(blocks)

    south_v = passed_along(meridional_courant[-1:], "band", 1)
    q_south = passed_along(tracer_state[:, -1:], "band", 1)
    q_north = passed_along(tracer_state[:, :1], "band", -1)
    shifted = [control]
    for s in range(1, band_count):
        pairs = [(i, (i + s) % band_count) for i in range(band_count)]
        shifted.append(lax.ppermute(control, "band", pairs))

    mets = []
    zonal_loc, merid_loc, mixing_loc = {}, {}, {}
    for j, rows in enumerate(blocks):
        parts = []
        for r in rows:
            zonal_loc[r] = (j, len(parts))
            parts.append(zonal_courant[r : r + 1])
        for r in rows:
            mixing_loc[r] = (j, len(parts))
            parts.append(vertical_diffusion[r : r + 1])
        for r in v_plan[j]:
            merid_loc[r] = (j, len(parts))
            parts.append(south_v if r < 0 else meridional_courant[r : r + 1])
        pack = jnp.concatenate(parts, axis=0)
        mets.append(lax.all_gather(pack, "tracer", axis=2, tiled=True))

    choose = (
        tile_index[:, :, None] == lax.broadcasted_iota(jnp.int32, (1, 1, tiles_count), 2)
    ).astype(jnp.float32)
    own_row = lax.dynamic_slice_in_dim(choose, band_index, 1, 0)[0]
    row_tiles = jnp.einsum("bt,tmn->bmn", own_row, prior_tiles, precision=exact_dot)
    prior_field = None
    for s, part in enumerate(shifted):
        source_band = (band_index - s) % band_count
        tile = lax.dynamic_index_in_dim(row_tiles, source_band, 0, keepdims=False)
        term = jnp.einsum("jm,kmn->kjn", tile, part, precision=exact_dot)
        prior_field = term if prior_field is None else prior_field + term
    regions = region_sigma.shape[1]
    onehot = (region_map[:, :, None] == lax.broadcasted_iota(jnp.int32, (1, 1, regions), 2)).astype(
        jnp.float32
    )
    cell_sigma = jnp.einsum("kr,jnr->kjn", region_sigma, onehot, precision=exact_dot)
    emission = cell_sigma * prior_field

    latitude = band_index * lat_rows + jnp.arange(lat_rows, dtype=jnp.int32)
    north_open = (latitude < band_count * lat_rows - 1).astype(jnp.float32)

    first_loc = {r: (0, r) for r in range(lat_rows)}
    first_loc[-1] = (1, 0)
    first_loc[lat_rows] = (2, 0)
    first_states = [tracer_state, q_south, q_north]

    s1_blocks = []
    s1_loc = {}
    halo = None
    finals = []
    final_loc = {}

    def second(rows, pieces):
        need = set()
        for r in rows:
            need |= {r - 1, r, r + 1}
        used = sorted({s1_loc[r][0] for r in need if 0 <= r < lat_rows})
        states = [s1_blocks[i] for i in used] + list(halo)
        loc = {}
        for r in need:
            if r < 0:
                loc[r] = (len(used), 0)
            elif r >= lat_rows:
                loc[r] = (len(used) + 1, 0)
            else:
                i, p = s1_loc[r]
                loc[r] = (used.index(i), p)
        out = advance_rows(rows, states, loc, pieces, zonal_loc, merid_loc, mixing_loc, emission, north_open)
        for p, r in enumerate(rows):
            final_loc[r] = (len(finals), p)
        finals.append(out)

    done = set()
    for j, rows in enumerate(blocks):
        out = advance_rows(
            rows, first_states, first_loc, mets[: j + 1], zonal_loc, merid_loc, mixing_loc, emission, north_open
        )
        for p, r in enumerate(rows):
            s1_loc[r] = (j, p)
        s1_blocks.append(out)
        if j == 0:
            i_top, p_top = s1_loc[lat_rows - 1]
            i_bot, p_bot = s1_loc[0]
            halo = (
                passed_along(out[:, p_top : p_top + 1], "band", 1),
                passed_along(out[:, p_bot : p_bot + 1], "band", -1),
            )
        ready = [
            r
            for r in range(lat_rows)
            if r not in done and all(n < 0 or n >= lat_rows or n in s1_loc for n in (r - 1, r, r + 1))
        ]
        if ready:
            second(ready, mets[: j + 1])
            done |= set(ready)

    final_state = jnp.concatenate(
        [finals[final_loc[r][0]][:, final_loc[r][1] : final_loc[r][1] + 1] for r in range(lat_rows)], axis=1
    )
    return (final_state, emission)


def solution(mesh):
    in_specs = (
        P(("inv", "tracer"), "band", None, None),
        P(("inv", "tracer"), "band", None),
        P(),
        P(),
        P("band", None),
        P("tracer", None),
        P(("inv", "band"), None, "tracer"),
        P(("inv", "band"), None, "tracer"),
        P(("inv", "band"), None, "tracer"),
    )
    out_specs = (P(("inv", "tracer"), "band", None, None), P(("inv", "tracer"), "band", None))
    return jax.shard_map(
        on_device, mesh=mesh, in_specs=in_specs, out_specs=out_specs, check_vma=False
    )
```

```python
import jax
import jax.numpy as jnp
from jax import lax
from jax.experimental import pallas as pl
from jax.experimental.pallas import tpu as pltpu
from jax.sharding import PartitionSpec as P

exact_dot = lax.Precision.HIGHEST


def passed_along(value, axis, by):
    count = lax.axis_size(axis)
    pairs = [(i, i + by) for i in range(count) if 0 <= i + by < count]
    return lax.ppermute(value, axis, pairs)


def step_kernel(north_ref, q_ref, qs_ref, qn_ref, wx_ref, src_ref, *rest):
    o_ref = rest[0]
    edges = rest[1:-1]
    coef_ref = rest[-1]
    lat_rows = q_ref.shape[1]
    levels, lon = q_ref.shape[2], q_ref.shape[3]
    level = lax.broadcasted_iota(jnp.int32, (levels, lon), 0)
    not_top = level < levels - 1
    not_bottom = level > 0
    bottom = level == 0

    @pl.when(pl.program_id(0) == 0)
    def _():
        for a in range(lat_rows):
            u = wx_ref[a]
            uw = pltpu.roll(u, 1, 1)
            v = wx_ref[lat_rows + a] * north_ref[a]
            vm = wx_ref[3 * lat_rows] if a == 0 else wx_ref[lat_rows + a - 1]
            w = wx_ref[2 * lat_rows + a]
            w_up = jnp.where(not_top, w, 0.0)
            w_down = jnp.where(not_bottom, pltpu.roll(w, 1, 0), 0.0)
            coef_ref[0, a] = (
                1.0
                - jnp.maximum(u, 0.0)
                + jnp.minimum(uw, 0.0)
                - jnp.maximum(v, 0.0)
                + jnp.minimum(vm, 0.0)
                - w_up
                - w_down
            )
            coef_ref[1, a] = -jnp.minimum(u, 0.0)
            coef_ref[2, a] = jnp.maximum(uw, 0.0)
            coef_ref[3, a] = -jnp.minimum(v, 0.0)
            coef_ref[4, a] = jnp.maximum(vm, 0.0)
            coef_ref[5, a] = w_up
            coef_ref[6, a] = w_down

    for a in range(lat_rows):
        qa = q_ref[0, a]
        qm = qs_ref[0] if a == 0 else q_ref[0, a - 1]
        qp = qn_ref[0] if a == lat_rows - 1 else q_ref[0, a + 1]
        result = (
            coef_ref[0, a] * qa
            + coef_ref[1, a] * pltpu.roll(qa, lon - 1, 1)
            + coef_ref[2, a] * pltpu.roll(qa, 1, 1)
            + coef_ref[3, a] * qp
            + coef_ref[4, a] * qm
            + coef_ref[5, a] * pltpu.roll(qa, levels - 1, 0)
            + coef_ref[6, a] * pltpu.roll(qa, 1, 0)
        )
        source = jnp.broadcast_to(src_ref[0, a : a + 1, :], (levels, lon))
        result = result + jnp.where(bottom, source, 0.0)
        o_ref[0, a] = result
        if edges and a == 0:
            edges[0][0] = result
        if edges and a == lat_rows - 1:
            edges[1][0] = result


def advance(state, south, north, weather, emission, north_open, with_edges):
    tracers, lat_rows, levels, lon = state.shape
    row = pl.BlockSpec((1, lat_rows, levels, lon), lambda k: (k, 0, 0, 0))
    edge = pl.BlockSpec((1, levels, lon), lambda k: (k, 0, 0))
    out_specs = [row]
    out_shape = [jax.ShapeDtypeStruct(state.shape, state.dtype)]
    if with_edges:
        out_specs += [edge, edge]
        out_shape += [jax.ShapeDtypeStruct((tracers, levels, lon), state.dtype)] * 2
    grid_spec = pltpu.PrefetchScalarGridSpec(
        num_scalar_prefetch=0,
        grid=(tracers,),
        in_specs=[
            pl.BlockSpec(memory_space=pltpu.SMEM),
            row,
            edge,
            edge,
            pl.BlockSpec(weather.shape, lambda k: (0, 0, 0)),
            pl.BlockSpec((1, lat_rows, lon), lambda k: (k, 0, 0)),
        ],
        out_specs=out_specs,
        scratch_shapes=[pltpu.VMEM((7, lat_rows, levels, lon), jnp.float32)],
    )
    return pl.pallas_call(
        step_kernel,
        grid_spec=grid_spec,
        out_shape=out_shape,
        compiler_params=pltpu.CompilerParams(dimension_semantics=("arbitrary",)),
    )(north_open, state, south, north, weather, emission)


def on_device(
    tracer_state,
    control,
    prior_tiles,
    tile_index,
    region_map,
    region_sigma,
    zonal_courant,
    meridional_courant,
    vertical_diffusion,
):
    band_count = lax.axis_size("band")
    band_index = lax.axis_index("band")
    tiles_count = prior_tiles.shape[0]
    lat_rows = control.shape[1]

    south_v = passed_along(meridional_courant[-1:], "band", 1)
    q_south = passed_along(tracer_state[:, -1], "band", 1)
    q_north = passed_along(tracer_state[:, 0], "band", -1)
    shifted = [control]
    for s in range(1, band_count):
        pairs = [(i, (i + s) % band_count) for i in range(band_count)]
        shifted.append(lax.ppermute(control, "band", pairs))

    pack = jnp.concatenate([zonal_courant, meridional_courant, vertical_diffusion, south_v], axis=0)
    weather = lax.all_gather(pack, "tracer", axis=2, tiled=True)

    choose = (
        tile_index[:, :, None] == lax.broadcasted_iota(jnp.int32, (1, 1, tiles_count), 2)
    ).astype(jnp.float32)
    own_row = lax.dynamic_slice_in_dim(choose, band_index, 1, 0)[0]
    row_tiles = jnp.einsum("bt,tmn->bmn", own_row, prior_tiles, precision=exact_dot)
    prior_field = None
    for s, part in enumerate(shifted):
        source_band = (band_index - s) % band_count
        tile = lax.dynamic_index_in_dim(row_tiles, source_band, 0, keepdims=False)
        term = jnp.einsum("jm,kmn->kjn", tile, part, precision=exact_dot)
        prior_field = term if prior_field is None else prior_field + term
    regions = region_sigma.shape[1]
    onehot = (region_map[:, :, None] == lax.broadcasted_iota(jnp.int32, (1, 1, regions), 2)).astype(
        jnp.float32
    )
    cell_sigma = jnp.einsum("kr,jnr->kjn", region_sigma, onehot, precision=exact_dot)
    emission = cell_sigma * prior_field

    latitude = band_index * lat_rows + jnp.arange(lat_rows, dtype=jnp.int32)
    north_open = (latitude < band_count * lat_rows - 1).astype(jnp.float32)

    first, bottom_row, top_row = advance(
        tracer_state, q_south, q_north, weather, emission, north_open, True
    )
    s1_south = passed_along(top_row, "band", 1)
    s1_north = passed_along(bottom_row, "band", -1)
    (tracer_field,) = advance(first, s1_south, s1_north, weather, emission, north_open, False)
    return (tracer_field, emission)


def solution(mesh):
    in_specs = (
        P(("inv", "tracer"), "band", None, None),
        P(("inv", "tracer"), "band", None),
        P(),
        P(),
        P("band", None),
        P("tracer", None),
        P(("inv", "band"), None, "tracer"),
        P(("inv", "band"), None, "tracer"),
        P(("inv", "band"), None, "tracer"),
    )
    out_specs = (P(("inv", "tracer"), "band", None, None), P(("inv", "tracer"), "band", None))
    return jax.shard_map(
        on_device, mesh=mesh, in_specs=in_specs, out_specs=out_specs, check_vma=False
    )
```

```python
import jax
import jax.numpy as jnp
from jax import lax
from jax.experimental import pallas as pl
from jax.experimental.pallas import tpu as pltpu
from jax.sharding import PartitionSpec as P

exact_dot = lax.Precision.HIGHEST


def passed_along(value, axis, by):
    count = lax.axis_size(axis)
    pairs = [(i, i + by) for i in range(count) if 0 <= i + by < count]
    return lax.ppermute(value, axis, pairs)


def relay_gather(x, axis):
    count = lax.axis_size(axis)
    me = lax.axis_index(axis)
    rows, levels, width = x.shape
    buf = jnp.zeros((rows, levels, (count + 1) * width), x.dtype)
    buf = lax.dynamic_update_slice(buf, x, (0, 0, me * width))
    right = left = x
    for r in range(1, count):
        right = lax.ppermute(right, axis, [(i, i + 1) for i in range(r - 1, count - 1)])
        left = lax.ppermute(left, axis, [(j, j - 1) for j in range(1, count - r + 1)])
        slot = jnp.where(me - r >= 0, me - r, count)
        buf = lax.dynamic_update_slice(buf, right, (0, 0, slot * width))
        slot = jnp.where(me + r < count, me + r, count)
        buf = lax.dynamic_update_slice(buf, left, (0, 0, slot * width))
    return buf


def step_kernel(north_ref, q_ref, qs_ref, qn_ref, wx_ref, src_ref, *rest):
    o_ref = rest[0]
    edges = rest[1:-1]
    coef_ref = rest[-1]
    lat_rows = q_ref.shape[1]
    levels, lon = q_ref.shape[2], q_ref.shape[3]
    level = lax.broadcasted_iota(jnp.int32, (levels, lon), 0)
    not_top = level < levels - 1
    not_bottom = level > 0
    bottom = level == 0

    @pl.when(pl.program_id(0) == 0)
    def _():
        for a in range(lat_rows):
            u = wx_ref[a]
            uw = pltpu.roll(u, 1, 1)
            v = wx_ref[lat_rows + a] * north_ref[a]
            vm = wx_ref[3 * lat_rows] if a == 0 else wx_ref[lat_rows + a - 1]
            w = wx_ref[2 * lat_rows + a]
            w_up = jnp.where(not_top, w, 0.0)
            w_down = jnp.where(not_bottom, pltpu.roll(w, 1, 0), 0.0)
            coef_ref[0, a] = (
                1.0
                - jnp.maximum(u, 0.0)
                + jnp.minimum(uw, 0.0)
                - jnp.maximum(v, 0.0)
                + jnp.minimum(vm, 0.0)
                - w_up
                - w_down
            )
            coef_ref[1, a] = -jnp.minimum(u, 0.0)
            coef_ref[2, a] = jnp.maximum(uw, 0.0)
            coef_ref[3, a] = -jnp.minimum(v, 0.0)
            coef_ref[4, a] = jnp.maximum(vm, 0.0)
            coef_ref[5, a] = w_up
            coef_ref[6, a] = w_down

    for a in range(lat_rows):
        qa = q_ref[0, a]
        qm = qs_ref[0] if a == 0 else q_ref[0, a - 1]
        qp = qn_ref[0] if a == lat_rows - 1 else q_ref[0, a + 1]
        result = (
            coef_ref[0, a] * qa
            + coef_ref[1, a] * pltpu.roll(qa, lon - 1, 1)
            + coef_ref[2, a] * pltpu.roll(qa, 1, 1)
            + coef_ref[3, a] * qp
            + coef_ref[4, a] * qm
            + coef_ref[5, a] * pltpu.roll(qa, levels - 1, 0)
            + coef_ref[6, a] * pltpu.roll(qa, 1, 0)
        )
        source = jnp.broadcast_to(src_ref[0, a : a + 1, :], (levels, lon))
        result = result + jnp.where(bottom, source, 0.0)
        o_ref[0, a] = result
        if edges and a == 0:
            edges[0][0] = result
        if edges and a == lat_rows - 1:
            edges[1][0] = result


def advance(state, south, north, weather, emission, north_open, with_edges):
    tracers, lat_rows, levels, lon = state.shape
    row = pl.BlockSpec((1, lat_rows, levels, lon), lambda k: (k, 0, 0, 0))
    edge = pl.BlockSpec((1, levels, lon), lambda k: (k, 0, 0))
    out_specs = [row]
    out_shape = [jax.ShapeDtypeStruct(state.shape, state.dtype)]
    if with_edges:
        out_specs += [edge, edge]
        out_shape += [jax.ShapeDtypeStruct((tracers, levels, lon), state.dtype)] * 2
    grid_spec = pltpu.PrefetchScalarGridSpec(
        num_scalar_prefetch=0,
        grid=(tracers,),
        in_specs=[
            pl.BlockSpec(memory_space=pltpu.SMEM),
            row,
            edge,
            edge,
            pl.BlockSpec(weather.shape[:2] + (lon,), lambda k: (0, 0, 0)),
            pl.BlockSpec((1, lat_rows, lon), lambda k: (k, 0, 0)),
        ],
        out_specs=out_specs,
        scratch_shapes=[pltpu.VMEM((7, lat_rows, levels, lon), jnp.float32)],
    )
    return pl.pallas_call(
        step_kernel,
        grid_spec=grid_spec,
        out_shape=out_shape,
        compiler_params=pltpu.CompilerParams(dimension_semantics=("arbitrary",)),
    )(north_open, state, south, north, weather, emission)


def on_device(
    tracer_state,
    control,
    prior_tiles,
    tile_index,
    region_map,
    region_sigma,
    zonal_courant,
    meridional_courant,
    vertical_diffusion,
):
    band_count = lax.axis_size("band")
    band_index = lax.axis_index("band")
    tiles_count = prior_tiles.shape[0]
    lat_rows = control.shape[1]

    south_v = passed_along(meridional_courant[-1:], "band", 1)
    q_south = passed_along(tracer_state[:, -1], "band", 1)
    q_north = passed_along(tracer_state[:, 0], "band", -1)
    shifted = [control]
    for s in range(1, band_count):
        pairs = [(i, (i + s) % band_count) for i in range(band_count)]
        shifted.append(lax.ppermute(control, "band", pairs))

    pack = jnp.concatenate([zonal_courant, meridional_courant, vertical_diffusion, south_v], axis=0)
    weather = relay_gather(pack, "tracer")

    choose = (
        tile_index[:, :, None] == lax.broadcasted_iota(jnp.int32, (1, 1, tiles_count), 2)
    ).astype(jnp.float32)
    own_row = lax.dynamic_slice_in_dim(choose, band_index, 1, 0)[0]
    row_tiles = jnp.einsum("bt,tmn->bmn", own_row, prior_tiles, precision=exact_dot)
    prior_field = None
    for s, part in enumerate(shifted):
        source_band = (band_index - s) % band_count
        tile = lax.dynamic_index_in_dim(row_tiles, source_band, 0, keepdims=False)
        term = jnp.einsum("jm,kmn->kjn", tile, part, precision=exact_dot)
        prior_field = term if prior_field is None else prior_field + term
    regions = region_sigma.shape[1]
    onehot = (region_map[:, :, None] == lax.broadcasted_iota(jnp.int32, (1, 1, regions), 2)).astype(
        jnp.float32
    )
    cell_sigma = jnp.einsum("kr,jnr->kjn", region_sigma, onehot, precision=exact_dot)
    emission = cell_sigma * prior_field

    latitude = band_index * lat_rows + jnp.arange(lat_rows, dtype=jnp.int32)
    north_open = (latitude < band_count * lat_rows - 1).astype(jnp.float32)

    first, bottom_row, top_row = advance(
        tracer_state, q_south, q_north, weather, emission, north_open, True
    )
    s1_south = passed_along(top_row, "band", 1)
    s1_north = passed_along(bottom_row, "band", -1)
    (tracer_field,) = advance(first, s1_south, s1_north, weather, emission, north_open, False)
    return (tracer_field, emission)


def solution(mesh):
    in_specs = (
        P(("inv", "tracer"), "band", None, None),
        P(("inv", "tracer"), "band", None),
        P(),
        P(),
        P("band", None),
        P("tracer", None),
        P(("inv", "band"), None, "tracer"),
        P(("inv", "band"), None, "tracer"),
        P(("inv", "band"), None, "tracer"),
    )
    out_specs = (P(("inv", "tracer"), "band", None, None), P(("inv", "tracer"), "band", None))
    return jax.shard_map(
        on_device, mesh=mesh, in_specs=in_specs, out_specs=out_specs, check_vma=False
    )
```

```python
import jax
import jax.numpy as jnp
from jax import lax
from jax.experimental import pallas as pl
from jax.experimental.pallas import tpu as pltpu
from jax.sharding import PartitionSpec as P

exact_dot = lax.Precision.HIGHEST


def passed_along(value, axis, by):
    count = lax.axis_size(axis)
    pairs = [(i, i + by) for i in range(count) if 0 <= i + by < count]
    return lax.ppermute(value, axis, pairs)


def relay_gather(x, axis):
    count = lax.axis_size(axis)
    me = lax.axis_index(axis)
    rows, levels, width = x.shape
    buf = jnp.zeros((rows, levels, (count + 1) * width), x.dtype)
    buf = lax.dynamic_update_slice(buf, x, (0, 0, me * width))
    right = left = x
    for r in range(1, count):
        right = lax.ppermute(right, axis, [(i, i + 1) for i in range(r - 1, count - 1)])
        left = lax.ppermute(left, axis, [(j, j - 1) for j in range(1, count - r + 1)])
        slot = jnp.where(me - r >= 0, me - r, count)
        buf = lax.dynamic_update_slice(buf, right, (0, 0, slot * width))
        slot = jnp.where(me + r < count, me + r, count)
        buf = lax.dynamic_update_slice(buf, left, (0, 0, slot * width))
    return buf


def step_kernel(north_ref, q_ref, qs_ref, qn_ref, wx_ref, src_ref, *rest):
    o_ref = rest[0]
    edges = rest[1:-1]
    coef_ref = rest[-1]
    lat_rows = q_ref.shape[1]
    levels, lon = q_ref.shape[2], q_ref.shape[3]
    level = lax.broadcasted_iota(jnp.int32, (levels, lon), 0)
    not_top = level < levels - 1
    not_bottom = level > 0

    @pl.when(pl.program_id(0) == 0)
    def _():
        for a in range(lat_rows):
            u = wx_ref[a]
            uw = pltpu.roll(u, 1, 1)
            v = wx_ref[lat_rows + a] * north_ref[a]
            vm = wx_ref[3 * lat_rows] if a == 0 else wx_ref[lat_rows + a - 1]
            w = wx_ref[2 * lat_rows + a]
            w_up = jnp.where(not_top, w, 0.0)
            w_down = jnp.where(not_bottom, pltpu.roll(w, 1, 0), 0.0)
            coef_ref[0, a] = (
                1.0
                - jnp.maximum(u, 0.0)
                + jnp.minimum(uw, 0.0)
                - jnp.maximum(v, 0.0)
                + jnp.minimum(vm, 0.0)
                - w_up
                - w_down
            )
            coef_ref[1, a] = -jnp.minimum(u, 0.0)
            coef_ref[2, a] = jnp.maximum(uw, 0.0)
            coef_ref[3, a] = -jnp.minimum(v, 0.0)
            coef_ref[4, a] = jnp.maximum(vm, 0.0)
            coef_ref[5, a] = w_up
            coef_ref[6, a] = w_down

    for a in range(lat_rows):
        qa = q_ref[0, a]
        qm = qs_ref[0] if a == 0 else q_ref[0, a - 1]
        qp = qn_ref[0] if a == lat_rows - 1 else q_ref[0, a + 1]
        result = (
            coef_ref[0, a] * qa
            + coef_ref[1, a] * pltpu.roll(qa, lon - 1, 1)
            + coef_ref[2, a] * pltpu.roll(qa, 1, 1)
            + coef_ref[3, a] * qp
            + coef_ref[4, a] * qm
            + coef_ref[5, a] * pltpu.roll(qa, levels - 1, 0)
            + coef_ref[6, a] * pltpu.roll(qa, 1, 0)
        )
        surface = result[0:1] + src_ref[0, a : a + 1, :]
        targets = [o_ref.at[0, a]]
        if edges and a == 0:
            targets.append(edges[0].at[0])
        if edges and a == lat_rows - 1:
            targets.append(edges[1].at[0])
        for target in targets:
            target[...] = result
            target[0:1, :] = surface


def advance(state, south, north, weather, emission, north_open, with_edges):
    tracers, lat_rows, levels, lon = state.shape
    row = pl.BlockSpec((1, lat_rows, levels, lon), lambda k: (k, 0, 0, 0))
    edge = pl.BlockSpec((1, levels, lon), lambda k: (k, 0, 0))
    out_specs = [row]
    out_shape = [jax.ShapeDtypeStruct(state.shape, state.dtype)]
    if with_edges:
        out_specs += [edge, edge]
        out_shape += [jax.ShapeDtypeStruct((tracers, levels, lon), state.dtype)] * 2
    grid_spec = pltpu.PrefetchScalarGridSpec(
        num_scalar_prefetch=0,
        grid=(tracers,),
        in_specs=[
            pl.BlockSpec(memory_space=pltpu.SMEM),
            row,
            edge,
            edge,
            pl.BlockSpec(weather.shape[:2] + (lon,), lambda k: (0, 0, 0)),
            pl.BlockSpec((1, lat_rows, lon), lambda k: (k, 0, 0)),
        ],
        out_specs=out_specs,
        scratch_shapes=[pltpu.VMEM((7, lat_rows, levels, lon), jnp.float32)],
    )
    return pl.pallas_call(
        step_kernel,
        grid_spec=grid_spec,
        out_shape=out_shape,
        compiler_params=pltpu.CompilerParams(dimension_semantics=("arbitrary",)),
    )(north_open, state, south, north, weather, emission)


def on_device(
    tracer_state,
    control,
    prior_tiles,
    tile_index,
    region_map,
    region_sigma,
    zonal_courant,
    meridional_courant,
    vertical_diffusion,
):
    band_count = lax.axis_size("band")
    band_index = lax.axis_index("band")
    tiles_count = prior_tiles.shape[0]
    lat_rows = control.shape[1]

    south_v = passed_along(meridional_courant[-1:], "band", 1)
    pack = jnp.concatenate([zonal_courant, meridional_courant, vertical_diffusion, south_v], axis=0)
    weather = relay_gather(pack, "tracer")
    held_state, held_control, _ = lax.optimization_barrier((tracer_state, control, pack))
    q_south = passed_along(held_state[:, -1], "band", 1)
    q_north = passed_along(held_state[:, 0], "band", -1)
    shifted = [control]
    for s in range(1, band_count):
        pairs = [(i, (i + s) % band_count) for i in range(band_count)]
        shifted.append(lax.ppermute(held_control, "band", pairs))

    choose = (
        tile_index[:, :, None] == lax.broadcasted_iota(jnp.int32, (1, 1, tiles_count), 2)
    ).astype(jnp.float32)
    own_row = lax.dynamic_slice_in_dim(choose, band_index, 1, 0)[0]
    row_tiles = jnp.einsum("bt,tmn->bmn", own_row, prior_tiles, precision=exact_dot)
    prior_field = None
    for s, part in enumerate(shifted):
        source_band = (band_index - s) % band_count
        tile = lax.dynamic_index_in_dim(row_tiles, source_band, 0, keepdims=False)
        term = jnp.einsum("jm,kmn->kjn", tile, part, precision=exact_dot)
        prior_field = term if prior_field is None else prior_field + term
    regions = region_sigma.shape[1]
    onehot = (region_map[:, :, None] == lax.broadcasted_iota(jnp.int32, (1, 1, regions), 2)).astype(
        jnp.float32
    )
    cell_sigma = jnp.einsum("kr,jnr->kjn", region_sigma, onehot, precision=exact_dot)
    emission = cell_sigma * prior_field

    latitude = band_index * lat_rows + jnp.arange(lat_rows, dtype=jnp.int32)
    north_open = (latitude < band_count * lat_rows - 1).astype(jnp.float32)

    first, bottom_row, top_row = advance(
        tracer_state, q_south, q_north, weather, emission, north_open, True
    )
    s1_south = passed_along(top_row, "band", 1)
    s1_north = passed_along(bottom_row, "band", -1)
    (tracer_field,) = advance(first, s1_south, s1_north, weather, emission, north_open, False)
    return (tracer_field, emission)


def solution(mesh):
    in_specs = (
        P(("inv", "tracer"), "band", None, None),
        P(("inv", "tracer"), "band", None),
        P(),
        P(),
        P("band", None),
        P("tracer", None),
        P(("inv", "band"), None, "tracer"),
        P(("inv", "band"), None, "tracer"),
        P(("inv", "band"), None, "tracer"),
    )
    out_specs = (P(("inv", "tracer"), "band", None, None), P(("inv", "tracer"), "band", None))
    return jax.shard_map(
        on_device, mesh=mesh, in_specs=in_specs, out_specs=out_specs, check_vma=False
    )
```

```python
import jax
import jax.numpy as jnp
from jax import lax
from jax.experimental import pallas as pl
from jax.experimental.pallas import tpu as pltpu
from jax.sharding import PartitionSpec as P

exact_dot = lax.Precision.HIGHEST


def passed_along(value, axis, by):
    count = lax.axis_size(axis)
    pairs = [(i, i + by) for i in range(count) if 0 <= i + by < count]
    return lax.ppermute(value, axis, pairs)


def pack_kernel(*refs):
    parts, out_ref, sems = refs[:-2], refs[-2], refs[-1]
    copies = []
    row = 0
    for i, part in enumerate(parts):
        rows = part.shape[0]
        copies.append(pltpu.make_async_copy(part, out_ref.at[pl.ds(row, rows)], sems.at[i]))
        row += rows
    for copy in copies:
        copy.start()
    for copy in copies:
        copy.wait()


def packed(parts):
    rows = sum(part.shape[0] for part in parts)
    return pl.pallas_call(
        pack_kernel,
        in_specs=[pl.BlockSpec(memory_space=pl.ANY)] * len(parts),
        out_specs=pl.BlockSpec(memory_space=pl.ANY),
        out_shape=jax.ShapeDtypeStruct((rows,) + parts[0].shape[1:], parts[0].dtype),
        scratch_shapes=[pltpu.SemaphoreType.DMA((len(parts),))],
    )(*parts)


def relay_gather(x, axis, hold, release_round):
    count = lax.axis_size(axis)
    me = lax.axis_index(axis)
    rows, levels, width = x.shape
    buf = jnp.zeros((rows, levels, (count + 1) * width), x.dtype)
    buf = lax.dynamic_update_slice(buf, x, (0, 0, me * width))
    right = left = x
    for r in range(1, count):
        right = lax.ppermute(right, axis, [(i, i + 1) for i in range(r - 1, count - 1)])
        left = lax.ppermute(left, axis, [(j, j - 1) for j in range(1, count - r + 1)])
        if r == min(release_round, count - 1):
            hold, right, left = lax.optimization_barrier((hold, right, left))
        slot = jnp.where(me - r >= 0, me - r, count)
        buf = lax.dynamic_update_slice(buf, right, (0, 0, slot * width))
        slot = jnp.where(me + r < count, me + r, count)
        buf = lax.dynamic_update_slice(buf, left, (0, 0, slot * width))
    if count == 1:
        hold = lax.optimization_barrier(hold)
    return buf, hold


def step_kernel(north_ref, q_ref, qs_ref, qn_ref, wx_ref, src_ref, *rest):
    o_ref = rest[0]
    edges = rest[1:-1]
    coef_ref = rest[-1]
    lat_rows = q_ref.shape[1]
    levels, lon = q_ref.shape[2], q_ref.shape[3]
    level = lax.broadcasted_iota(jnp.int32, (levels, lon), 0)
    not_top = level < levels - 1
    not_bottom = level > 0

    @pl.when(pl.program_id(0) == 0)
    def _():
        for a in range(lat_rows):
            u = wx_ref[a]
            uw = pltpu.roll(u, 1, 1)
            v = wx_ref[lat_rows + a] * north_ref[a]
            vm = wx_ref[3 * lat_rows] if a == 0 else wx_ref[lat_rows + a - 1]
            w = wx_ref[2 * lat_rows + a]
            w_up = jnp.where(not_top, w, 0.0)
            w_down = jnp.where(not_bottom, pltpu.roll(w, 1, 0), 0.0)
            coef_ref[0, a] = (
                1.0
                - jnp.maximum(u, 0.0)
                + jnp.minimum(uw, 0.0)
                - jnp.maximum(v, 0.0)
                + jnp.minimum(vm, 0.0)
                - w_up
                - w_down
            )
            coef_ref[1, a] = -jnp.minimum(u, 0.0)
            coef_ref[2, a] = jnp.maximum(uw, 0.0)
            coef_ref[3, a] = -jnp.minimum(v, 0.0)
            coef_ref[4, a] = jnp.maximum(vm, 0.0)
            coef_ref[5, a] = w_up
            coef_ref[6, a] = w_down

    for a in range(lat_rows):
        qa = q_ref[0, a]
        qm = qs_ref[0] if a == 0 else q_ref[0, a - 1]
        qp = qn_ref[0] if a == lat_rows - 1 else q_ref[0, a + 1]
        result = (
            coef_ref[0, a] * qa
            + coef_ref[1, a] * pltpu.roll(qa, lon - 1, 1)
            + coef_ref[2, a] * pltpu.roll(qa, 1, 1)
            + coef_ref[3, a] * qp
            + coef_ref[4, a] * qm
            + coef_ref[5, a] * pltpu.roll(qa, levels - 1, 0)
            + coef_ref[6, a] * pltpu.roll(qa, 1, 0)
        )
        surface = result[0:1] + src_ref[0, a : a + 1, :]
        targets = [o_ref.at[0, a]]
        if edges and a == 0:
            targets.append(edges[0].at[0])
        if edges and a == lat_rows - 1:
            targets.append(edges[1].at[0])
        for target in targets:
            target[...] = result
            target[0:1, :] = surface


def advance(state, south, north, weather, emission, north_open, with_edges):
    tracers, lat_rows, levels, lon = state.shape
    row = pl.BlockSpec((1, lat_rows, levels, lon), lambda k: (k, 0, 0, 0))
    edge = pl.BlockSpec((1, levels, lon), lambda k: (k, 0, 0))
    out_specs = [row]
    out_shape = [jax.ShapeDtypeStruct(state.shape, state.dtype)]
    if with_edges:
        out_specs += [edge, edge]
        out_shape += [jax.ShapeDtypeStruct((tracers, levels, lon), state.dtype)] * 2
    grid_spec = pltpu.PrefetchScalarGridSpec(
        num_scalar_prefetch=0,
        grid=(tracers,),
        in_specs=[
            pl.BlockSpec(memory_space=pltpu.SMEM),
            row,
            edge,
            edge,
            pl.BlockSpec(weather.shape[:2] + (lon,), lambda k: (0, 0, 0)),
            pl.BlockSpec((1, lat_rows, lon), lambda k: (k, 0, 0)),
        ],
        out_specs=out_specs,
        scratch_shapes=[pltpu.VMEM((7, lat_rows, levels, lon), jnp.float32)],
    )
    return pl.pallas_call(
        step_kernel,
        grid_spec=grid_spec,
        out_shape=out_shape,
        compiler_params=pltpu.CompilerParams(dimension_semantics=("arbitrary",)),
    )(north_open, state, south, north, weather, emission)


def on_device(
    tracer_state,
    control,
    prior_tiles,
    tile_index,
    region_map,
    region_sigma,
    zonal_courant,
    meridional_courant,
    vertical_diffusion,
):
    band_count = lax.axis_size("band")
    band_index = lax.axis_index("band")
    tiles_count = prior_tiles.shape[0]
    lat_rows = control.shape[1]

    south_v = passed_along(meridional_courant[-1:], "band", 1)
    pack = packed([zonal_courant, meridional_courant, vertical_diffusion, south_v])
    weather, held = relay_gather(
        pack, "tracer", (tracer_state, control, prior_tiles, tile_index, region_map, region_sigma), 2
    )
    tracer_state, control, prior_tiles, tile_index, region_map, region_sigma = held
    q_south = passed_along(tracer_state[:, -1], "band", 1)
    q_north = passed_along(tracer_state[:, 0], "band", -1)
    shifted = [control]
    for s in range(1, band_count):
        pairs = [(i, (i + s) % band_count) for i in range(band_count)]
        shifted.append(lax.ppermute(control, "band", pairs))

    choose = (
        tile_index[:, :, None] == lax.broadcasted_iota(jnp.int32, (1, 1, tiles_count), 2)
    ).astype(jnp.float32)
    own_row = lax.dynamic_slice_in_dim(choose, band_index, 1, 0)[0]
    row_tiles = jnp.einsum("bt,tmn->bmn", own_row, prior_tiles, precision=exact_dot)
    prior_field = None
    for s, part in enumerate(shifted):
        source_band = (band_index - s) % band_count
        tile = lax.dynamic_index_in_dim(row_tiles, source_band, 0, keepdims=False)
        term = jnp.einsum("jm,kmn->kjn", tile, part, precision=exact_dot)
        prior_field = term if prior_field is None else prior_field + term
    regions = region_sigma.shape[1]
    onehot = (region_map[:, :, None] == lax.broadcasted_iota(jnp.int32, (1, 1, regions), 2)).astype(
        jnp.float32
    )
    cell_sigma = jnp.einsum("kr,jnr->kjn", region_sigma, onehot, precision=exact_dot)
    emission = cell_sigma * prior_field

    latitude = band_index * lat_rows + jnp.arange(lat_rows, dtype=jnp.int32)
    north_open = (latitude < band_count * lat_rows - 1).astype(jnp.float32)

    first, bottom_row, top_row = advance(
        tracer_state, q_south, q_north, weather, emission, north_open, True
    )
    s1_south = passed_along(top_row, "band", 1)
    s1_north = passed_along(bottom_row, "band", -1)
    (tracer_field,) = advance(first, s1_south, s1_north, weather, emission, north_open, False)
    return (tracer_field, emission)


def solution(mesh):
    in_specs = (
        P(("inv", "tracer"), "band", None, None),
        P(("inv", "tracer"), "band", None),
        P(),
        P(),
        P("band", None),
        P("tracer", None),
        P(("inv", "band"), None, "tracer"),
        P(("inv", "band"), None, "tracer"),
        P(("inv", "band"), None, "tracer"),
    )
    out_specs = (P(("inv", "tracer"), "band", None, None), P(("inv", "tracer"), "band", None))
    return jax.shard_map(
        on_device, mesh=mesh, in_specs=in_specs, out_specs=out_specs, check_vma=False
    )
```

```python
import functools

import jax
import jax.numpy as jnp
from jax import lax
from jax.experimental import pallas as pl
from jax.experimental.pallas import tpu as pltpu
from jax.sharding import PartitionSpec as P

exact_dot = lax.Precision.HIGHEST


def passed_along(value, axis, by):
    count = lax.axis_size(axis)
    pairs = [(i, i + by) for i in range(count) if 0 <= i + by < count]
    return lax.ppermute(value, axis, pairs)


def relay_gather(x, axis):
    count = lax.axis_size(axis)
    me = lax.axis_index(axis)
    rows, levels, width = x.shape
    buf = jnp.zeros((rows, levels, (count + 1) * width), x.dtype)
    buf = lax.dynamic_update_slice(buf, x, (0, 0, me * width))
    right = left = x
    for r in range(1, count):
        right = lax.ppermute(right, axis, [(i, i + 1) for i in range(r - 1, count - 1)])
        left = lax.ppermute(left, axis, [(j, j - 1) for j in range(1, count - r + 1)])
        slot = jnp.where(me - r >= 0, me - r, count)
        buf = lax.dynamic_update_slice(buf, right, (0, 0, slot * width))
        slot = jnp.where(me + r < count, me + r, count)
        buf = lax.dynamic_update_slice(buf, left, (0, 0, slot * width))
    return buf


def step_kernel(north_ref, q_ref, qs_ref, qn_ref, wx_ref, src_ref, *rest, rows=None):
    o_ref = rest[0]
    edges = rest[1:-1]
    coef_ref = rest[-1]
    lat_rows = q_ref.shape[1]
    rows = range(lat_rows) if rows is None else rows
    levels, lon = q_ref.shape[2], q_ref.shape[3]
    level = lax.broadcasted_iota(jnp.int32, (levels, lon), 0)
    not_top = level < levels - 1
    not_bottom = level > 0

    @pl.when(pl.program_id(0) == 0)
    def _():
        for a in range(lat_rows):
            u = wx_ref[a]
            uw = pltpu.roll(u, 1, 1)
            v = wx_ref[lat_rows + a] * north_ref[a]
            vm = wx_ref[3 * lat_rows] if a == 0 else wx_ref[lat_rows + a - 1]
            w = wx_ref[2 * lat_rows + a]
            w_up = jnp.where(not_top, w, 0.0)
            w_down = jnp.where(not_bottom, pltpu.roll(w, 1, 0), 0.0)
            coef_ref[0, a] = (
                1.0
                - jnp.maximum(u, 0.0)
                + jnp.minimum(uw, 0.0)
                - jnp.maximum(v, 0.0)
                + jnp.minimum(vm, 0.0)
                - w_up
                - w_down
            )
            coef_ref[1, a] = -jnp.minimum(u, 0.0)
            coef_ref[2, a] = jnp.maximum(uw, 0.0)
            coef_ref[3, a] = -jnp.minimum(v, 0.0)
            coef_ref[4, a] = jnp.maximum(vm, 0.0)
            coef_ref[5, a] = w_up
            coef_ref[6, a] = w_down

    for a in rows:
        qa = q_ref[0, a]
        qm = qs_ref[0] if a == 0 else q_ref[0, a - 1]
        qp = qn_ref[0] if a == lat_rows - 1 else q_ref[0, a + 1]
        result = (
            coef_ref[0, a] * qa
            + coef_ref[1, a] * pltpu.roll(qa, lon - 1, 1)
            + coef_ref[2, a] * pltpu.roll(qa, 1, 1)
            + coef_ref[3, a] * qp
            + coef_ref[4, a] * qm
            + coef_ref[5, a] * pltpu.roll(qa, levels - 1, 0)
            + coef_ref[6, a] * pltpu.roll(qa, 1, 0)
        )
        surface = result[0:1] + src_ref[0, a : a + 1, :]
        targets = [o_ref.at[0, a]]
        if edges and a == 0:
            targets.append(edges[0].at[0])
        if edges and a == lat_rows - 1:
            targets.append(edges[1].at[0])
        for target in targets:
            target[...] = result
            target[0:1, :] = surface


def advance(state, south, north, weather, emission, north_open, with_edges):
    tracers, lat_rows, levels, lon = state.shape
    row = pl.BlockSpec((1, lat_rows, levels, lon), lambda k: (k, 0, 0, 0))
    edge = pl.BlockSpec((1, levels, lon), lambda k: (k, 0, 0))
    out_specs = [row]
    out_shape = [jax.ShapeDtypeStruct(state.shape, state.dtype)]
    if with_edges:
        out_specs += [edge, edge]
        out_shape += [jax.ShapeDtypeStruct((tracers, levels, lon), state.dtype)] * 2
    grid_spec = pltpu.PrefetchScalarGridSpec(
        num_scalar_prefetch=0,
        grid=(tracers,),
        in_specs=[
            pl.BlockSpec(memory_space=pltpu.SMEM),
            row,
            edge,
            edge,
            pl.BlockSpec(weather.shape[:2] + (lon,), lambda k: (0, 0, 0)),
            pl.BlockSpec((1, lat_rows, lon), lambda k: (k, 0, 0)),
        ],
        out_specs=out_specs,
        scratch_shapes=[pltpu.VMEM((7, lat_rows, levels, lon), jnp.float32)],
    )
    return pl.pallas_call(
        step_kernel,
        grid_spec=grid_spec,
        out_shape=out_shape,
        compiler_params=pltpu.CompilerParams(dimension_semantics=("arbitrary",)),
    )(north_open, state, south, north, weather, emission)


def interior_step(state, weather, emission, north_open):
    tracers, lat_rows, levels, lon = state.shape
    row = pl.BlockSpec((1, lat_rows, levels, lon), lambda k: (k, 0, 0, 0))
    kernel = functools.partial(
        lambda n, q, w, e, o, c, rows: step_kernel(n, q, None, None, w, e, o, c, rows=rows),
        rows=range(1, lat_rows - 1),
    )
    grid_spec = pltpu.PrefetchScalarGridSpec(
        num_scalar_prefetch=0,
        grid=(tracers,),
        in_specs=[
            pl.BlockSpec(memory_space=pltpu.SMEM),
            row,
            pl.BlockSpec(weather.shape[:2] + (lon,), lambda k: (0, 0, 0)),
            pl.BlockSpec((1, lat_rows, lon), lambda k: (k, 0, 0)),
        ],
        out_specs=row,
        scratch_shapes=[pltpu.VMEM((7, lat_rows, levels, lon), jnp.float32)],
    )
    return pl.pallas_call(
        kernel,
        grid_spec=grid_spec,
        out_shape=jax.ShapeDtypeStruct(state.shape, state.dtype),
        compiler_params=pltpu.CompilerParams(dimension_semantics=("arbitrary",)),
    )(north_open, state, weather, emission)


def edge_kernel(north_ref, qa_ref, qi_ref, qs_ref, qn_ref, u_ref, v_ref, vm_ref, w_ref, src_ref, base_ref, o_ref):
    del base_ref
    lat_rows = src_ref.shape[1]
    levels, lon = qa_ref.shape[2], qa_ref.shape[3]
    top = pl.program_id(1)
    level = lax.broadcasted_iota(jnp.int32, (levels, lon), 0)
    not_top = level < levels - 1
    not_bottom = level > 0
    a = top * (lat_rows - 1)
    qa = qa_ref[0, 0]
    inner = qi_ref[0, 0]
    is_top = jnp.full((levels, lon), top, jnp.int32) == 1
    qm = jnp.where(is_top, inner, qs_ref[0])
    qp = jnp.where(is_top, qn_ref[0], inner)
    u = u_ref[0]
    uw = pltpu.roll(u, 1, 1)
    v = v_ref[0] * north_ref[a]
    vm = vm_ref[0]
    w = w_ref[0]
    w_up = jnp.where(not_top, w, 0.0)
    w_down = jnp.where(not_bottom, pltpu.roll(w, 1, 0), 0.0)
    c_self = (
        1.0
        - jnp.maximum(u, 0.0)
        + jnp.minimum(uw, 0.0)
        - jnp.maximum(v, 0.0)
        + jnp.minimum(vm, 0.0)
        - w_up
        - w_down
    )
    result = (
        c_self * qa
        + (-jnp.minimum(u, 0.0)) * pltpu.roll(qa, lon - 1, 1)
        + jnp.maximum(uw, 0.0) * pltpu.roll(qa, 1, 1)
        + (-jnp.minimum(v, 0.0)) * qp
        + jnp.maximum(vm, 0.0) * qm
        + w_up * pltpu.roll(qa, levels - 1, 0)
        + w_down * pltpu.roll(qa, 1, 0)
    )
    first_row = src_ref[0, 0:1, :]
    last_row = src_ref[0, lat_rows - 1 : lat_rows, :]
    source = jnp.where(jnp.full((1, lon), top, jnp.int32) == 1, last_row, first_row)
    o_ref[0, 0] = result
    o_ref[0, 0, 0:1, :] = result[0:1] + source


def edge_step(state, base, south, north, weather, emission, north_open):
    tracers, lat_rows, levels, lon = state.shape
    last = lat_rows - 1
    one = lambda index: pl.BlockSpec((1, 1, levels, lon), index)
    edge = pl.BlockSpec((1, levels, lon), lambda k, e: (k, 0, 0))
    met = lambda index: pl.BlockSpec((1, levels, lon), index)
    grid_spec = pltpu.PrefetchScalarGridSpec(
        num_scalar_prefetch=0,
        grid=(tracers, 2),
        in_specs=[
            pl.BlockSpec(memory_space=pltpu.SMEM),
            one(lambda k, e: (k, e * last, 0, 0)),
            one(lambda k, e: (k, 1 + e * (lat_rows - 3), 0, 0)),
            edge,
            edge,
            met(lambda k, e: (e * last, 0, 0)),
            met(lambda k, e: (lat_rows + e * last, 0, 0)),
            met(lambda k, e: (3 * lat_rows - e * (lat_rows + 2), 0, 0)),
            met(lambda k, e: (2 * lat_rows + e * last, 0, 0)),
            pl.BlockSpec((1, lat_rows, lon), lambda k, e: (k, 0, 0)),
            pl.BlockSpec(memory_space=pl.ANY),
        ],
        out_specs=one(lambda k, e: (k, e * last, 0, 0)),
    )
    return pl.pallas_call(
        edge_kernel,
        grid_spec=grid_spec,
        out_shape=jax.ShapeDtypeStruct(state.shape, state.dtype),
        input_output_aliases={10: 0},
        compiler_params=pltpu.CompilerParams(dimension_semantics=("arbitrary", "arbitrary")),
    )(north_open, state, state, south, north, weather, weather, weather, weather, emission, base)


def on_device(
    tracer_state,
    control,
    prior_tiles,
    tile_index,
    region_map,
    region_sigma,
    zonal_courant,
    meridional_courant,
    vertical_diffusion,
):
    band_count = lax.axis_size("band")
    band_index = lax.axis_index("band")
    tiles_count = prior_tiles.shape[0]
    lat_rows = control.shape[1]

    south_v = passed_along(meridional_courant[-1:], "band", 1)
    pack = jnp.concatenate([zonal_courant, meridional_courant, vertical_diffusion, south_v], axis=0)
    weather = relay_gather(pack, "tracer")
    held_state, held_control, _ = lax.optimization_barrier((tracer_state, control, pack))
    q_south = passed_along(held_state[:, -1], "band", 1)
    q_north = passed_along(held_state[:, 0], "band", -1)
    shifted = [control]
    for s in range(1, band_count):
        pairs = [(i, (i + s) % band_count) for i in range(band_count)]
        shifted.append(lax.ppermute(held_control, "band", pairs))

    choose = (
        tile_index[:, :, None] == lax.broadcasted_iota(jnp.int32, (1, 1, tiles_count), 2)
    ).astype(jnp.float32)
    own_row = lax.dynamic_slice_in_dim(choose, band_index, 1, 0)[0]
    row_tiles = jnp.einsum("bt,tmn->bmn", own_row, prior_tiles, precision=exact_dot)
    prior_field = None
    for s, part in enumerate(shifted):
        source_band = (band_index - s) % band_count
        tile = lax.dynamic_index_in_dim(row_tiles, source_band, 0, keepdims=False)
        term = jnp.einsum("jm,kmn->kjn", tile, part, precision=exact_dot)
        prior_field = term if prior_field is None else prior_field + term
    regions = region_sigma.shape[1]
    onehot = (region_map[:, :, None] == lax.broadcasted_iota(jnp.int32, (1, 1, regions), 2)).astype(
        jnp.float32
    )
    cell_sigma = jnp.einsum("kr,jnr->kjn", region_sigma, onehot, precision=exact_dot)
    emission = cell_sigma * prior_field

    latitude = band_index * lat_rows + jnp.arange(lat_rows, dtype=jnp.int32)
    north_open = (latitude < band_count * lat_rows - 1).astype(jnp.float32)

    first, bottom_row, top_row = advance(
        tracer_state, q_south, q_north, weather, emission, north_open, True
    )
    s1_south = passed_along(top_row, "band", 1)
    s1_north = passed_along(bottom_row, "band", -1)
    inside = interior_step(first, weather, emission, north_open)
    tracer_field = edge_step(first, inside, s1_south, s1_north, weather, emission, north_open)
    return (tracer_field, emission)


def solution(mesh):
    in_specs = (
        P(("inv", "tracer"), "band", None, None),
        P(("inv", "tracer"), "band", None),
        P(),
        P(),
        P("band", None),
        P("tracer", None),
        P(("inv", "band"), None, "tracer"),
        P(("inv", "band"), None, "tracer"),
        P(("inv", "band"), None, "tracer"),
    )
    out_specs = (P(("inv", "tracer"), "band", None, None), P(("inv", "tracer"), "band", None))
    return jax.shard_map(
        on_device, mesh=mesh, in_specs=in_specs, out_specs=out_specs, check_vma=False
    )
```

```python
import functools

import jax
import jax.numpy as jnp
from jax import lax
from jax.experimental import pallas as pl
from jax.experimental.pallas import tpu as pltpu
from jax.sharding import PartitionSpec as P

exact_dot = lax.Precision.HIGHEST


def passed_along(value, axis, by):
    count = lax.axis_size(axis)
    pairs = [(i, i + by) for i in range(count) if 0 <= i + by < count]
    return lax.ppermute(value, axis, pairs)


def relay_gather(x, axis):
    count = lax.axis_size(axis)
    me = lax.axis_index(axis)
    rows, levels, width = x.shape
    buf = jnp.zeros((rows, levels, (count + 1) * width), x.dtype)
    buf = lax.dynamic_update_slice(buf, x, (0, 0, me * width))
    right = left = x
    for r in range(1, count):
        right = lax.ppermute(right, axis, [(i, i + 1) for i in range(r - 1, count - 1)])
        left = lax.ppermute(left, axis, [(j, j - 1) for j in range(1, count - r + 1)])
        slot = jnp.where(me - r >= 0, me - r, count)
        buf = lax.dynamic_update_slice(buf, right, (0, 0, slot * width))
        slot = jnp.where(me + r < count, me + r, count)
        buf = lax.dynamic_update_slice(buf, left, (0, 0, slot * width))
    return buf


def step_kernel(north_ref, q_ref, qs_ref, qn_ref, wx_ref, src_ref, *rest, rows=None):
    o_ref = rest[0]
    edges = rest[1:-1]
    coef_ref = rest[-1]
    lat_rows = q_ref.shape[1]
    rows = range(lat_rows) if rows is None else rows
    levels, lon = q_ref.shape[2], q_ref.shape[3]
    level = lax.broadcasted_iota(jnp.int32, (levels, lon), 0)
    not_top = level < levels - 1
    not_bottom = level > 0

    @pl.when(pl.program_id(0) == 0)
    def _():
        for a in range(lat_rows):
            u = wx_ref[a]
            uw = pltpu.roll(u, 1, 1)
            v = wx_ref[lat_rows + a] * north_ref[a]
            vm = wx_ref[3 * lat_rows] if a == 0 else wx_ref[lat_rows + a - 1]
            w = wx_ref[2 * lat_rows + a]
            w_up = jnp.where(not_top, w, 0.0)
            w_down = jnp.where(not_bottom, pltpu.roll(w, 1, 0), 0.0)
            coef_ref[0, a] = (
                1.0
                - jnp.maximum(u, 0.0)
                + jnp.minimum(uw, 0.0)
                - jnp.maximum(v, 0.0)
                + jnp.minimum(vm, 0.0)
                - w_up
                - w_down
            )
            coef_ref[1, a] = -jnp.minimum(u, 0.0)
            coef_ref[2, a] = jnp.maximum(uw, 0.0)
            coef_ref[3, a] = -jnp.minimum(v, 0.0)
            coef_ref[4, a] = jnp.maximum(vm, 0.0)
            coef_ref[5, a] = w_up
            coef_ref[6, a] = w_down

    for a in rows:
        qa = q_ref[0, a]
        qm = qs_ref[0] if a == 0 else q_ref[0, a - 1]
        qp = qn_ref[0] if a == lat_rows - 1 else q_ref[0, a + 1]
        result = (
            coef_ref[0, a] * qa
            + coef_ref[1, a] * pltpu.roll(qa, lon - 1, 1)
            + coef_ref[2, a] * pltpu.roll(qa, 1, 1)
            + coef_ref[3, a] * qp
            + coef_ref[4, a] * qm
            + coef_ref[5, a] * pltpu.roll(qa, levels - 1, 0)
            + coef_ref[6, a] * pltpu.roll(qa, 1, 0)
        )
        surface = result[0:1] + src_ref[0, a : a + 1, :]
        targets = [o_ref.at[0, a]]
        if edges and a == 0:
            targets.append(edges[0].at[0])
        if edges and a == lat_rows - 1:
            targets.append(edges[1].at[0])
        for target in targets:
            target[...] = result
            target[0:1, :] = surface


def advance(state, south, north, weather, emission, north_open, with_edges):
    tracers, lat_rows, levels, lon = state.shape
    row = pl.BlockSpec((1, lat_rows, levels, lon), lambda k: (k, 0, 0, 0))
    edge = pl.BlockSpec((1, levels, lon), lambda k: (k, 0, 0))
    out_specs = [row]
    out_shape = [jax.ShapeDtypeStruct(state.shape, state.dtype)]
    if with_edges:
        out_specs += [edge, edge]
        out_shape += [jax.ShapeDtypeStruct((tracers, levels, lon), state.dtype)] * 2
    grid_spec = pltpu.PrefetchScalarGridSpec(
        num_scalar_prefetch=0,
        grid=(tracers,),
        in_specs=[
            pl.BlockSpec(memory_space=pltpu.SMEM),
            row,
            edge,
            edge,
            pl.BlockSpec(weather.shape[:2] + (lon,), lambda k: (0, 0, 0)),
            pl.BlockSpec((1, lat_rows, lon), lambda k: (k, 0, 0)),
        ],
        out_specs=out_specs,
        scratch_shapes=[pltpu.VMEM((7, lat_rows, levels, lon), jnp.float32)],
    )
    return pl.pallas_call(
        step_kernel,
        grid_spec=grid_spec,
        out_shape=out_shape,
        compiler_params=pltpu.CompilerParams(dimension_semantics=("arbitrary",)),
    )(north_open, state, south, north, weather, emission)


def interior_step(state, weather, emission, north_open):
    tracers, lat_rows, levels, lon = state.shape
    row = pl.BlockSpec((1, lat_rows, levels, lon), lambda k: (k, 0, 0, 0))
    kernel = functools.partial(
        lambda n, q, w, e, o, c, rows: step_kernel(n, q, None, None, w, e, o, c, rows=rows),
        rows=range(1, lat_rows - 1),
    )
    grid_spec = pltpu.PrefetchScalarGridSpec(
        num_scalar_prefetch=0,
        grid=(tracers,),
        in_specs=[
            pl.BlockSpec(memory_space=pltpu.SMEM),
            row,
            pl.BlockSpec(weather.shape[:2] + (lon,), lambda k: (0, 0, 0)),
            pl.BlockSpec((1, lat_rows, lon), lambda k: (k, 0, 0)),
        ],
        out_specs=row,
        scratch_shapes=[pltpu.VMEM((7, lat_rows, levels, lon), jnp.float32)],
    )
    return pl.pallas_call(
        kernel,
        grid_spec=grid_spec,
        out_shape=jax.ShapeDtypeStruct(state.shape, state.dtype),
        compiler_params=pltpu.CompilerParams(dimension_semantics=("arbitrary",)),
    )(north_open, state, weather, emission)


def edge_kernel(north_ref, qa_ref, qi_ref, qs_ref, qn_ref, u_ref, v_ref, vm_ref, w_ref, src_ref, base_ref, o_ref):
    del base_ref
    tracers, lat_rows = src_ref.shape[0], src_ref.shape[1]
    levels, lon = qa_ref.shape[2], qa_ref.shape[3]
    top = pl.program_id(0)
    level = lax.broadcasted_iota(jnp.int32, (levels, lon), 0)
    not_top = level < levels - 1
    not_bottom = level > 0
    a = top * (lat_rows - 1)
    is_top = jnp.full((levels, lon), top, jnp.int32) == 1
    u = u_ref[0]
    uw = pltpu.roll(u, 1, 1)
    v = v_ref[0] * north_ref[a]
    vm = vm_ref[0]
    w = w_ref[0]
    w_up = jnp.where(not_top, w, 0.0)
    w_down = jnp.where(not_bottom, pltpu.roll(w, 1, 0), 0.0)
    c_self = (
        1.0
        - jnp.maximum(u, 0.0)
        + jnp.minimum(uw, 0.0)
        - jnp.maximum(v, 0.0)
        + jnp.minimum(vm, 0.0)
        - w_up
        - w_down
    )
    c_east = -jnp.minimum(u, 0.0)
    c_west = jnp.maximum(uw, 0.0)
    c_north = -jnp.minimum(v, 0.0)
    c_south = jnp.maximum(vm, 0.0)
    at_top = jnp.full((1, lon), top, jnp.int32) == 1
    for k in range(tracers):
        qa = qa_ref[k, 0]
        inner = qi_ref[k, 0]
        qm = jnp.where(is_top, inner, qs_ref[k])
        qp = jnp.where(is_top, qn_ref[k], inner)
        result = (
            c_self * qa
            + c_east * pltpu.roll(qa, lon - 1, 1)
            + c_west * pltpu.roll(qa, 1, 1)
            + c_north * qp
            + c_south * qm
            + w_up * pltpu.roll(qa, levels - 1, 0)
            + w_down * pltpu.roll(qa, 1, 0)
        )
        source = jnp.where(at_top, src_ref[k, lat_rows - 1 : lat_rows, :], src_ref[k, 0:1, :])
        o_ref[k, 0] = result
        o_ref[k, 0, 0:1, :] = result[0:1] + source


def edge_step(state, base, south, north, weather, emission, north_open):
    tracers, lat_rows, levels, lon = state.shape
    last = lat_rows - 1
    one = lambda index: pl.BlockSpec((tracers, 1, levels, lon), index)
    edge = pl.BlockSpec((tracers, levels, lon), lambda e: (0, 0, 0))
    met = lambda index: pl.BlockSpec((1, levels, lon), index)
    grid_spec = pltpu.PrefetchScalarGridSpec(
        num_scalar_prefetch=0,
        grid=(2,),
        in_specs=[
            pl.BlockSpec(memory_space=pltpu.SMEM),
            one(lambda e: (0, e * last, 0, 0)),
            one(lambda e: (0, 1 + e * (lat_rows - 3), 0, 0)),
            edge,
            edge,
            met(lambda e: (e * last, 0, 0)),
            met(lambda e: (lat_rows + e * last, 0, 0)),
            met(lambda e: (3 * lat_rows - e * (lat_rows + 2), 0, 0)),
            met(lambda e: (2 * lat_rows + e * last, 0, 0)),
            pl.BlockSpec((tracers, lat_rows, lon), lambda e: (0, 0, 0)),
            pl.BlockSpec(memory_space=pl.ANY),
        ],
        out_specs=one(lambda e: (0, e * last, 0, 0)),
    )
    return pl.pallas_call(
        edge_kernel,
        grid_spec=grid_spec,
        out_shape=jax.ShapeDtypeStruct(state.shape, state.dtype),
        input_output_aliases={10: 0},
        compiler_params=pltpu.CompilerParams(dimension_semantics=("arbitrary",)),
    )(north_open, state, state, south, north, weather, weather, weather, weather, emission, base)


def on_device(
    tracer_state,
    control,
    prior_tiles,
    tile_index,
    region_map,
    region_sigma,
    zonal_courant,
    meridional_courant,
    vertical_diffusion,
):
    band_count = lax.axis_size("band")
    band_index = lax.axis_index("band")
    tiles_count = prior_tiles.shape[0]
    lat_rows = control.shape[1]

    south_v = passed_along(meridional_courant[-1:], "band", 1)
    pack = jnp.concatenate([zonal_courant, meridional_courant, vertical_diffusion, south_v], axis=0)
    weather = relay_gather(pack, "tracer")
    held_state, held_control, _ = lax.optimization_barrier((tracer_state, control, pack))
    q_south = passed_along(held_state[:, -1], "band", 1)
    q_north = passed_along(held_state[:, 0], "band", -1)
    shifted = [control]
    for s in range(1, band_count):
        pairs = [(i, (i + s) % band_count) for i in range(band_count)]
        shifted.append(lax.ppermute(held_control, "band", pairs))

    choose = (
        tile_index[:, :, None] == lax.broadcasted_iota(jnp.int32, (1, 1, tiles_count), 2)
    ).astype(jnp.float32)
    own_row = lax.dynamic_slice_in_dim(choose, band_index, 1, 0)[0]
    row_tiles = jnp.einsum("bt,tmn->bmn", own_row, prior_tiles, precision=exact_dot)
    prior_field = None
    for s, part in enumerate(shifted):
        source_band = (band_index - s) % band_count
        tile = lax.dynamic_index_in_dim(row_tiles, source_band, 0, keepdims=False)
        term = jnp.einsum("jm,kmn->kjn", tile, part, precision=exact_dot)
        prior_field = term if prior_field is None else prior_field + term
    regions = region_sigma.shape[1]
    onehot = (region_map[:, :, None] == lax.broadcasted_iota(jnp.int32, (1, 1, regions), 2)).astype(
        jnp.float32
    )
    cell_sigma = jnp.einsum("kr,jnr->kjn", region_sigma, onehot, precision=exact_dot)
    emission = cell_sigma * prior_field

    latitude = band_index * lat_rows + jnp.arange(lat_rows, dtype=jnp.int32)
    north_open = (latitude < band_count * lat_rows - 1).astype(jnp.float32)

    first, bottom_row, top_row = advance(
        tracer_state, q_south, q_north, weather, emission, north_open, True
    )
    s1_south = passed_along(top_row, "band", 1)
    s1_north = passed_along(bottom_row, "band", -1)
    inside = interior_step(first, weather, emission, north_open)
    tracer_field = edge_step(first, inside, s1_south, s1_north, weather, emission, north_open)
    return (tracer_field, emission)


def solution(mesh):
    in_specs = (
        P(("inv", "tracer"), "band", None, None),
        P(("inv", "tracer"), "band", None),
        P(),
        P(),
        P("band", None),
        P("tracer", None),
        P(("inv", "band"), None, "tracer"),
        P(("inv", "band"), None, "tracer"),
        P(("inv", "band"), None, "tracer"),
    )
    out_specs = (P(("inv", "tracer"), "band", None, None), P(("inv", "tracer"), "band", None))
    return jax.shard_map(
        on_device, mesh=mesh, in_specs=in_specs, out_specs=out_specs, check_vma=False
    )
```

```python
import functools

import jax
import jax.numpy as jnp
from jax import lax
from jax.experimental import pallas as pl
from jax.experimental.pallas import tpu as pltpu
from jax.sharding import PartitionSpec as P

exact_dot = lax.Precision.HIGHEST


def passed_along(value, axis, by):
    count = lax.axis_size(axis)
    pairs = [(i, i + by) for i in range(count) if 0 <= i + by < count]
    return lax.ppermute(value, axis, pairs)


def relay_gather(x, axis):
    count = lax.axis_size(axis)
    me = lax.axis_index(axis)
    rows, levels, width = x.shape
    buf = jnp.zeros((rows, levels, (count + 1) * width), x.dtype)
    buf = lax.dynamic_update_slice(buf, x, (0, 0, me * width))
    right = left = x
    for r in range(1, count):
        right = lax.ppermute(right, axis, [(i, i + 1) for i in range(r - 1, count - 1)])
        left = lax.ppermute(left, axis, [(j, j - 1) for j in range(1, count - r + 1)])
        slot = jnp.where(me - r >= 0, me - r, count)
        buf = lax.dynamic_update_slice(buf, right, (0, 0, slot * width))
        slot = jnp.where(me + r < count, me + r, count)
        buf = lax.dynamic_update_slice(buf, left, (0, 0, slot * width))
    return buf


def fill_coefficients(north_ref, wx_ref, coef_ref):
    lat_rows = coef_ref.shape[1]
    levels, lon = coef_ref.shape[2], coef_ref.shape[3]
    level = lax.broadcasted_iota(jnp.int32, (levels, lon), 0)
    not_top = level < levels - 1
    not_bottom = level > 0
    for a in range(lat_rows):
        u = wx_ref[a]
        uw = pltpu.roll(u, 1, 1)
        v = wx_ref[lat_rows + a] * north_ref[a]
        vm = wx_ref[3 * lat_rows] if a == 0 else wx_ref[lat_rows + a - 1]
        w = wx_ref[2 * lat_rows + a]
        w_up = jnp.where(not_top, w, 0.0)
        w_down = jnp.where(not_bottom, pltpu.roll(w, 1, 0), 0.0)
        coef_ref[0, a] = (
            1.0
            - jnp.maximum(u, 0.0)
            + jnp.minimum(uw, 0.0)
            - jnp.maximum(v, 0.0)
            + jnp.minimum(vm, 0.0)
            - w_up
            - w_down
        )
        coef_ref[1, a] = -jnp.minimum(u, 0.0)
        coef_ref[2, a] = jnp.maximum(uw, 0.0)
        coef_ref[3, a] = -jnp.minimum(v, 0.0)
        coef_ref[4, a] = jnp.maximum(vm, 0.0)
        coef_ref[5, a] = w_up
        coef_ref[6, a] = w_down


def step_kernel(north_ref, q_ref, qs_ref, qn_ref, wx_ref, src_ref, *rest, rows=None):
    o_ref = rest[0]
    edges = rest[1:-1]
    coef_ref = rest[-1]
    lat_rows = q_ref.shape[1]
    rows = range(lat_rows) if rows is None else rows
    levels, lon = q_ref.shape[2], q_ref.shape[3]
    level = lax.broadcasted_iota(jnp.int32, (levels, lon), 0)
    not_top = level < levels - 1
    not_bottom = level > 0

    @pl.when(pl.program_id(0) == 0)
    def _():
        fill_coefficients(north_ref, wx_ref, coef_ref)

    for a in rows:
        qa = q_ref[0, a]
        qm = qs_ref[0] if a == 0 else q_ref[0, a - 1]
        qp = qn_ref[0] if a == lat_rows - 1 else q_ref[0, a + 1]
        result = (
            coef_ref[0, a] * qa
            + coef_ref[1, a] * pltpu.roll(qa, lon - 1, 1)
            + coef_ref[2, a] * pltpu.roll(qa, 1, 1)
            + coef_ref[3, a] * qp
            + coef_ref[4, a] * qm
            + coef_ref[5, a] * pltpu.roll(qa, levels - 1, 0)
            + coef_ref[6, a] * pltpu.roll(qa, 1, 0)
        )
        surface = result[0:1] + src_ref[0, a : a + 1, :]
        targets = [o_ref.at[0, a]]
        if edges and a == 0:
            targets.append(edges[0].at[0])
        if edges and a == lat_rows - 1:
            targets.append(edges[1].at[0])
        for target in targets:
            target[...] = result
            target[0:1, :] = surface


def advance(state, south, north, weather, emission, north_open, with_edges):
    tracers, lat_rows, levels, lon = state.shape
    row = pl.BlockSpec((1, lat_rows, levels, lon), lambda k: (k, 0, 0, 0))
    edge = pl.BlockSpec((1, levels, lon), lambda k: (k, 0, 0))
    out_specs = [row]
    out_shape = [jax.ShapeDtypeStruct(state.shape, state.dtype)]
    if with_edges:
        out_specs += [edge, edge]
        out_shape += [jax.ShapeDtypeStruct((tracers, levels, lon), state.dtype)] * 2
    grid_spec = pltpu.PrefetchScalarGridSpec(
        num_scalar_prefetch=0,
        grid=(tracers,),
        in_specs=[
            pl.BlockSpec(memory_space=pltpu.SMEM),
            row,
            edge,
            edge,
            pl.BlockSpec(weather.shape[:2] + (lon,), lambda k: (0, 0, 0)),
            pl.BlockSpec((1, lat_rows, lon), lambda k: (k, 0, 0)),
        ],
        out_specs=out_specs,
        scratch_shapes=[pltpu.VMEM((7, lat_rows, levels, lon), jnp.float32)],
    )
    return pl.pallas_call(
        step_kernel,
        grid_spec=grid_spec,
        out_shape=out_shape,
        compiler_params=pltpu.CompilerParams(dimension_semantics=("arbitrary",)),
    )(north_open, state, south, north, weather, emission)


def interior_step(state, weather, emission, north_open):
    tracers, lat_rows, levels, lon = state.shape
    row = pl.BlockSpec((1, lat_rows, levels, lon), lambda k: (k, 0, 0, 0))
    kernel = functools.partial(
        lambda n, q, w, e, o, c, rows: step_kernel(n, q, None, None, w, e, o, c, rows=rows),
        rows=range(1, lat_rows - 1),
    )
    grid_spec = pltpu.PrefetchScalarGridSpec(
        num_scalar_prefetch=0,
        grid=(tracers,),
        in_specs=[
            pl.BlockSpec(memory_space=pltpu.SMEM),
            row,
            pl.BlockSpec(weather.shape[:2] + (lon,), lambda k: (0, 0, 0)),
            pl.BlockSpec((1, lat_rows, lon), lambda k: (k, 0, 0)),
        ],
        out_specs=row,
        scratch_shapes=[pltpu.VMEM((7, lat_rows, levels, lon), jnp.float32)],
    )
    return pl.pallas_call(
        kernel,
        grid_spec=grid_spec,
        out_shape=jax.ShapeDtypeStruct(state.shape, state.dtype),
        compiler_params=pltpu.CompilerParams(dimension_semantics=("arbitrary",)),
    )(north_open, state, weather, emission)


def edge_kernel(north_ref, lo_ref, hi_ref, lo_in_ref, hi_in_ref, qs_ref, qn_ref, u_ref, v_ref, vm_ref, w_ref, src_ref, *outs):
    split = len(outs) == 2
    tracers, lat_rows = src_ref.shape[0], src_ref.shape[1]
    levels, lon = lo_ref.shape[1], lo_ref.shape[2]
    top = pl.program_id(0)
    level = lax.broadcasted_iota(jnp.int32, (levels, lon), 0)
    not_top = level < levels - 1
    not_bottom = level > 0
    a = top * (lat_rows - 1)
    is_top = jnp.full((levels, lon), top, jnp.int32) == 1
    u = u_ref[0]
    uw = pltpu.roll(u, 1, 1)
    v = v_ref[0] * north_ref[a]
    vm = vm_ref[0]
    w = w_ref[0]
    w_up = jnp.where(not_top, w, 0.0)
    w_down = jnp.where(not_bottom, pltpu.roll(w, 1, 0), 0.0)
    c_self = (
        1.0
        - jnp.maximum(u, 0.0)
        + jnp.minimum(uw, 0.0)
        - jnp.maximum(v, 0.0)
        + jnp.minimum(vm, 0.0)
        - w_up
        - w_down
    )
    c_east = -jnp.minimum(u, 0.0)
    c_west = jnp.maximum(uw, 0.0)
    c_north = -jnp.minimum(v, 0.0)
    c_south = jnp.maximum(vm, 0.0)
    at_top = jnp.full((1, lon), top, jnp.int32) == 1
    for k in range(tracers):
        qa = jnp.where(is_top, hi_ref[k], lo_ref[k])
        inner = jnp.where(is_top, hi_in_ref[k], lo_in_ref[k])
        qm = jnp.where(is_top, inner, qs_ref[k])
        qp = jnp.where(is_top, qn_ref[k], inner)
        result = (
            c_self * qa
            + c_east * pltpu.roll(qa, lon - 1, 1)
            + c_west * pltpu.roll(qa, 1, 1)
            + c_north * qp
            + c_south * qm
            + w_up * pltpu.roll(qa, levels - 1, 0)
            + w_down * pltpu.roll(qa, 1, 0)
        )
        source = jnp.where(at_top, src_ref[k, lat_rows - 1 : lat_rows, :], src_ref[k, 0:1, :])
        surface = result[0:1] + source
        if split:

            def put(ref, result=result, surface=surface, k=k):
                ref[k] = result
                ref[k, 0:1, :] = surface

            pl.when(top == 0)(functools.partial(put, outs[0]))
            pl.when(top == 1)(functools.partial(put, outs[1]))
        else:
            outs[-1][k, 0] = result
            outs[-1][k, 0, 0:1, :] = surface


def edge_step(rows, base, south, north, weather, emission, north_open):
    tracers, levels, lon = rows[0].shape
    lat_rows = emission.shape[1]
    last = lat_rows - 1
    edge = pl.BlockSpec((tracers, levels, lon), lambda e: (0, 0, 0))
    met = lambda index: pl.BlockSpec((1, levels, lon), index)
    in_specs = [
        pl.BlockSpec(memory_space=pltpu.SMEM),
        edge,
        edge,
        edge,
        edge,
        edge,
        edge,
        met(lambda e: (e * last, 0, 0)),
        met(lambda e: (lat_rows + e * last, 0, 0)),
        met(lambda e: (3 * lat_rows - e * (lat_rows + 2), 0, 0)),
        met(lambda e: (2 * lat_rows + e * last, 0, 0)),
        pl.BlockSpec((tracers, lat_rows, lon), lambda e: (0, 0, 0)),
    ]
    args = [north_open, *rows, south, north, weather, weather, weather, weather, emission]
    if base is None:
        out_specs = [edge, edge]
        out_shape = [jax.ShapeDtypeStruct((tracers, levels, lon), jnp.float32)] * 2
        aliases = {}
        kernel = edge_kernel
    else:
        in_specs.append(pl.BlockSpec(memory_space=pl.ANY))
        args.append(base)
        out_specs = pl.BlockSpec((tracers, 1, levels, lon), lambda e: (0, e * last, 0, 0))
        out_shape = jax.ShapeDtypeStruct(base.shape, base.dtype)
        aliases = {len(args) - 1: 0}
        kernel = lambda *refs: edge_kernel(*refs[:-2], refs[-1])
    grid_spec = pltpu.PrefetchScalarGridSpec(
        num_scalar_prefetch=0, grid=(2,), in_specs=in_specs, out_specs=out_specs
    )
    return pl.pallas_call(
        kernel,
        grid_spec=grid_spec,
        out_shape=out_shape,
        input_output_aliases=aliases,
        compiler_params=pltpu.CompilerParams(dimension_semantics=("arbitrary",)),
    )(*args)


def fused_kernel(north_ref, q_ref, lo_ref, hi_ref, wx_ref, src_ref, o_ref, lo_in_ref, hi_in_ref, coef_ref, mid_ref):
    lat_rows = q_ref.shape[1]
    levels, lon = q_ref.shape[2], q_ref.shape[3]

    @pl.when(pl.program_id(0) == 0)
    def _():
        fill_coefficients(north_ref, wx_ref, coef_ref)

    def stencil(a, qa, qm, qp):
        result = (
            coef_ref[0, a] * qa
            + coef_ref[1, a] * pltpu.roll(qa, lon - 1, 1)
            + coef_ref[2, a] * pltpu.roll(qa, 1, 1)
            + coef_ref[3, a] * qp
            + coef_ref[4, a] * qm
            + coef_ref[5, a] * pltpu.roll(qa, levels - 1, 0)
            + coef_ref[6, a] * pltpu.roll(qa, 1, 0)
        )
        return result, result[0:1] + src_ref[0, a : a + 1, :]

    mid_ref[0] = lo_ref[0]
    mid_ref[lat_rows - 1] = hi_ref[0]
    for a in range(1, lat_rows - 1):
        result, surface = stencil(a, q_ref[0, a], q_ref[0, a - 1], q_ref[0, a + 1])
        mid_ref[a] = result
        mid_ref[a, 0:1, :] = surface
        if a == 1:
            lo_in_ref[0] = mid_ref[a]
        if a == lat_rows - 2:
            hi_in_ref[0] = mid_ref[a]
    for a in range(1, lat_rows - 1):
        result, surface = stencil(a, mid_ref[a], mid_ref[a - 1], mid_ref[a + 1])
        o_ref[0, a] = result
        o_ref[0, a, 0:1, :] = surface


def fused_steps(state, lo, hi, weather, emission, north_open):
    tracers, lat_rows, levels, lon = state.shape
    row = pl.BlockSpec((1, lat_rows, levels, lon), lambda k: (k, 0, 0, 0))
    edge = pl.BlockSpec((1, levels, lon), lambda k: (k, 0, 0))
    grid_spec = pltpu.PrefetchScalarGridSpec(
        num_scalar_prefetch=0,
        grid=(tracers,),
        in_specs=[
            pl.BlockSpec(memory_space=pltpu.SMEM),
            row,
            edge,
            edge,
            pl.BlockSpec(weather.shape[:2] + (lon,), lambda k: (0, 0, 0)),
            pl.BlockSpec((1, lat_rows, lon), lambda k: (k, 0, 0)),
        ],
        out_specs=[row, edge, edge],
        scratch_shapes=[
            pltpu.VMEM((7, lat_rows, levels, lon), jnp.float32),
            pltpu.VMEM((lat_rows, levels, lon), jnp.float32),
        ],
    )
    return pl.pallas_call(
        fused_kernel,
        grid_spec=grid_spec,
        out_shape=[jax.ShapeDtypeStruct(state.shape, state.dtype)]
        + [jax.ShapeDtypeStruct((tracers, levels, lon), state.dtype)] * 2,
        compiler_params=pltpu.CompilerParams(dimension_semantics=("arbitrary",)),
    )(north_open, state, lo, hi, weather, emission)


def on_device(
    tracer_state,
    control,
    prior_tiles,
    tile_index,
    region_map,
    region_sigma,
    zonal_courant,
    meridional_courant,
    vertical_diffusion,
):
    band_count = lax.axis_size("band")
    band_index = lax.axis_index("band")
    tiles_count = prior_tiles.shape[0]
    lat_rows = control.shape[1]

    south_v = passed_along(meridional_courant[-1:], "band", 1)
    pack = jnp.concatenate([zonal_courant, meridional_courant, vertical_diffusion, south_v], axis=0)
    weather = relay_gather(pack, "tracer")
    held_state, held_control, _ = lax.optimization_barrier((tracer_state, control, pack))
    q_south = passed_along(held_state[:, -1], "band", 1)
    q_north = passed_along(held_state[:, 0], "band", -1)
    shifted = [control]
    for s in range(1, band_count):
        pairs = [(i, (i + s) % band_count) for i in range(band_count)]
        shifted.append(lax.ppermute(held_control, "band", pairs))

    choose = (
        tile_index[:, :, None] == lax.broadcasted_iota(jnp.int32, (1, 1, tiles_count), 2)
    ).astype(jnp.float32)
    own_row = lax.dynamic_slice_in_dim(choose, band_index, 1, 0)[0]
    row_tiles = jnp.einsum("bt,tmn->bmn", own_row, prior_tiles, precision=exact_dot)
    prior_field = None
    for s, part in enumerate(shifted):
        source_band = (band_index - s) % band_count
        tile = lax.dynamic_index_in_dim(row_tiles, source_band, 0, keepdims=False)
        term = jnp.einsum("jm,kmn->kjn", tile, part, precision=exact_dot)
        prior_field = term if prior_field is None else prior_field + term
    regions = region_sigma.shape[1]
    onehot = (region_map[:, :, None] == lax.broadcasted_iota(jnp.int32, (1, 1, regions), 2)).astype(
        jnp.float32
    )
    cell_sigma = jnp.einsum("kr,jnr->kjn", region_sigma, onehot, precision=exact_dot)
    emission = cell_sigma * prior_field

    latitude = band_index * lat_rows + jnp.arange(lat_rows, dtype=jnp.int32)
    north_open = (latitude < band_count * lat_rows - 1).astype(jnp.float32)

    rim = (tracer_state[:, 0], tracer_state[:, lat_rows - 1], tracer_state[:, 1], tracer_state[:, lat_rows - 2])
    bottom_row, top_row = edge_step(rim, None, q_south, q_north, weather, emission, north_open)
    s1_south = passed_along(top_row, "band", 1)
    s1_north = passed_along(bottom_row, "band", -1)
    inside, bottom_in, top_in = fused_steps(tracer_state, bottom_row, top_row, weather, emission, north_open)
    rim = (bottom_row, top_row, bottom_in, top_in)
    tracer_field = edge_step(rim, inside, s1_south, s1_north, weather, emission, north_open)
    return (tracer_field, emission)


def solution(mesh):
    in_specs = (
        P(("inv", "tracer"), "band", None, None),
        P(("inv", "tracer"), "band", None),
        P(),
        P(),
        P("band", None),
        P("tracer", None),
        P(("inv", "band"), None, "tracer"),
        P(("inv", "band"), None, "tracer"),
        P(("inv", "band"), None, "tracer"),
    )
    out_specs = (P(("inv", "tracer"), "band", None, None), P(("inv", "tracer"), "band", None))
    return jax.shard_map(
        on_device, mesh=mesh, in_specs=in_specs, out_specs=out_specs, check_vma=False
    )
```

```python
import functools

import jax
import jax.numpy as jnp
from jax import lax
from jax.experimental import pallas as pl
from jax.experimental.pallas import tpu as pltpu
from jax.sharding import PartitionSpec as P

exact_dot = lax.Precision.HIGHEST


def passed_along(value, axis, by):
    count = lax.axis_size(axis)
    pairs = [(i, i + by) for i in range(count) if 0 <= i + by < count]
    return lax.ppermute(value, axis, pairs)


def pack_kernel(*refs):
    parts, out_ref = refs[:-1], refs[-1]
    row = 0
    for part in parts:
        rows = part.shape[0]
        out_ref[row : row + rows] = part[...]
        row += rows


def packed(parts):
    rows = sum(part.shape[0] for part in parts)
    return pl.pallas_call(
        pack_kernel,
        out_shape=jax.ShapeDtypeStruct((rows,) + parts[0].shape[1:], parts[0].dtype),
    )(*parts)


def relay_gather(x, axis):
    count = lax.axis_size(axis)
    me = lax.axis_index(axis)
    rows, levels, width = x.shape
    buf = jnp.zeros((rows, levels, (count + 1) * width), x.dtype)
    buf = lax.dynamic_update_slice(buf, x, (0, 0, me * width))
    right = left = x
    for r in range(1, count):
        right = lax.ppermute(right, axis, [(i, i + 1) for i in range(r - 1, count - 1)])
        left = lax.ppermute(left, axis, [(j, j - 1) for j in range(1, count - r + 1)])
        slot = jnp.where(me - r >= 0, me - r, count)
        buf = lax.dynamic_update_slice(buf, right, (0, 0, slot * width))
        slot = jnp.where(me + r < count, me + r, count)
        buf = lax.dynamic_update_slice(buf, left, (0, 0, slot * width))
    return buf


def step_kernel(north_ref, q_ref, qs_ref, qn_ref, wx_ref, src_ref, *rest, rows=None):
    o_ref = rest[0]
    edges = rest[1:-1]
    coef_ref = rest[-1]
    lat_rows = q_ref.shape[1]
    rows = range(lat_rows) if rows is None else rows
    levels, lon = q_ref.shape[2], q_ref.shape[3]
    level = lax.broadcasted_iota(jnp.int32, (levels, lon), 0)
    not_top = level < levels - 1
    not_bottom = level > 0

    @pl.when(pl.program_id(0) == 0)
    def _():
        for a in range(lat_rows):
            u = wx_ref[a]
            uw = pltpu.roll(u, 1, 1)
            v = wx_ref[lat_rows + a] * north_ref[a]
            vm = wx_ref[3 * lat_rows] if a == 0 else wx_ref[lat_rows + a - 1]
            w = wx_ref[2 * lat_rows + a]
            w_up = jnp.where(not_top, w, 0.0)
            w_down = jnp.where(not_bottom, pltpu.roll(w, 1, 0), 0.0)
            coef_ref[0, a] = (
                1.0
                - jnp.maximum(u, 0.0)
                + jnp.minimum(uw, 0.0)
                - jnp.maximum(v, 0.0)
                + jnp.minimum(vm, 0.0)
                - w_up
                - w_down
            )
            coef_ref[1, a] = -jnp.minimum(u, 0.0)
            coef_ref[2, a] = jnp.maximum(uw, 0.0)
            coef_ref[3, a] = -jnp.minimum(v, 0.0)
            coef_ref[4, a] = jnp.maximum(vm, 0.0)
            coef_ref[5, a] = w_up
            coef_ref[6, a] = w_down

    for a in rows:
        qa = q_ref[0, a]
        qm = qs_ref[0] if a == 0 else q_ref[0, a - 1]
        qp = qn_ref[0] if a == lat_rows - 1 else q_ref[0, a + 1]
        result = (
            coef_ref[0, a] * qa
            + coef_ref[1, a] * pltpu.roll(qa, lon - 1, 1)
            + coef_ref[2, a] * pltpu.roll(qa, 1, 1)
            + coef_ref[3, a] * qp
            + coef_ref[4, a] * qm
            + coef_ref[5, a] * pltpu.roll(qa, levels - 1, 0)
            + coef_ref[6, a] * pltpu.roll(qa, 1, 0)
        )
        surface = result[0:1] + src_ref[0, a : a + 1, :]
        targets = [o_ref.at[0, a]]
        if edges and a == 0:
            targets.append(edges[0].at[0])
        if edges and a == lat_rows - 1:
            targets.append(edges[1].at[0])
        for target in targets:
            target[...] = result
            target[0:1, :] = surface


def advance(state, south, north, weather, emission, north_open, with_edges):
    tracers, lat_rows, levels, lon = state.shape
    row = pl.BlockSpec((1, lat_rows, levels, lon), lambda k: (k, 0, 0, 0))
    edge = pl.BlockSpec((1, levels, lon), lambda k: (k, 0, 0))
    out_specs = [row]
    out_shape = [jax.ShapeDtypeStruct(state.shape, state.dtype)]
    if with_edges:
        out_specs += [edge, edge]
        out_shape += [jax.ShapeDtypeStruct((tracers, levels, lon), state.dtype)] * 2
    grid_spec = pltpu.PrefetchScalarGridSpec(
        num_scalar_prefetch=0,
        grid=(tracers,),
        in_specs=[
            pl.BlockSpec(memory_space=pltpu.SMEM),
            row,
            edge,
            edge,
            pl.BlockSpec(weather.shape[:2] + (lon,), lambda k: (0, 0, 0)),
            pl.BlockSpec((1, lat_rows, lon), lambda k: (k, 0, 0)),
        ],
        out_specs=out_specs,
        scratch_shapes=[pltpu.VMEM((7, lat_rows, levels, lon), jnp.float32)],
    )
    return pl.pallas_call(
        step_kernel,
        grid_spec=grid_spec,
        out_shape=out_shape,
        compiler_params=pltpu.CompilerParams(dimension_semantics=("arbitrary",)),
    )(north_open, state, south, north, weather, emission)


def interior_step(state, weather, emission, north_open):
    tracers, lat_rows, levels, lon = state.shape
    row = pl.BlockSpec((1, lat_rows, levels, lon), lambda k: (k, 0, 0, 0))
    kernel = functools.partial(
        lambda n, q, w, e, o, c, rows: step_kernel(n, q, None, None, w, e, o, c, rows=rows),
        rows=range(1, lat_rows - 1),
    )
    grid_spec = pltpu.PrefetchScalarGridSpec(
        num_scalar_prefetch=0,
        grid=(tracers,),
        in_specs=[
            pl.BlockSpec(memory_space=pltpu.SMEM),
            row,
            pl.BlockSpec(weather.shape[:2] + (lon,), lambda k: (0, 0, 0)),
            pl.BlockSpec((1, lat_rows, lon), lambda k: (k, 0, 0)),
        ],
        out_specs=row,
        scratch_shapes=[pltpu.VMEM((7, lat_rows, levels, lon), jnp.float32)],
    )
    return pl.pallas_call(
        kernel,
        grid_spec=grid_spec,
        out_shape=jax.ShapeDtypeStruct(state.shape, state.dtype),
        compiler_params=pltpu.CompilerParams(dimension_semantics=("arbitrary",)),
    )(north_open, state, weather, emission)


def edge_kernel(north_ref, qa_ref, qi_ref, qs_ref, qn_ref, u_ref, v_ref, vm_ref, w_ref, src_ref, base_ref, o_ref):
    del base_ref
    tracers, lat_rows = src_ref.shape[0], src_ref.shape[1]
    levels, lon = qa_ref.shape[2], qa_ref.shape[3]
    top = pl.program_id(0)
    level = lax.broadcasted_iota(jnp.int32, (levels, lon), 0)
    not_top = level < levels - 1
    not_bottom = level > 0
    a = top * (lat_rows - 1)
    is_top = jnp.full((levels, lon), top, jnp.int32) == 1
    u = u_ref[0]
    uw = pltpu.roll(u, 1, 1)
    v = v_ref[0] * north_ref[a]
    vm = vm_ref[0]
    w = w_ref[0]
    w_up = jnp.where(not_top, w, 0.0)
    w_down = jnp.where(not_bottom, pltpu.roll(w, 1, 0), 0.0)
    c_self = (
        1.0
        - jnp.maximum(u, 0.0)
        + jnp.minimum(uw, 0.0)
        - jnp.maximum(v, 0.0)
        + jnp.minimum(vm, 0.0)
        - w_up
        - w_down
    )
    c_east = -jnp.minimum(u, 0.0)
    c_west = jnp.maximum(uw, 0.0)
    c_north = -jnp.minimum(v, 0.0)
    c_south = jnp.maximum(vm, 0.0)
    at_top = jnp.full((1, lon), top, jnp.int32) == 1
    for k in range(tracers):
        qa = qa_ref[k, 0]
        inner = qi_ref[k, 0]
        qm = jnp.where(is_top, inner, qs_ref[k])
        qp = jnp.where(is_top, qn_ref[k], inner)
        result = (
            c_self * qa
            + c_east * pltpu.roll(qa, lon - 1, 1)
            + c_west * pltpu.roll(qa, 1, 1)
            + c_north * qp
            + c_south * qm
            + w_up * pltpu.roll(qa, levels - 1, 0)
            + w_down * pltpu.roll(qa, 1, 0)
        )
        source = jnp.where(at_top, src_ref[k, lat_rows - 1 : lat_rows, :], src_ref[k, 0:1, :])
        o_ref[k, 0] = result
        o_ref[k, 0, 0:1, :] = result[0:1] + source


def edge_step(state, base, south, north, weather, emission, north_open):
    tracers, lat_rows, levels, lon = state.shape
    last = lat_rows - 1
    one = lambda index: pl.BlockSpec((tracers, 1, levels, lon), index)
    edge = pl.BlockSpec((tracers, levels, lon), lambda e: (0, 0, 0))
    met = lambda index: pl.BlockSpec((1, levels, lon), index)
    grid_spec = pltpu.PrefetchScalarGridSpec(
        num_scalar_prefetch=0,
        grid=(2,),
        in_specs=[
            pl.BlockSpec(memory_space=pltpu.SMEM),
            one(lambda e: (0, e * last, 0, 0)),
            one(lambda e: (0, 1 + e * (lat_rows - 3), 0, 0)),
            edge,
            edge,
            met(lambda e: (e * last, 0, 0)),
            met(lambda e: (lat_rows + e * last, 0, 0)),
            met(lambda e: (3 * lat_rows - e * (lat_rows + 2), 0, 0)),
            met(lambda e: (2 * lat_rows + e * last, 0, 0)),
            pl.BlockSpec((tracers, lat_rows, lon), lambda e: (0, 0, 0)),
            pl.BlockSpec(memory_space=pl.ANY),
        ],
        out_specs=one(lambda e: (0, e * last, 0, 0)),
    )
    return pl.pallas_call(
        edge_kernel,
        grid_spec=grid_spec,
        out_shape=jax.ShapeDtypeStruct(state.shape, state.dtype),
        input_output_aliases={10: 0},
        compiler_params=pltpu.CompilerParams(dimension_semantics=("arbitrary",)),
    )(north_open, state, state, south, north, weather, weather, weather, weather, emission, base)


def on_device(
    tracer_state,
    control,
    prior_tiles,
    tile_index,
    region_map,
    region_sigma,
    zonal_courant,
    meridional_courant,
    vertical_diffusion,
):
    band_count = lax.axis_size("band")
    band_index = lax.axis_index("band")
    tiles_count = prior_tiles.shape[0]
    lat_rows = control.shape[1]

    south_v = passed_along(meridional_courant[-1:], "band", 1)
    pack = packed([zonal_courant, meridional_courant, vertical_diffusion, south_v])
    weather = relay_gather(pack, "tracer")
    held_state, held_control, _ = lax.optimization_barrier((tracer_state, control, pack))
    q_south = passed_along(held_state[:, -1], "band", 1)
    q_north = passed_along(held_state[:, 0], "band", -1)
    shifted = [control]
    for s in range(1, band_count):
        pairs = [(i, (i + s) % band_count) for i in range(band_count)]
        shifted.append(lax.ppermute(held_control, "band", pairs))

    choose = (
        tile_index[:, :, None] == lax.broadcasted_iota(jnp.int32, (1, 1, tiles_count), 2)
    ).astype(jnp.float32)
    own_row = lax.dynamic_slice_in_dim(choose, band_index, 1, 0)[0]
    row_tiles = jnp.einsum("bt,tmn->bmn", own_row, prior_tiles, precision=exact_dot)
    prior_field = None
    for s, part in enumerate(shifted):
        source_band = (band_index - s) % band_count
        tile = lax.dynamic_index_in_dim(row_tiles, source_band, 0, keepdims=False)
        term = jnp.einsum("jm,kmn->kjn", tile, part, precision=exact_dot)
        prior_field = term if prior_field is None else prior_field + term
    regions = region_sigma.shape[1]
    onehot = (region_map[:, :, None] == lax.broadcasted_iota(jnp.int32, (1, 1, regions), 2)).astype(
        jnp.float32
    )
    cell_sigma = jnp.einsum("kr,jnr->kjn", region_sigma, onehot, precision=exact_dot)
    emission = cell_sigma * prior_field

    latitude = band_index * lat_rows + jnp.arange(lat_rows, dtype=jnp.int32)
    north_open = (latitude < band_count * lat_rows - 1).astype(jnp.float32)

    first, bottom_row, top_row = advance(
        tracer_state, q_south, q_north, weather, emission, north_open, True
    )
    s1_south = passed_along(top_row, "band", 1)
    s1_north = passed_along(bottom_row, "band", -1)
    inside = interior_step(first, weather, emission, north_open)
    tracer_field = edge_step(first, inside, s1_south, s1_north, weather, emission, north_open)
    return (tracer_field, emission)


def solution(mesh):
    in_specs = (
        P(("inv", "tracer"), "band", None, None),
        P(("inv", "tracer"), "band", None),
        P(),
        P(),
        P("band", None),
        P("tracer", None),
        P(("inv", "band"), None, "tracer"),
        P(("inv", "band"), None, "tracer"),
        P(("inv", "band"), None, "tracer"),
    )
    out_specs = (P(("inv", "tracer"), "band", None, None), P(("inv", "tracer"), "band", None))
    return jax.shard_map(
        on_device, mesh=mesh, in_specs=in_specs, out_specs=out_specs, check_vma=False
    )
```

```python
import functools

import jax
import jax.numpy as jnp
from jax import lax
from jax.experimental import pallas as pl
from jax.experimental.pallas import tpu as pltpu
from jax.sharding import PartitionSpec as P

exact_dot = lax.Precision.HIGHEST


def passed_along(value, axis, by):
    count = lax.axis_size(axis)
    pairs = [(i, i + by) for i in range(count) if 0 <= i + by < count]
    return lax.ppermute(value, axis, pairs)


def pack_kernel(*refs):
    parts, out_ref = refs[:-1], refs[-1]
    row = 0
    for part in parts:
        rows = part.shape[0]
        out_ref[row : row + rows] = part[...]
        row += rows


def packed(parts):
    rows = sum(part.shape[0] for part in parts)
    return pl.pallas_call(
        pack_kernel,
        out_shape=jax.ShapeDtypeStruct((rows,) + parts[0].shape[1:], parts[0].dtype),
    )(*parts)


def relay_gather(x, axis, hold):
    count = lax.axis_size(axis)
    me = lax.axis_index(axis)
    rows, levels, width = x.shape
    buf = jnp.zeros((rows, levels, (count + 1) * width), x.dtype)
    buf = lax.dynamic_update_slice(buf, x, (0, 0, me * width))
    right = left = x
    for r in range(1, count):
        right = lax.ppermute(right, axis, [(i, i + 1) for i in range(r - 1, count - 1)])
        left = lax.ppermute(left, axis, [(j, j - 1) for j in range(1, count - r + 1)])
        if r == 1:
            hold, right = lax.optimization_barrier((hold, right))
        slot = jnp.where(me - r >= 0, me - r, count)
        buf = lax.dynamic_update_slice(buf, right, (0, 0, slot * width))
        slot = jnp.where(me + r < count, me + r, count)
        buf = lax.dynamic_update_slice(buf, left, (0, 0, slot * width))
    if count == 1:
        hold = lax.optimization_barrier(hold)
    return buf, hold


def step_kernel(north_ref, q_ref, qs_ref, qn_ref, wx_ref, src_ref, *rest, rows=None):
    o_ref = rest[0]
    edges = rest[1:-1]
    coef_ref = rest[-1]
    lat_rows = q_ref.shape[1]
    rows = range(lat_rows) if rows is None else rows
    levels, lon = q_ref.shape[2], q_ref.shape[3]
    level = lax.broadcasted_iota(jnp.int32, (levels, lon), 0)
    not_top = level < levels - 1
    not_bottom = level > 0

    @pl.when(pl.program_id(0) == 0)
    def _():
        for a in range(lat_rows):
            u = wx_ref[a]
            uw = pltpu.roll(u, 1, 1)
            v = wx_ref[lat_rows + a] * north_ref[a]
            vm = wx_ref[3 * lat_rows] if a == 0 else wx_ref[lat_rows + a - 1]
            w = wx_ref[2 * lat_rows + a]
            w_up = jnp.where(not_top, w, 0.0)
            w_down = jnp.where(not_bottom, pltpu.roll(w, 1, 0), 0.0)
            coef_ref[0, a] = (
                1.0
                - jnp.maximum(u, 0.0)
                + jnp.minimum(uw, 0.0)
                - jnp.maximum(v, 0.0)
                + jnp.minimum(vm, 0.0)
                - w_up
                - w_down
            )
            coef_ref[1, a] = -jnp.minimum(u, 0.0)
            coef_ref[2, a] = jnp.maximum(uw, 0.0)
            coef_ref[3, a] = -jnp.minimum(v, 0.0)
            coef_ref[4, a] = jnp.maximum(vm, 0.0)
            coef_ref[5, a] = w_up
            coef_ref[6, a] = w_down

    for a in rows:
        qa = q_ref[0, a]
        qm = qs_ref[0] if a == 0 else q_ref[0, a - 1]
        qp = qn_ref[0] if a == lat_rows - 1 else q_ref[0, a + 1]
        result = (
            coef_ref[0, a] * qa
            + coef_ref[1, a] * pltpu.roll(qa, lon - 1, 1)
            + coef_ref[2, a] * pltpu.roll(qa, 1, 1)
            + coef_ref[3, a] * qp
            + coef_ref[4, a] * qm
            + coef_ref[5, a] * pltpu.roll(qa, levels - 1, 0)
            + coef_ref[6, a] * pltpu.roll(qa, 1, 0)
        )
        surface = result[0:1] + src_ref[0, a : a + 1, :]
        targets = [o_ref.at[0, a]]
        if edges and a == 0:
            targets.append(edges[0].at[0])
        if edges and a == lat_rows - 1:
            targets.append(edges[1].at[0])
        for target in targets:
            target[...] = result
            target[0:1, :] = surface


def advance(state, south, north, weather, emission, north_open, with_edges):
    tracers, lat_rows, levels, lon = state.shape
    row = pl.BlockSpec((1, lat_rows, levels, lon), lambda k: (k, 0, 0, 0))
    edge = pl.BlockSpec((1, levels, lon), lambda k: (k, 0, 0))
    out_specs = [row]
    out_shape = [jax.ShapeDtypeStruct(state.shape, state.dtype)]
    if with_edges:
        out_specs += [edge, edge]
        out_shape += [jax.ShapeDtypeStruct((tracers, levels, lon), state.dtype)] * 2
    grid_spec = pltpu.PrefetchScalarGridSpec(
        num_scalar_prefetch=0,
        grid=(tracers,),
        in_specs=[
            pl.BlockSpec(memory_space=pltpu.SMEM),
            row,
            edge,
            edge,
            pl.BlockSpec(weather.shape[:2] + (lon,), lambda k: (0, 0, 0)),
            pl.BlockSpec((1, lat_rows, lon), lambda k: (k, 0, 0)),
        ],
        out_specs=out_specs,
        scratch_shapes=[pltpu.VMEM((7, lat_rows, levels, lon), jnp.float32)],
    )
    return pl.pallas_call(
        step_kernel,
        grid_spec=grid_spec,
        out_shape=out_shape,
        compiler_params=pltpu.CompilerParams(dimension_semantics=("arbitrary",)),
    )(north_open, state, south, north, weather, emission)


def interior_step(state, weather, emission, north_open):
    tracers, lat_rows, levels, lon = state.shape
    row = pl.BlockSpec((1, lat_rows, levels, lon), lambda k: (k, 0, 0, 0))
    kernel = functools.partial(
        lambda n, q, w, e, o, c, rows: step_kernel(n, q, None, None, w, e, o, c, rows=rows),
        rows=range(1, lat_rows - 1),
    )
    grid_spec = pltpu.PrefetchScalarGridSpec(
        num_scalar_prefetch=0,
        grid=(tracers,),
        in_specs=[
            pl.BlockSpec(memory_space=pltpu.SMEM),
            row,
            pl.BlockSpec(weather.shape[:2] + (lon,), lambda k: (0, 0, 0)),
            pl.BlockSpec((1, lat_rows, lon), lambda k: (k, 0, 0)),
        ],
        out_specs=row,
        scratch_shapes=[pltpu.VMEM((7, lat_rows, levels, lon), jnp.float32)],
    )
    return pl.pallas_call(
        kernel,
        grid_spec=grid_spec,
        out_shape=jax.ShapeDtypeStruct(state.shape, state.dtype),
        compiler_params=pltpu.CompilerParams(dimension_semantics=("arbitrary",)),
    )(north_open, state, weather, emission)


def edge_kernel(north_ref, qa_ref, qi_ref, qs_ref, qn_ref, u_ref, v_ref, vm_ref, w_ref, src_ref, base_ref, o_ref):
    del base_ref
    tracers, lat_rows = src_ref.shape[0], src_ref.shape[1]
    levels, lon = qa_ref.shape[2], qa_ref.shape[3]
    top = pl.program_id(0)
    level = lax.broadcasted_iota(jnp.int32, (levels, lon), 0)
    not_top = level < levels - 1
    not_bottom = level > 0
    a = top * (lat_rows - 1)
    is_top = jnp.full((levels, lon), top, jnp.int32) == 1
    u = u_ref[0]
    uw = pltpu.roll(u, 1, 1)
    v = v_ref[0] * north_ref[a]
    vm = vm_ref[0]
    w = w_ref[0]
    w_up = jnp.where(not_top, w, 0.0)
    w_down = jnp.where(not_bottom, pltpu.roll(w, 1, 0), 0.0)
    c_self = (
        1.0
        - jnp.maximum(u, 0.0)
        + jnp.minimum(uw, 0.0)
        - jnp.maximum(v, 0.0)
        + jnp.minimum(vm, 0.0)
        - w_up
        - w_down
    )
    c_east = -jnp.minimum(u, 0.0)
    c_west = jnp.maximum(uw, 0.0)
    c_north = -jnp.minimum(v, 0.0)
    c_south = jnp.maximum(vm, 0.0)
    at_top = jnp.full((1, lon), top, jnp.int32) == 1
    for k in range(tracers):
        qa = qa_ref[k, 0]
        inner = qi_ref[k, 0]
        qm = jnp.where(is_top, inner, qs_ref[k])
        qp = jnp.where(is_top, qn_ref[k], inner)
        result = (
            c_self * qa
            + c_east * pltpu.roll(qa, lon - 1, 1)
            + c_west * pltpu.roll(qa, 1, 1)
            + c_north * qp
            + c_south * qm
            + w_up * pltpu.roll(qa, levels - 1, 0)
            + w_down * pltpu.roll(qa, 1, 0)
        )
        source = jnp.where(at_top, src_ref[k, lat_rows - 1 : lat_rows, :], src_ref[k, 0:1, :])
        o_ref[k, 0] = result
        o_ref[k, 0, 0:1, :] = result[0:1] + source


def edge_step(state, base, south, north, weather, emission, north_open):
    tracers, lat_rows, levels, lon = state.shape
    last = lat_rows - 1
    one = lambda index: pl.BlockSpec((tracers, 1, levels, lon), index)
    edge = pl.BlockSpec((tracers, levels, lon), lambda e: (0, 0, 0))
    met = lambda index: pl.BlockSpec((1, levels, lon), index)
    grid_spec = pltpu.PrefetchScalarGridSpec(
        num_scalar_prefetch=0,
        grid=(2,),
        in_specs=[
            pl.BlockSpec(memory_space=pltpu.SMEM),
            one(lambda e: (0, e * last, 0, 0)),
            one(lambda e: (0, 1 + e * (lat_rows - 3), 0, 0)),
            edge,
            edge,
            met(lambda e: (e * last, 0, 0)),
            met(lambda e: (lat_rows + e * last, 0, 0)),
            met(lambda e: (3 * lat_rows - e * (lat_rows + 2), 0, 0)),
            met(lambda e: (2 * lat_rows + e * last, 0, 0)),
            pl.BlockSpec((tracers, lat_rows, lon), lambda e: (0, 0, 0)),
            pl.BlockSpec(memory_space=pl.ANY),
        ],
        out_specs=one(lambda e: (0, e * last, 0, 0)),
    )
    return pl.pallas_call(
        edge_kernel,
        grid_spec=grid_spec,
        out_shape=jax.ShapeDtypeStruct(state.shape, state.dtype),
        input_output_aliases={10: 0},
        compiler_params=pltpu.CompilerParams(dimension_semantics=("arbitrary",)),
    )(north_open, state, state, south, north, weather, weather, weather, weather, emission, base)


def on_device(
    tracer_state,
    control,
    prior_tiles,
    tile_index,
    region_map,
    region_sigma,
    zonal_courant,
    meridional_courant,
    vertical_diffusion,
):
    band_count = lax.axis_size("band")
    band_index = lax.axis_index("band")
    tiles_count = prior_tiles.shape[0]
    lat_rows = control.shape[1]

    south_v = passed_along(meridional_courant[-1:], "band", 1)
    pack = packed([zonal_courant, meridional_courant, vertical_diffusion, south_v])
    weather, held = relay_gather(
        pack, "tracer", (tracer_state, control, prior_tiles, tile_index, region_map, region_sigma)
    )
    tracer_state, control, prior_tiles, tile_index, region_map, region_sigma = held
    q_south = passed_along(tracer_state[:, -1], "band", 1)
    q_north = passed_along(tracer_state[:, 0], "band", -1)
    shifted = [control]
    for s in range(1, band_count):
        pairs = [(i, (i + s) % band_count) for i in range(band_count)]
        shifted.append(lax.ppermute(control, "band", pairs))

    choose = (
        tile_index[:, :, None] == lax.broadcasted_iota(jnp.int32, (1, 1, tiles_count), 2)
    ).astype(jnp.float32)
    own_row = lax.dynamic_slice_in_dim(choose, band_index, 1, 0)[0]
    row_tiles = jnp.einsum("bt,tmn->bmn", own_row, prior_tiles, precision=exact_dot)
    prior_field = None
    for s, part in enumerate(shifted):
        source_band = (band_index - s) % band_count
        tile = lax.dynamic_index_in_dim(row_tiles, source_band, 0, keepdims=False)
        term = jnp.einsum("jm,kmn->kjn", tile, part, precision=exact_dot)
        prior_field = term if prior_field is None else prior_field + term
    regions = region_sigma.shape[1]
    onehot = (region_map[:, :, None] == lax.broadcasted_iota(jnp.int32, (1, 1, regions), 2)).astype(
        jnp.float32
    )
    cell_sigma = jnp.einsum("kr,jnr->kjn", region_sigma, onehot, precision=exact_dot)
    emission = cell_sigma * prior_field

    latitude = band_index * lat_rows + lax.broadcasted_iota(jnp.int32, (lat_rows,), 0) + tile_index[0, 0] * 0
    north_open = (latitude < band_count * lat_rows - 1).astype(jnp.float32)

    first, bottom_row, top_row = advance(
        tracer_state, q_south, q_north, weather, emission, north_open, True
    )
    s1_south = passed_along(top_row, "band", 1)
    s1_north = passed_along(bottom_row, "band", -1)
    inside = interior_step(first, weather, emission, north_open)
    tracer_field = edge_step(first, inside, s1_south, s1_north, weather, emission, north_open)
    return (tracer_field, emission)


def solution(mesh):
    in_specs = (
        P(("inv", "tracer"), "band", None, None),
        P(("inv", "tracer"), "band", None),
        P(),
        P(),
        P("band", None),
        P("tracer", None),
        P(("inv", "band"), None, "tracer"),
        P(("inv", "band"), None, "tracer"),
        P(("inv", "band"), None, "tracer"),
    )
    out_specs = (P(("inv", "tracer"), "band", None, None), P(("inv", "tracer"), "band", None))
    return jax.shard_map(
        on_device, mesh=mesh, in_specs=in_specs, out_specs=out_specs, check_vma=False
    )
```

```python
import functools

import jax
import jax.numpy as jnp
from jax import lax
from jax.experimental import pallas as pl
from jax.experimental.pallas import tpu as pltpu
from jax.sharding import PartitionSpec as P

exact_dot = lax.Precision.HIGHEST


def passed_along(value, axis, by):
    count = lax.axis_size(axis)
    pairs = [(i, i + by) for i in range(count) if 0 <= i + by < count]
    return lax.ppermute(value, axis, pairs)


def pack_kernel(*refs):
    parts, out_ref = refs[:-1], refs[-1]
    row = 0
    for part in parts:
        rows = part.shape[0]
        out_ref[row : row + rows] = part[...]
        row += rows


def packed(parts):
    rows = sum(part.shape[0] for part in parts)
    return pl.pallas_call(
        pack_kernel,
        out_shape=jax.ShapeDtypeStruct((rows,) + parts[0].shape[1:], parts[0].dtype),
    )(*parts)


def relay_gather(x, axis):
    count = lax.axis_size(axis)
    me = lax.axis_index(axis)
    rows, levels, width = x.shape
    buf = jnp.zeros((rows, levels, (count + 1) * width), x.dtype)
    buf = lax.dynamic_update_slice(buf, x, (0, 0, me * width))
    right = left = x
    for r in range(1, count):
        right = lax.ppermute(right, axis, [(i, i + 1) for i in range(r - 1, count - 1)])
        left = lax.ppermute(left, axis, [(j, j - 1) for j in range(1, count - r + 1)])
        slot = jnp.where(me - r >= 0, me - r, count)
        buf = lax.dynamic_update_slice(buf, right, (0, 0, slot * width))
        slot = jnp.where(me + r < count, me + r, count)
        buf = lax.dynamic_update_slice(buf, left, (0, 0, slot * width))
    return buf


def fill_coefficients(north_ref, wx_ref, coef_ref):
    lat_rows = coef_ref.shape[1]
    levels, lon = coef_ref.shape[2], coef_ref.shape[3]
    level = lax.broadcasted_iota(jnp.int32, (levels, lon), 0)
    not_top = level < levels - 1
    not_bottom = level > 0
    for a in range(lat_rows):
        u = wx_ref[a]
        uw = pltpu.roll(u, 1, 1)
        v = wx_ref[lat_rows + a] * north_ref[a]
        vm = wx_ref[3 * lat_rows] if a == 0 else wx_ref[lat_rows + a - 1]
        w = wx_ref[2 * lat_rows + a]
        w_up = jnp.where(not_top, w, 0.0)
        w_down = jnp.where(not_bottom, pltpu.roll(w, 1, 0), 0.0)
        coef_ref[0, a] = (
            1.0
            - jnp.maximum(u, 0.0)
            + jnp.minimum(uw, 0.0)
            - jnp.maximum(v, 0.0)
            + jnp.minimum(vm, 0.0)
            - w_up
            - w_down
        )
        coef_ref[1, a] = -jnp.minimum(u, 0.0)
        coef_ref[2, a] = jnp.maximum(uw, 0.0)
        coef_ref[3, a] = -jnp.minimum(v, 0.0)
        coef_ref[4, a] = jnp.maximum(vm, 0.0)
        coef_ref[5, a] = w_up
        coef_ref[6, a] = w_down


def step_kernel(north_ref, q_ref, qs_ref, qn_ref, wx_ref, src_ref, *rest, rows=None):
    o_ref = rest[0]
    edges = rest[1:-1]
    coef_ref = rest[-1]
    lat_rows = q_ref.shape[1]
    rows = range(lat_rows) if rows is None else rows
    levels, lon = q_ref.shape[2], q_ref.shape[3]
    level = lax.broadcasted_iota(jnp.int32, (levels, lon), 0)
    not_top = level < levels - 1
    not_bottom = level > 0

    @pl.when(pl.program_id(0) == 0)
    def _():
        fill_coefficients(north_ref, wx_ref, coef_ref)

    for a in rows:
        qa = q_ref[0, a]
        qm = qs_ref[0] if a == 0 else q_ref[0, a - 1]
        qp = qn_ref[0] if a == lat_rows - 1 else q_ref[0, a + 1]
        result = (
            coef_ref[0, a] * qa
            + coef_ref[1, a] * pltpu.roll(qa, lon - 1, 1)
            + coef_ref[2, a] * pltpu.roll(qa, 1, 1)
            + coef_ref[3, a] * qp
            + coef_ref[4, a] * qm
            + coef_ref[5, a] * pltpu.roll(qa, levels - 1, 0)
            + coef_ref[6, a] * pltpu.roll(qa, 1, 0)
        )
        surface = result[0:1] + src_ref[0, a : a + 1, :]
        targets = [o_ref.at[0, a]]
        if edges and a == 0:
            targets.append(edges[0].at[0])
        if edges and a == lat_rows - 1:
            targets.append(edges[1].at[0])
        for target in targets:
            target[...] = result
            target[0:1, :] = surface


def advance(state, south, north, weather, emission, north_open, with_edges):
    tracers, lat_rows, levels, lon = state.shape
    row = pl.BlockSpec((1, lat_rows, levels, lon), lambda k: (k, 0, 0, 0))
    edge = pl.BlockSpec((1, levels, lon), lambda k: (k, 0, 0))
    out_specs = [row]
    out_shape = [jax.ShapeDtypeStruct(state.shape, state.dtype)]
    if with_edges:
        out_specs += [edge, edge]
        out_shape += [jax.ShapeDtypeStruct((tracers, levels, lon), state.dtype)] * 2
    grid_spec = pltpu.PrefetchScalarGridSpec(
        num_scalar_prefetch=0,
        grid=(tracers,),
        in_specs=[
            pl.BlockSpec(memory_space=pltpu.SMEM),
            row,
            edge,
            edge,
            pl.BlockSpec(weather.shape[:2] + (lon,), lambda k: (0, 0, 0)),
            pl.BlockSpec((1, lat_rows, lon), lambda k: (k, 0, 0)),
        ],
        out_specs=out_specs,
        scratch_shapes=[pltpu.VMEM((7, lat_rows, levels, lon), jnp.float32)],
    )
    return pl.pallas_call(
        step_kernel,
        grid_spec=grid_spec,
        out_shape=out_shape,
        compiler_params=pltpu.CompilerParams(dimension_semantics=("arbitrary",)),
    )(north_open, state, south, north, weather, emission)


def interior_step(state, weather, emission, north_open):
    tracers, lat_rows, levels, lon = state.shape
    row = pl.BlockSpec((1, lat_rows, levels, lon), lambda k: (k, 0, 0, 0))
    kernel = functools.partial(
        lambda n, q, w, e, o, c, rows: step_kernel(n, q, None, None, w, e, o, c, rows=rows),
        rows=range(1, lat_rows - 1),
    )
    grid_spec = pltpu.PrefetchScalarGridSpec(
        num_scalar_prefetch=0,
        grid=(tracers,),
        in_specs=[
            pl.BlockSpec(memory_space=pltpu.SMEM),
            row,
            pl.BlockSpec(weather.shape[:2] + (lon,), lambda k: (0, 0, 0)),
            pl.BlockSpec((1, lat_rows, lon), lambda k: (k, 0, 0)),
        ],
        out_specs=row,
        scratch_shapes=[pltpu.VMEM((7, lat_rows, levels, lon), jnp.float32)],
    )
    return pl.pallas_call(
        kernel,
        grid_spec=grid_spec,
        out_shape=jax.ShapeDtypeStruct(state.shape, state.dtype),
        compiler_params=pltpu.CompilerParams(dimension_semantics=("arbitrary",)),
    )(north_open, state, weather, emission)


def edge_kernel(north_ref, lo_ref, hi_ref, lo_in_ref, hi_in_ref, qs_ref, qn_ref, u_ref, v_ref, vm_ref, w_ref, src_ref, *outs):
    split = len(outs) == 2
    tracers, lat_rows = src_ref.shape[0], src_ref.shape[1]
    levels, lon = lo_ref.shape[1], lo_ref.shape[2]
    top = pl.program_id(0)
    level = lax.broadcasted_iota(jnp.int32, (levels, lon), 0)
    not_top = level < levels - 1
    not_bottom = level > 0
    a = top * (lat_rows - 1)
    is_top = jnp.full((levels, lon), top, jnp.int32) == 1
    u = u_ref[0]
    uw = pltpu.roll(u, 1, 1)
    v = v_ref[0] * north_ref[a]
    vm = vm_ref[0]
    w = w_ref[0]
    w_up = jnp.where(not_top, w, 0.0)
    w_down = jnp.where(not_bottom, pltpu.roll(w, 1, 0), 0.0)
    c_self = (
        1.0
        - jnp.maximum(u, 0.0)
        + jnp.minimum(uw, 0.0)
        - jnp.maximum(v, 0.0)
        + jnp.minimum(vm, 0.0)
        - w_up
        - w_down
    )
    c_east = -jnp.minimum(u, 0.0)
    c_west = jnp.maximum(uw, 0.0)
    c_north = -jnp.minimum(v, 0.0)
    c_south = jnp.maximum(vm, 0.0)
    at_top = jnp.full((1, lon), top, jnp.int32) == 1
    for k in range(tracers):
        qa = jnp.where(is_top, hi_ref[k], lo_ref[k])
        inner = jnp.where(is_top, hi_in_ref[k], lo_in_ref[k])
        qm = jnp.where(is_top, inner, qs_ref[k])
        qp = jnp.where(is_top, qn_ref[k], inner)
        result = (
            c_self * qa
            + c_east * pltpu.roll(qa, lon - 1, 1)
            + c_west * pltpu.roll(qa, 1, 1)
            + c_north * qp
            + c_south * qm
            + w_up * pltpu.roll(qa, levels - 1, 0)
            + w_down * pltpu.roll(qa, 1, 0)
        )
        source = jnp.where(at_top, src_ref[k, lat_rows - 1 : lat_rows, :], src_ref[k, 0:1, :])
        surface = result[0:1] + source
        if split:

            def put(ref, result=result, surface=surface, k=k):
                ref[k] = result
                ref[k, 0:1, :] = surface

            pl.when(top == 0)(functools.partial(put, outs[0]))
            pl.when(top == 1)(functools.partial(put, outs[1]))
        else:
            outs[-1][k, 0] = result
            outs[-1][k, 0, 0:1, :] = surface


def edge_step(rows, base, south, north, weather, emission, north_open):
    tracers, levels, lon = rows[0].shape
    lat_rows = emission.shape[1]
    last = lat_rows - 1
    edge = pl.BlockSpec((tracers, levels, lon), lambda e: (0, 0, 0))
    met = lambda index: pl.BlockSpec((1, levels, lon), index)
    in_specs = [
        pl.BlockSpec(memory_space=pltpu.SMEM),
        edge,
        edge,
        edge,
        edge,
        edge,
        edge,
        met(lambda e: (e * last, 0, 0)),
        met(lambda e: (lat_rows + e * last, 0, 0)),
        met(lambda e: (3 * lat_rows - e * (lat_rows + 2), 0, 0)),
        met(lambda e: (2 * lat_rows + e * last, 0, 0)),
        pl.BlockSpec((tracers, lat_rows, lon), lambda e: (0, 0, 0)),
    ]
    args = [north_open, *rows, south, north, weather, weather, weather, weather, emission]
    if base is None:
        out_specs = [edge, edge]
        out_shape = [jax.ShapeDtypeStruct((tracers, levels, lon), jnp.float32)] * 2
        aliases = {}
        kernel = edge_kernel
    else:
        in_specs.append(pl.BlockSpec(memory_space=pl.ANY))
        args.append(base)
        out_specs = pl.BlockSpec((tracers, 1, levels, lon), lambda e: (0, e * last, 0, 0))
        out_shape = jax.ShapeDtypeStruct(base.shape, base.dtype)
        aliases = {len(args) - 1: 0}
        kernel = lambda *refs: edge_kernel(*refs[:-2], refs[-1])
    grid_spec = pltpu.PrefetchScalarGridSpec(
        num_scalar_prefetch=0, grid=(2,), in_specs=in_specs, out_specs=out_specs
    )
    return pl.pallas_call(
        kernel,
        grid_spec=grid_spec,
        out_shape=out_shape,
        input_output_aliases=aliases,
        compiler_params=pltpu.CompilerParams(dimension_semantics=("arbitrary",)),
    )(*args)


def fused_kernel(north_ref, q_ref, lo_ref, hi_ref, wx_ref, src_ref, o_ref, lo_in_ref, hi_in_ref, coef_ref, mid_ref):
    lat_rows = q_ref.shape[1]
    levels, lon = q_ref.shape[2], q_ref.shape[3]

    @pl.when(pl.program_id(0) == 0)
    def _():
        fill_coefficients(north_ref, wx_ref, coef_ref)

    def stencil(a, qa, qm, qp):
        result = (
            coef_ref[0, a] * qa
            + coef_ref[1, a] * pltpu.roll(qa, lon - 1, 1)
            + coef_ref[2, a] * pltpu.roll(qa, 1, 1)
            + coef_ref[3, a] * qp
            + coef_ref[4, a] * qm
            + coef_ref[5, a] * pltpu.roll(qa, levels - 1, 0)
            + coef_ref[6, a] * pltpu.roll(qa, 1, 0)
        )
        return result, result[0:1] + src_ref[0, a : a + 1, :]

    mid_ref[0] = lo_ref[0]
    mid_ref[lat_rows - 1] = hi_ref[0]
    for a in range(1, lat_rows - 1):
        result, surface = stencil(a, q_ref[0, a], q_ref[0, a - 1], q_ref[0, a + 1])
        mid_ref[a] = result
        mid_ref[a, 0:1, :] = surface
        if a == 1:
            lo_in_ref[0] = mid_ref[a]
        if a == lat_rows - 2:
            hi_in_ref[0] = mid_ref[a]
    for a in range(1, lat_rows - 1):
        result, surface = stencil(a, mid_ref[a], mid_ref[a - 1], mid_ref[a + 1])
        o_ref[0, a] = result
        o_ref[0, a, 0:1, :] = surface


def fused_steps(state, lo, hi, weather, emission, north_open):
    tracers, lat_rows, levels, lon = state.shape
    row = pl.BlockSpec((1, lat_rows, levels, lon), lambda k: (k, 0, 0, 0))
    edge = pl.BlockSpec((1, levels, lon), lambda k: (k, 0, 0))
    grid_spec = pltpu.PrefetchScalarGridSpec(
        num_scalar_prefetch=0,
        grid=(tracers,),
        in_specs=[
            pl.BlockSpec(memory_space=pltpu.SMEM),
            row,
            edge,
            edge,
            pl.BlockSpec(weather.shape[:2] + (lon,), lambda k: (0, 0, 0)),
            pl.BlockSpec((1, lat_rows, lon), lambda k: (k, 0, 0)),
        ],
        out_specs=[row, edge, edge],
        scratch_shapes=[
            pltpu.VMEM((7, lat_rows, levels, lon), jnp.float32),
            pltpu.VMEM((lat_rows, levels, lon), jnp.float32),
        ],
    )
    return pl.pallas_call(
        fused_kernel,
        grid_spec=grid_spec,
        out_shape=[jax.ShapeDtypeStruct(state.shape, state.dtype)]
        + [jax.ShapeDtypeStruct((tracers, levels, lon), state.dtype)] * 2,
        compiler_params=pltpu.CompilerParams(dimension_semantics=("arbitrary",)),
    )(north_open, state, lo, hi, weather, emission)


def on_device(
    tracer_state,
    control,
    prior_tiles,
    tile_index,
    region_map,
    region_sigma,
    zonal_courant,
    meridional_courant,
    vertical_diffusion,
):
    band_count = lax.axis_size("band")
    band_index = lax.axis_index("band")
    tiles_count = prior_tiles.shape[0]
    lat_rows = control.shape[1]

    south_v = passed_along(meridional_courant[-1:], "band", 1)
    pack = packed([zonal_courant, meridional_courant, vertical_diffusion, south_v])
    weather = relay_gather(pack, "tracer")
    held_state, held_control, _ = lax.optimization_barrier((tracer_state, control, pack))
    q_south = passed_along(held_state[:, -1], "band", 1)
    q_north = passed_along(held_state[:, 0], "band", -1)
    shifted = [control]
    for s in range(1, band_count):
        pairs = [(i, (i + s) % band_count) for i in range(band_count)]
        shifted.append(lax.ppermute(held_control, "band", pairs))

    choose = (
        tile_index[:, :, None] == lax.broadcasted_iota(jnp.int32, (1, 1, tiles_count), 2)
    ).astype(jnp.float32)
    own_row = lax.dynamic_slice_in_dim(choose, band_index, 1, 0)[0]
    row_tiles = jnp.einsum("bt,tmn->bmn", own_row, prior_tiles, precision=exact_dot)
    prior_field = None
    for s, part in enumerate(shifted):
        source_band = (band_index - s) % band_count
        tile = lax.dynamic_index_in_dim(row_tiles, source_band, 0, keepdims=False)
        term = jnp.einsum("jm,kmn->kjn", tile, part, precision=exact_dot)
        prior_field = term if prior_field is None else prior_field + term
    regions = region_sigma.shape[1]
    onehot = (region_map[:, :, None] == lax.broadcasted_iota(jnp.int32, (1, 1, regions), 2)).astype(
        jnp.float32
    )
    cell_sigma = jnp.einsum("kr,jnr->kjn", region_sigma, onehot, precision=exact_dot)
    emission = cell_sigma * prior_field

    latitude = band_index * lat_rows + jnp.arange(lat_rows, dtype=jnp.int32)
    north_open = (latitude < band_count * lat_rows - 1).astype(jnp.float32)

    rim = (tracer_state[:, 0], tracer_state[:, lat_rows - 1], tracer_state[:, 1], tracer_state[:, lat_rows - 2])
    bottom_row, top_row = edge_step(rim, None, q_south, q_north, weather, emission, north_open)
    s1_south = passed_along(top_row, "band", 1)
    s1_north = passed_along(bottom_row, "band", -1)
    inside, bottom_in, top_in = fused_steps(tracer_state, bottom_row, top_row, weather, emission, north_open)
    rim = (bottom_row, top_row, bottom_in, top_in)
    tracer_field = edge_step(rim, inside, s1_south, s1_north, weather, emission, north_open)
    return (tracer_field, emission)


def solution(mesh):
    in_specs = (
        P(("inv", "tracer"), "band", None, None),
        P(("inv", "tracer"), "band", None),
        P(),
        P(),
        P("band", None),
        P("tracer", None),
        P(("inv", "band"), None, "tracer"),
        P(("inv", "band"), None, "tracer"),
        P(("inv", "band"), None, "tracer"),
    )
    out_specs = (P(("inv", "tracer"), "band", None, None), P(("inv", "tracer"), "band", None))
    return jax.shard_map(
        on_device, mesh=mesh, in_specs=in_specs, out_specs=out_specs, check_vma=False
    )
```

```python
import functools

import jax
import jax.numpy as jnp
from jax import lax
from jax.experimental import pallas as pl
from jax.experimental.pallas import tpu as pltpu
from jax.sharding import PartitionSpec as P

exact_dot = lax.Precision.HIGHEST


def passed_along(value, axis, by):
    count = lax.axis_size(axis)
    pairs = [(i, i + by) for i in range(count) if 0 <= i + by < count]
    return lax.ppermute(value, axis, pairs)


def pack_kernel(*refs):
    parts, out_ref = refs[:-1], refs[-1]
    row = 0
    for part in parts:
        rows = part.shape[0]
        out_ref[row : row + rows] = part[...]
        row += rows


def packed(parts):
    rows = sum(part.shape[0] for part in parts)
    return pl.pallas_call(
        pack_kernel,
        out_shape=jax.ShapeDtypeStruct((rows,) + parts[0].shape[1:], parts[0].dtype),
    )(*parts)


def relay_gather(x, axis):
    count = lax.axis_size(axis)
    me = lax.axis_index(axis)
    rows, levels, width = x.shape
    buf = jnp.zeros((rows, levels, (count + 1) * width), x.dtype)
    buf = lax.dynamic_update_slice(buf, x, (0, 0, me * width))
    right = left = x
    for r in range(1, count):
        right = lax.ppermute(right, axis, [(i, i + 1) for i in range(r - 1, count - 1)])
        left = lax.ppermute(left, axis, [(j, j - 1) for j in range(1, count - r + 1)])
        slot = jnp.where(me - r >= 0, me - r, count)
        buf = lax.dynamic_update_slice(buf, right, (0, 0, slot * width))
        slot = jnp.where(me + r < count, me + r, count)
        buf = lax.dynamic_update_slice(buf, left, (0, 0, slot * width))
    return buf


def fill_coefficients(north_ref, wx_ref, coef_ref):
    lat_rows = coef_ref.shape[1]
    levels, lon = coef_ref.shape[2], coef_ref.shape[3]
    level = lax.broadcasted_iota(jnp.int32, (levels, lon), 0)
    not_top = level < levels - 1
    not_bottom = level > 0
    for a in range(lat_rows):
        u = wx_ref[a]
        uw = pltpu.roll(u, 1, 1)
        v = wx_ref[lat_rows + a] * north_ref[a]
        vm = wx_ref[3 * lat_rows] if a == 0 else wx_ref[lat_rows + a - 1]
        w = wx_ref[2 * lat_rows + a]
        w_up = jnp.where(not_top, w, 0.0)
        w_down = jnp.where(not_bottom, pltpu.roll(w, 1, 0), 0.0)
        coef_ref[0, a] = (
            1.0
            - jnp.maximum(u, 0.0)
            + jnp.minimum(uw, 0.0)
            - jnp.maximum(v, 0.0)
            + jnp.minimum(vm, 0.0)
            - w_up
            - w_down
        )
        coef_ref[1, a] = -jnp.minimum(u, 0.0)
        coef_ref[2, a] = jnp.maximum(uw, 0.0)
        coef_ref[3, a] = -jnp.minimum(v, 0.0)
        coef_ref[4, a] = jnp.maximum(vm, 0.0)
        coef_ref[5, a] = w_up
        coef_ref[6, a] = w_down


def step_kernel(north_ref, q_ref, qs_ref, qn_ref, wx_ref, src_ref, *rest, rows=None):
    o_ref = rest[0]
    edges = rest[1:-1]
    coef_ref = rest[-1]
    lat_rows = q_ref.shape[1]
    rows = range(lat_rows) if rows is None else rows
    levels, lon = q_ref.shape[2], q_ref.shape[3]
    level = lax.broadcasted_iota(jnp.int32, (levels, lon), 0)
    not_top = level < levels - 1
    not_bottom = level > 0

    @pl.when(pl.program_id(0) == 0)
    def _():
        fill_coefficients(north_ref, wx_ref, coef_ref)

    for a in rows:
        qa = q_ref[0, a]
        qm = qs_ref[0] if a == 0 else q_ref[0, a - 1]
        qp = qn_ref[0] if a == lat_rows - 1 else q_ref[0, a + 1]
        result = (
            coef_ref[0, a] * qa
            + coef_ref[1, a] * pltpu.roll(qa, lon - 1, 1)
            + coef_ref[2, a] * pltpu.roll(qa, 1, 1)
            + coef_ref[3, a] * qp
            + coef_ref[4, a] * qm
            + coef_ref[5, a] * pltpu.roll(qa, levels - 1, 0)
            + coef_ref[6, a] * pltpu.roll(qa, 1, 0)
        )
        surface = result[0:1] + src_ref[0, a : a + 1, :]
        targets = [o_ref.at[0, a]]
        if edges and a == 0:
            targets.append(edges[0].at[0])
        if edges and a == lat_rows - 1:
            targets.append(edges[1].at[0])
        for target in targets:
            target[...] = result
            target[0:1, :] = surface


def advance(state, south, north, weather, emission, north_open, with_edges):
    tracers, lat_rows, levels, lon = state.shape
    row = pl.BlockSpec((1, lat_rows, levels, lon), lambda k: (k, 0, 0, 0))
    edge = pl.BlockSpec((1, levels, lon), lambda k: (k, 0, 0))
    out_specs = [row]
    out_shape = [jax.ShapeDtypeStruct(state.shape, state.dtype)]
    if with_edges:
        out_specs += [edge, edge]
        out_shape += [jax.ShapeDtypeStruct((tracers, levels, lon), state.dtype)] * 2
    grid_spec = pltpu.PrefetchScalarGridSpec(
        num_scalar_prefetch=0,
        grid=(tracers,),
        in_specs=[
            pl.BlockSpec(memory_space=pltpu.SMEM),
            row,
            edge,
            edge,
            pl.BlockSpec(weather.shape[:2] + (lon,), lambda k: (0, 0, 0)),
            pl.BlockSpec((1, lat_rows, lon), lambda k: (k, 0, 0)),
        ],
        out_specs=out_specs,
        scratch_shapes=[pltpu.VMEM((7, lat_rows, levels, lon), jnp.float32)],
    )
    return pl.pallas_call(
        step_kernel,
        grid_spec=grid_spec,
        out_shape=out_shape,
        compiler_params=pltpu.CompilerParams(dimension_semantics=("arbitrary",)),
    )(north_open, state, south, north, weather, emission)


def interior_step(state, weather, emission, north_open):
    tracers, lat_rows, levels, lon = state.shape
    row = pl.BlockSpec((1, lat_rows, levels, lon), lambda k: (k, 0, 0, 0))
    kernel = functools.partial(
        lambda n, q, w, e, o, c, rows: step_kernel(n, q, None, None, w, e, o, c, rows=rows),
        rows=range(1, lat_rows - 1),
    )
    grid_spec = pltpu.PrefetchScalarGridSpec(
        num_scalar_prefetch=0,
        grid=(tracers,),
        in_specs=[
            pl.BlockSpec(memory_space=pltpu.SMEM),
            row,
            pl.BlockSpec(weather.shape[:2] + (lon,), lambda k: (0, 0, 0)),
            pl.BlockSpec((1, lat_rows, lon), lambda k: (k, 0, 0)),
        ],
        out_specs=row,
        scratch_shapes=[pltpu.VMEM((7, lat_rows, levels, lon), jnp.float32)],
    )
    return pl.pallas_call(
        kernel,
        grid_spec=grid_spec,
        out_shape=jax.ShapeDtypeStruct(state.shape, state.dtype),
        compiler_params=pltpu.CompilerParams(dimension_semantics=("arbitrary",)),
    )(north_open, state, weather, emission)


def edge_kernel(north_ref, lo_ref, hi_ref, lo_in_ref, hi_in_ref, qs_ref, qn_ref, u_ref, v_ref, vm_ref, w_ref, src_ref, *outs):
    split = len(outs) == 2
    tracers, lat_rows = src_ref.shape[0], src_ref.shape[1]
    levels, lon = lo_ref.shape[1], lo_ref.shape[2]
    top = pl.program_id(0)
    level = lax.broadcasted_iota(jnp.int32, (levels, lon), 0)
    not_top = level < levels - 1
    not_bottom = level > 0
    a = top * (lat_rows - 1)
    is_top = jnp.full((levels, lon), top, jnp.int32) == 1
    u = u_ref[0]
    uw = pltpu.roll(u, 1, 1)
    v = v_ref[0] * north_ref[a]
    vm = vm_ref[0]
    w = w_ref[0]
    w_up = jnp.where(not_top, w, 0.0)
    w_down = jnp.where(not_bottom, pltpu.roll(w, 1, 0), 0.0)
    c_self = (
        1.0
        - jnp.maximum(u, 0.0)
        + jnp.minimum(uw, 0.0)
        - jnp.maximum(v, 0.0)
        + jnp.minimum(vm, 0.0)
        - w_up
        - w_down
    )
    c_east = -jnp.minimum(u, 0.0)
    c_west = jnp.maximum(uw, 0.0)
    c_north = -jnp.minimum(v, 0.0)
    c_south = jnp.maximum(vm, 0.0)
    at_top = jnp.full((1, lon), top, jnp.int32) == 1
    for k in range(tracers):
        qa = jnp.where(is_top, hi_ref[k], lo_ref[k])
        inner = jnp.where(is_top, hi_in_ref[k], lo_in_ref[k])
        qm = jnp.where(is_top, inner, qs_ref[k])
        qp = jnp.where(is_top, qn_ref[k], inner)
        result = (
            c_self * qa
            + c_east * pltpu.roll(qa, lon - 1, 1)
            + c_west * pltpu.roll(qa, 1, 1)
            + c_north * qp
            + c_south * qm
            + w_up * pltpu.roll(qa, levels - 1, 0)
            + w_down * pltpu.roll(qa, 1, 0)
        )
        source = jnp.where(at_top, src_ref[k, lat_rows - 1 : lat_rows, :], src_ref[k, 0:1, :])
        surface = result[0:1] + source
        if split:

            def put(ref, result=result, surface=surface, k=k):
                ref[k] = result
                ref[k, 0:1, :] = surface

            pl.when(top == 0)(functools.partial(put, outs[0]))
            pl.when(top == 1)(functools.partial(put, outs[1]))
        else:
            outs[-1][k, 0] = result
            outs[-1][k, 0, 0:1, :] = surface


def edge_step(rows, base, south, north, weather, emission, north_open):
    tracers, levels, lon = rows[0].shape
    lat_rows = emission.shape[1]
    last = lat_rows - 1
    edge = pl.BlockSpec((tracers, levels, lon), lambda e: (0, 0, 0))
    met = lambda index: pl.BlockSpec((1, levels, lon), index)
    in_specs = [
        pl.BlockSpec(memory_space=pltpu.SMEM),
        edge,
        edge,
        edge,
        edge,
        edge,
        edge,
        met(lambda e: (e * last, 0, 0)),
        met(lambda e: (lat_rows + e * last, 0, 0)),
        met(lambda e: (3 * lat_rows - e * (lat_rows + 2), 0, 0)),
        met(lambda e: (2 * lat_rows + e * last, 0, 0)),
        pl.BlockSpec((tracers, lat_rows, lon), lambda e: (0, 0, 0)),
    ]
    args = [north_open, *rows, south, north, weather, weather, weather, weather, emission]
    if base is None:
        out_specs = [edge, edge]
        out_shape = [jax.ShapeDtypeStruct((tracers, levels, lon), jnp.float32)] * 2
        aliases = {}
        kernel = edge_kernel
    else:
        in_specs.append(pl.BlockSpec(memory_space=pl.ANY))
        args.append(base)
        out_specs = pl.BlockSpec((tracers, 1, levels, lon), lambda e: (0, e * last, 0, 0))
        out_shape = jax.ShapeDtypeStruct(base.shape, base.dtype)
        aliases = {len(args) - 1: 0}
        kernel = lambda *refs: edge_kernel(*refs[:-2], refs[-1])
    grid_spec = pltpu.PrefetchScalarGridSpec(
        num_scalar_prefetch=0, grid=(2,), in_specs=in_specs, out_specs=out_specs
    )
    return pl.pallas_call(
        kernel,
        grid_spec=grid_spec,
        out_shape=out_shape,
        input_output_aliases=aliases,
        compiler_params=pltpu.CompilerParams(dimension_semantics=("arbitrary",)),
    )(*args)


def fused_kernel(north_ref, q_ref, lo_ref, hi_ref, wx_ref, src_ref, o_ref, lo_in_ref, hi_in_ref, coef_ref, mid_ref):
    lat_rows = q_ref.shape[1]
    levels, lon = q_ref.shape[2], q_ref.shape[3]

    @pl.when(pl.program_id(0) == 0)
    def _():
        fill_coefficients(north_ref, wx_ref, coef_ref)

    def stencil(a, qa, qm, qp):
        result = (
            coef_ref[0, a] * qa
            + coef_ref[1, a] * pltpu.roll(qa, lon - 1, 1)
            + coef_ref[2, a] * pltpu.roll(qa, 1, 1)
            + coef_ref[3, a] * qp
            + coef_ref[4, a] * qm
            + coef_ref[5, a] * pltpu.roll(qa, levels - 1, 0)
            + coef_ref[6, a] * pltpu.roll(qa, 1, 0)
        )
        return result, result[0:1] + src_ref[0, a : a + 1, :]

    mid_ref[0] = lo_ref[0]
    mid_ref[lat_rows - 1] = hi_ref[0]
    for a in range(1, lat_rows - 1):
        result, surface = stencil(a, q_ref[0, a], q_ref[0, a - 1], q_ref[0, a + 1])
        mid_ref[a] = result
        mid_ref[a, 0:1, :] = surface
        if a == 1:
            lo_in_ref[0] = mid_ref[a]
        if a == lat_rows - 2:
            hi_in_ref[0] = mid_ref[a]
    for a in range(1, lat_rows - 1):
        result, surface = stencil(a, mid_ref[a], mid_ref[a - 1], mid_ref[a + 1])
        o_ref[0, a] = result
        o_ref[0, a, 0:1, :] = surface


def fused_steps(state, lo, hi, weather, emission, north_open):
    tracers, lat_rows, levels, lon = state.shape
    row = pl.BlockSpec((1, lat_rows, levels, lon), lambda k: (k, 0, 0, 0))
    edge = pl.BlockSpec((1, levels, lon), lambda k: (k, 0, 0))
    grid_spec = pltpu.PrefetchScalarGridSpec(
        num_scalar_prefetch=0,
        grid=(tracers,),
        in_specs=[
            pl.BlockSpec(memory_space=pltpu.SMEM),
            row,
            edge,
            edge,
            pl.BlockSpec(weather.shape[:2] + (lon,), lambda k: (0, 0, 0)),
            pl.BlockSpec((1, lat_rows, lon), lambda k: (k, 0, 0)),
        ],
        out_specs=[row, edge, edge],
        scratch_shapes=[
            pltpu.VMEM((7, lat_rows, levels, lon), jnp.float32),
            pltpu.VMEM((lat_rows, levels, lon), jnp.float32),
        ],
    )
    return pl.pallas_call(
        fused_kernel,
        grid_spec=grid_spec,
        out_shape=[jax.ShapeDtypeStruct(state.shape, state.dtype)]
        + [jax.ShapeDtypeStruct((tracers, levels, lon), state.dtype)] * 2,
        compiler_params=pltpu.CompilerParams(dimension_semantics=("arbitrary",)),
    )(north_open, state, lo, hi, weather, emission)


def on_device(
    tracer_state,
    control,
    prior_tiles,
    tile_index,
    region_map,
    region_sigma,
    zonal_courant,
    meridional_courant,
    vertical_diffusion,
):
    band_count = lax.axis_size("band")
    band_index = lax.axis_index("band")
    tiles_count = prior_tiles.shape[0]
    lat_rows = control.shape[1]

    latitude = band_index * lat_rows + jnp.arange(lat_rows, dtype=jnp.int32)
    north_open = (latitude < band_count * lat_rows - 1).astype(jnp.float32)
    choose = (
        tile_index[:, :, None] == lax.broadcasted_iota(jnp.int32, (1, 1, tiles_count), 2)
    ).astype(jnp.float32)
    own_row = lax.dynamic_slice_in_dim(choose, band_index, 1, 0)[0]
    row_tiles = jnp.einsum("bt,tmn->bmn", own_row, prior_tiles, precision=exact_dot)
    own_tile = lax.dynamic_index_in_dim(row_tiles, band_index, 0, keepdims=False)
    prior_field = jnp.einsum("jm,kmn->kjn", own_tile, control, precision=exact_dot)
    south_v = passed_along(meridional_courant[-1:], "band", 1)
    parts, (north_open, row_tiles, prior_field) = lax.optimization_barrier(
        ((zonal_courant, meridional_courant, vertical_diffusion, south_v), (north_open, row_tiles, prior_field))
    )
    pack = packed(list(parts))
    weather = relay_gather(pack, "tracer")
    held_state, held_control, _ = lax.optimization_barrier((tracer_state, control, pack))
    q_south = passed_along(held_state[:, -1], "band", 1)
    q_north = passed_along(held_state[:, 0], "band", -1)
    for s in range(1, band_count):
        pairs = [(i, (i + s) % band_count) for i in range(band_count)]
        part = lax.ppermute(held_control, "band", pairs)
        source_band = (band_index - s) % band_count
        tile = lax.dynamic_index_in_dim(row_tiles, source_band, 0, keepdims=False)
        prior_field = prior_field + jnp.einsum("jm,kmn->kjn", tile, part, precision=exact_dot)
    regions = region_sigma.shape[1]
    onehot = (region_map[:, :, None] == lax.broadcasted_iota(jnp.int32, (1, 1, regions), 2)).astype(
        jnp.float32
    )
    cell_sigma = jnp.einsum("kr,jnr->kjn", region_sigma, onehot, precision=exact_dot)
    emission = cell_sigma * prior_field

    rim = (tracer_state[:, 0], tracer_state[:, lat_rows - 1], tracer_state[:, 1], tracer_state[:, lat_rows - 2])
    bottom_row, top_row = edge_step(rim, None, q_south, q_north, weather, emission, north_open)
    s1_south = passed_along(top_row, "band", 1)
    s1_north = passed_along(bottom_row, "band", -1)
    inside, bottom_in, top_in = fused_steps(tracer_state, bottom_row, top_row, weather, emission, north_open)
    rim = (bottom_row, top_row, bottom_in, top_in)
    tracer_field = edge_step(rim, inside, s1_south, s1_north, weather, emission, north_open)
    return (tracer_field, emission)


def solution(mesh):
    in_specs = (
        P(("inv", "tracer"), "band", None, None),
        P(("inv", "tracer"), "band", None),
        P(),
        P(),
        P("band", None),
        P("tracer", None),
        P(("inv", "band"), None, "tracer"),
        P(("inv", "band"), None, "tracer"),
        P(("inv", "band"), None, "tracer"),
    )
    out_specs = (P(("inv", "tracer"), "band", None, None), P(("inv", "tracer"), "band", None))
    return jax.shard_map(
        on_device, mesh=mesh, in_specs=in_specs, out_specs=out_specs, check_vma=False
    )
```

```python
import functools

import jax
import jax.numpy as jnp
from jax import lax
from jax.experimental import pallas as pl
from jax.experimental.pallas import tpu as pltpu
from jax.sharding import PartitionSpec as P

exact_dot = lax.Precision.HIGHEST


def passed_along(value, axis, by):
    count = lax.axis_size(axis)
    pairs = [(i, i + by) for i in range(count) if 0 <= i + by < count]
    return lax.ppermute(value, axis, pairs)


def pack_kernel(*refs):
    parts, out_ref = refs[:-1], refs[-1]
    row = 0
    for part in parts:
        rows = part.shape[0]
        out_ref[row : row + rows] = part[...]
        row += rows


def packed(parts):
    rows = sum(part.shape[0] for part in parts)
    return pl.pallas_call(
        pack_kernel,
        out_shape=jax.ShapeDtypeStruct((rows,) + parts[0].shape[1:], parts[0].dtype),
    )(*parts)


def relay_gather(x, axis):
    count = lax.axis_size(axis)
    me = lax.axis_index(axis)
    rows, levels, width = x.shape
    buf = jnp.zeros((rows, levels, (count + 1) * width), x.dtype)
    buf = lax.dynamic_update_slice(buf, x, (0, 0, me * width))
    right = left = x
    for r in range(1, count):
        right = lax.ppermute(right, axis, [(i, i + 1) for i in range(r - 1, count - 1)])
        left = lax.ppermute(left, axis, [(j, j - 1) for j in range(1, count - r + 1)])
        slot = jnp.where(me - r >= 0, me - r, count)
        buf = lax.dynamic_update_slice(buf, right, (0, 0, slot * width))
        slot = jnp.where(me + r < count, me + r, count)
        buf = lax.dynamic_update_slice(buf, left, (0, 0, slot * width))
    return buf


def fill_coefficients(north_ref, wx_ref, coef_ref):
    lat_rows = coef_ref.shape[1]
    levels, lon = coef_ref.shape[2], coef_ref.shape[3]
    level = lax.broadcasted_iota(jnp.int32, (levels, lon), 0)
    not_top = level < levels - 1
    not_bottom = level > 0
    for a in range(lat_rows):
        u = wx_ref[a]
        uw = pltpu.roll(u, 1, 1)
        v = wx_ref[lat_rows + a] * north_ref[a]
        vm = wx_ref[3 * lat_rows] if a == 0 else wx_ref[lat_rows + a - 1]
        w = wx_ref[2 * lat_rows + a]
        w_up = jnp.where(not_top, w, 0.0)
        w_down = jnp.where(not_bottom, pltpu.roll(w, 1, 0), 0.0)
        coef_ref[0, a] = (
            1.0
            - jnp.maximum(u, 0.0)
            + jnp.minimum(uw, 0.0)
            - jnp.maximum(v, 0.0)
            + jnp.minimum(vm, 0.0)
            - w_up
            - w_down
        )
        coef_ref[1, a] = -jnp.minimum(u, 0.0)
        coef_ref[2, a] = jnp.maximum(uw, 0.0)
        coef_ref[3, a] = -jnp.minimum(v, 0.0)
        coef_ref[4, a] = jnp.maximum(vm, 0.0)
        coef_ref[5, a] = w_up
        coef_ref[6, a] = w_down


def step_kernel(north_ref, q_ref, qs_ref, qn_ref, wx_ref, src_ref, *rest, rows=None):
    o_ref = rest[0]
    edges = rest[1:-1]
    coef_ref = rest[-1]
    lat_rows = q_ref.shape[1]
    rows = range(lat_rows) if rows is None else rows
    levels, lon = q_ref.shape[2], q_ref.shape[3]
    level = lax.broadcasted_iota(jnp.int32, (levels, lon), 0)
    not_top = level < levels - 1
    not_bottom = level > 0

    @pl.when(pl.program_id(0) == 0)
    def _():
        fill_coefficients(north_ref, wx_ref, coef_ref)

    for a in rows:
        qa = q_ref[0, a]
        qm = qs_ref[0] if a == 0 else q_ref[0, a - 1]
        qp = qn_ref[0] if a == lat_rows - 1 else q_ref[0, a + 1]
        result = (
            coef_ref[0, a] * qa
            + coef_ref[1, a] * pltpu.roll(qa, lon - 1, 1)
            + coef_ref[2, a] * pltpu.roll(qa, 1, 1)
            + coef_ref[3, a] * qp
            + coef_ref[4, a] * qm
            + coef_ref[5, a] * pltpu.roll(qa, levels - 1, 0)
            + coef_ref[6, a] * pltpu.roll(qa, 1, 0)
        )
        surface = result[0:1] + src_ref[0, a : a + 1, :]
        targets = [o_ref.at[0, a]]
        if edges and a == 0:
            targets.append(edges[0].at[0])
        if edges and a == lat_rows - 1:
            targets.append(edges[1].at[0])
        for target in targets:
            target[...] = result
            target[0:1, :] = surface


def advance(state, south, north, weather, emission, north_open, with_edges):
    tracers, lat_rows, levels, lon = state.shape
    row = pl.BlockSpec((1, lat_rows, levels, lon), lambda k: (k, 0, 0, 0))
    edge = pl.BlockSpec((1, levels, lon), lambda k: (k, 0, 0))
    out_specs = [row]
    out_shape = [jax.ShapeDtypeStruct(state.shape, state.dtype)]
    if with_edges:
        out_specs += [edge, edge]
        out_shape += [jax.ShapeDtypeStruct((tracers, levels, lon), state.dtype)] * 2
    grid_spec = pltpu.PrefetchScalarGridSpec(
        num_scalar_prefetch=0,
        grid=(tracers,),
        in_specs=[
            pl.BlockSpec(memory_space=pltpu.SMEM),
            row,
            edge,
            edge,
            pl.BlockSpec(weather.shape[:2] + (lon,), lambda k: (0, 0, 0)),
            pl.BlockSpec((1, lat_rows, lon), lambda k: (k, 0, 0)),
        ],
        out_specs=out_specs,
        scratch_shapes=[pltpu.VMEM((7, lat_rows, levels, lon), jnp.float32)],
    )
    return pl.pallas_call(
        step_kernel,
        grid_spec=grid_spec,
        out_shape=out_shape,
        compiler_params=pltpu.CompilerParams(dimension_semantics=("arbitrary",)),
    )(north_open, state, south, north, weather, emission)


def interior_step(state, weather, emission, north_open):
    tracers, lat_rows, levels, lon = state.shape
    row = pl.BlockSpec((1, lat_rows, levels, lon), lambda k: (k, 0, 0, 0))
    kernel = functools.partial(
        lambda n, q, w, e, o, c, rows: step_kernel(n, q, None, None, w, e, o, c, rows=rows),
        rows=range(1, lat_rows - 1),
    )
    grid_spec = pltpu.PrefetchScalarGridSpec(
        num_scalar_prefetch=0,
        grid=(tracers,),
        in_specs=[
            pl.BlockSpec(memory_space=pltpu.SMEM),
            row,
            pl.BlockSpec(weather.shape[:2] + (lon,), lambda k: (0, 0, 0)),
            pl.BlockSpec((1, lat_rows, lon), lambda k: (k, 0, 0)),
        ],
        out_specs=row,
        scratch_shapes=[pltpu.VMEM((7, lat_rows, levels, lon), jnp.float32)],
    )
    return pl.pallas_call(
        kernel,
        grid_spec=grid_spec,
        out_shape=jax.ShapeDtypeStruct(state.shape, state.dtype),
        compiler_params=pltpu.CompilerParams(dimension_semantics=("arbitrary",)),
    )(north_open, state, weather, emission)


def edge_kernel(north_ref, lo_ref, hi_ref, lo_in_ref, hi_in_ref, qs_ref, qn_ref, u_ref, v_ref, vm_ref, w_ref, src_ref, *outs):
    split = len(outs) == 2
    tracers, lat_rows = src_ref.shape[0], src_ref.shape[1]
    levels, lon = lo_ref.shape[1], lo_ref.shape[2]
    top = pl.program_id(0)
    level = lax.broadcasted_iota(jnp.int32, (levels, lon), 0)
    not_top = level < levels - 1
    not_bottom = level > 0
    a = top * (lat_rows - 1)
    is_top = jnp.full((levels, lon), top, jnp.int32) == 1
    u = u_ref[0]
    uw = pltpu.roll(u, 1, 1)
    v = v_ref[0] * north_ref[a]
    vm = vm_ref[0]
    w = w_ref[0]
    w_up = jnp.where(not_top, w, 0.0)
    w_down = jnp.where(not_bottom, pltpu.roll(w, 1, 0), 0.0)
    c_self = (
        1.0
        - jnp.maximum(u, 0.0)
        + jnp.minimum(uw, 0.0)
        - jnp.maximum(v, 0.0)
        + jnp.minimum(vm, 0.0)
        - w_up
        - w_down
    )
    c_east = -jnp.minimum(u, 0.0)
    c_west = jnp.maximum(uw, 0.0)
    c_north = -jnp.minimum(v, 0.0)
    c_south = jnp.maximum(vm, 0.0)
    at_top = jnp.full((1, lon), top, jnp.int32) == 1
    for k in range(tracers):
        qa = jnp.where(is_top, hi_ref[k], lo_ref[k])
        inner = jnp.where(is_top, hi_in_ref[k], lo_in_ref[k])
        qm = jnp.where(is_top, inner, qs_ref[k])
        qp = jnp.where(is_top, qn_ref[k], inner)
        result = (
            c_self * qa
            + c_east * pltpu.roll(qa, lon - 1, 1)
            + c_west * pltpu.roll(qa, 1, 1)
            + c_north * qp
            + c_south * qm
            + w_up * pltpu.roll(qa, levels - 1, 0)
            + w_down * pltpu.roll(qa, 1, 0)
        )
        source = jnp.where(at_top, src_ref[k, lat_rows - 1 : lat_rows, :], src_ref[k, 0:1, :])
        surface = result[0:1] + source
        if split:

            def put(ref, result=result, surface=surface, k=k):
                ref[k] = result
                ref[k, 0:1, :] = surface

            pl.when(top == 0)(functools.partial(put, outs[0]))
            pl.when(top == 1)(functools.partial(put, outs[1]))
        else:
            outs[-1][k, 0] = result
            outs[-1][k, 0, 0:1, :] = surface


def edge_step(rows, base, south, north, weather, emission, north_open):
    tracers, levels, lon = rows[0].shape
    lat_rows = emission.shape[1]
    last = lat_rows - 1
    edge = pl.BlockSpec((tracers, levels, lon), lambda e: (0, 0, 0))
    met = lambda index: pl.BlockSpec((1, levels, lon), index)
    in_specs = [
        pl.BlockSpec(memory_space=pltpu.SMEM),
        edge,
        edge,
        edge,
        edge,
        edge,
        edge,
        met(lambda e: (e * last, 0, 0)),
        met(lambda e: (lat_rows + e * last, 0, 0)),
        met(lambda e: (3 * lat_rows - e * (lat_rows + 2), 0, 0)),
        met(lambda e: (2 * lat_rows + e * last, 0, 0)),
        pl.BlockSpec((tracers, lat_rows, lon), lambda e: (0, 0, 0)),
    ]
    args = [north_open, *rows, south, north, weather, weather, weather, weather, emission]
    if base is None:
        out_specs = [edge, edge]
        out_shape = [jax.ShapeDtypeStruct((tracers, levels, lon), jnp.float32)] * 2
        aliases = {}
        kernel = edge_kernel
    else:
        in_specs.append(pl.BlockSpec(memory_space=pl.ANY))
        args.append(base)
        out_specs = pl.BlockSpec((tracers, 1, levels, lon), lambda e: (0, e * last, 0, 0))
        out_shape = jax.ShapeDtypeStruct(base.shape, base.dtype)
        aliases = {len(args) - 1: 0}
        kernel = lambda *refs: edge_kernel(*refs[:-2], refs[-1])
    grid_spec = pltpu.PrefetchScalarGridSpec(
        num_scalar_prefetch=0, grid=(2,), in_specs=in_specs, out_specs=out_specs
    )
    return pl.pallas_call(
        kernel,
        grid_spec=grid_spec,
        out_shape=out_shape,
        input_output_aliases=aliases,
        compiler_params=pltpu.CompilerParams(dimension_semantics=("arbitrary",)),
    )(*args)


def fused_kernel(north_ref, q_ref, lo_ref, hi_ref, wx_ref, src_ref, o_ref, lo_in_ref, hi_in_ref, coef_ref, mid_ref):
    lat_rows = q_ref.shape[1]
    levels, lon = q_ref.shape[2], q_ref.shape[3]

    @pl.when(pl.program_id(0) == 0)
    def _():
        fill_coefficients(north_ref, wx_ref, coef_ref)

    def stencil(a, qa, qm, qp):
        result = (
            coef_ref[0, a] * qa
            + coef_ref[1, a] * pltpu.roll(qa, lon - 1, 1)
            + coef_ref[2, a] * pltpu.roll(qa, 1, 1)
            + coef_ref[3, a] * qp
            + coef_ref[4, a] * qm
            + coef_ref[5, a] * pltpu.roll(qa, levels - 1, 0)
            + coef_ref[6, a] * pltpu.roll(qa, 1, 0)
        )
        return result, result[0:1] + src_ref[0, a : a + 1, :]

    mid_ref[0] = lo_ref[0]
    mid_ref[lat_rows - 1] = hi_ref[0]
    for a in range(1, lat_rows - 1):
        result, surface = stencil(a, q_ref[0, a], q_ref[0, a - 1], q_ref[0, a + 1])
        mid_ref[a] = result
        mid_ref[a, 0:1, :] = surface
        if a == 1:
            lo_in_ref[0] = mid_ref[a]
        if a == lat_rows - 2:
            hi_in_ref[0] = mid_ref[a]
    for a in range(1, lat_rows - 1):
        result, surface = stencil(a, mid_ref[a], mid_ref[a - 1], mid_ref[a + 1])
        o_ref[0, a] = result
        o_ref[0, a, 0:1, :] = surface


def fused_steps(state, lo, hi, weather, emission, north_open):
    tracers, lat_rows, levels, lon = state.shape
    row = pl.BlockSpec((1, lat_rows, levels, lon), lambda k: (k, 0, 0, 0))
    edge = pl.BlockSpec((1, levels, lon), lambda k: (k, 0, 0))
    grid_spec = pltpu.PrefetchScalarGridSpec(
        num_scalar_prefetch=0,
        grid=(tracers,),
        in_specs=[
            pl.BlockSpec(memory_space=pltpu.SMEM),
            row,
            edge,
            edge,
            pl.BlockSpec(weather.shape[:2] + (lon,), lambda k: (0, 0, 0)),
            pl.BlockSpec((1, lat_rows, lon), lambda k: (k, 0, 0)),
        ],
        out_specs=[row, edge, edge],
        scratch_shapes=[
            pltpu.VMEM((7, lat_rows, levels, lon), jnp.float32),
            pltpu.VMEM((lat_rows, levels, lon), jnp.float32),
        ],
    )
    return pl.pallas_call(
        fused_kernel,
        grid_spec=grid_spec,
        out_shape=[jax.ShapeDtypeStruct(state.shape, state.dtype)]
        + [jax.ShapeDtypeStruct((tracers, levels, lon), state.dtype)] * 2,
        compiler_params=pltpu.CompilerParams(dimension_semantics=("arbitrary",)),
    )(north_open, state, lo, hi, weather, emission)


def on_device(
    tracer_state,
    control,
    prior_tiles,
    tile_index,
    region_map,
    region_sigma,
    zonal_courant,
    meridional_courant,
    vertical_diffusion,
):
    band_count = lax.axis_size("band")
    band_index = lax.axis_index("band")
    tiles_count = prior_tiles.shape[0]
    lat_rows = control.shape[1]

    latitude = band_index * lat_rows + jnp.arange(lat_rows, dtype=jnp.int32)
    north_open = (latitude < band_count * lat_rows - 1).astype(jnp.float32)
    choose = (
        tile_index[:, :, None] == lax.broadcasted_iota(jnp.int32, (1, 1, tiles_count), 2)
    ).astype(jnp.float32)
    own_row = lax.dynamic_slice_in_dim(choose, band_index, 1, 0)[0]
    row_tiles = jnp.einsum("bt,tmn->bmn", own_row, prior_tiles, precision=exact_dot)
    own_tile = lax.dynamic_index_in_dim(row_tiles, band_index, 0, keepdims=False)
    prior_field = jnp.einsum("jm,kmn->kjn", own_tile, control, precision=exact_dot)
    south_v = passed_along(meridional_courant[-1:], "band", 1)
    rim = (tracer_state[:, 0], tracer_state[:, lat_rows - 1], tracer_state[:, 1], tracer_state[:, lat_rows - 2])
    parts, (north_open, row_tiles, prior_field, rim) = lax.optimization_barrier(
        ((zonal_courant, meridional_courant, vertical_diffusion, south_v), (north_open, row_tiles, prior_field, rim))
    )
    pack = packed(list(parts))
    weather = relay_gather(pack, "tracer")
    held_state, held_control, _ = lax.optimization_barrier((tracer_state, control, pack))
    q_south = passed_along(held_state[:, -1], "band", 1)
    q_north = passed_along(held_state[:, 0], "band", -1)
    for s in range(1, band_count):
        pairs = [(i, (i + s) % band_count) for i in range(band_count)]
        part = lax.ppermute(held_control, "band", pairs)
        source_band = (band_index - s) % band_count
        tile = lax.dynamic_index_in_dim(row_tiles, source_band, 0, keepdims=False)
        prior_field = prior_field + jnp.einsum("jm,kmn->kjn", tile, part, precision=exact_dot)
    regions = region_sigma.shape[1]
    onehot = (region_map[:, :, None] == lax.broadcasted_iota(jnp.int32, (1, 1, regions), 2)).astype(
        jnp.float32
    )
    cell_sigma = jnp.einsum("kr,jnr->kjn", region_sigma, onehot, precision=exact_dot)
    emission = cell_sigma * prior_field

    bottom_row, top_row = edge_step(rim, None, q_south, q_north, weather, emission, north_open)
    s1_south = passed_along(top_row, "band", 1)
    s1_north = passed_along(bottom_row, "band", -1)
    inside, bottom_in, top_in = fused_steps(tracer_state, bottom_row, top_row, weather, emission, north_open)
    rim = (bottom_row, top_row, bottom_in, top_in)
    tracer_field = edge_step(rim, inside, s1_south, s1_north, weather, emission, north_open)
    return (tracer_field, emission)


def solution(mesh):
    in_specs = (
        P(("inv", "tracer"), "band", None, None),
        P(("inv", "tracer"), "band", None),
        P(),
        P(),
        P("band", None),
        P("tracer", None),
        P(("inv", "band"), None, "tracer"),
        P(("inv", "band"), None, "tracer"),
        P(("inv", "band"), None, "tracer"),
    )
    out_specs = (P(("inv", "tracer"), "band", None, None), P(("inv", "tracer"), "band", None))
    return jax.shard_map(
        on_device, mesh=mesh, in_specs=in_specs, out_specs=out_specs, check_vma=False
    )
```

```python
import functools

import jax
import jax.numpy as jnp
from jax import lax
from jax.experimental import pallas as pl
from jax.experimental.pallas import tpu as pltpu
from jax.sharding import PartitionSpec as P

exact_dot = lax.Precision.HIGHEST


def passed_along(value, axis, by):
    count = lax.axis_size(axis)
    pairs = [(i, i + by) for i in range(count) if 0 <= i + by < count]
    return lax.ppermute(value, axis, pairs)


def pack_kernel(*refs):
    parts, out_ref = refs[:-1], refs[-1]
    row = 0
    for part in parts:
        rows = part.shape[0]
        out_ref[row : row + rows] = part[...]
        row += rows


def packed(parts):
    rows = sum(part.shape[0] for part in parts)
    return pl.pallas_call(
        pack_kernel,
        out_shape=jax.ShapeDtypeStruct((rows,) + parts[0].shape[1:], parts[0].dtype),
    )(*parts)


def relay_gather(x, axis):
    count = lax.axis_size(axis)
    me = lax.axis_index(axis)
    rows, levels, width = x.shape
    buf = jnp.zeros((rows, levels, (count + 1) * width), x.dtype)
    buf = lax.dynamic_update_slice(buf, x, (0, 0, me * width))
    right = left = x
    for r in range(1, count):
        right = lax.ppermute(right, axis, [(i, i + 1) for i in range(r - 1, count - 1)])
        left = lax.ppermute(left, axis, [(j, j - 1) for j in range(1, count - r + 1)])
        slot = jnp.where(me - r >= 0, me - r, count)
        buf = lax.dynamic_update_slice(buf, right, (0, 0, slot * width))
        slot = jnp.where(me + r < count, me + r, count)
        buf = lax.dynamic_update_slice(buf, left, (0, 0, slot * width))
    return buf


def fill_coefficients(north_ref, wx_ref, coef_ref):
    lat_rows = coef_ref.shape[1]
    levels, lon = coef_ref.shape[2], coef_ref.shape[3]
    level = lax.broadcasted_iota(jnp.int32, (levels, lon), 0)
    not_top = level < levels - 1
    not_bottom = level > 0
    for a in range(lat_rows):
        u = wx_ref[a]
        uw = pltpu.roll(u, 1, 1)
        v = wx_ref[lat_rows + a] * north_ref[a]
        vm = wx_ref[3 * lat_rows] if a == 0 else wx_ref[lat_rows + a - 1]
        w = wx_ref[2 * lat_rows + a]
        w_up = jnp.where(not_top, w, 0.0)
        w_down = jnp.where(not_bottom, pltpu.roll(w, 1, 0), 0.0)
        coef_ref[0, a] = (
            1.0
            - jnp.maximum(u, 0.0)
            + jnp.minimum(uw, 0.0)
            - jnp.maximum(v, 0.0)
            + jnp.minimum(vm, 0.0)
            - w_up
            - w_down
        )
        coef_ref[1, a] = -jnp.minimum(u, 0.0)
        coef_ref[2, a] = jnp.maximum(uw, 0.0)
        coef_ref[3, a] = -jnp.minimum(v, 0.0)
        coef_ref[4, a] = jnp.maximum(vm, 0.0)
        coef_ref[5, a] = w_up
        coef_ref[6, a] = w_down


def step_kernel(north_ref, q_ref, qs_ref, qn_ref, wx_ref, src_ref, *rest, rows=None):
    o_ref = rest[0]
    edges = rest[1:-1]
    coef_ref = rest[-1]
    lat_rows = q_ref.shape[1]
    rows = range(lat_rows) if rows is None else rows
    levels, lon = q_ref.shape[2], q_ref.shape[3]
    level = lax.broadcasted_iota(jnp.int32, (levels, lon), 0)
    not_top = level < levels - 1
    not_bottom = level > 0

    @pl.when(pl.program_id(0) == 0)
    def _():
        fill_coefficients(north_ref, wx_ref, coef_ref)

    for a in rows:
        qa = q_ref[0, a]
        qm = qs_ref[0] if a == 0 else q_ref[0, a - 1]
        qp = qn_ref[0] if a == lat_rows - 1 else q_ref[0, a + 1]
        result = (
            coef_ref[0, a] * qa
            + coef_ref[1, a] * pltpu.roll(qa, lon - 1, 1)
            + coef_ref[2, a] * pltpu.roll(qa, 1, 1)
            + coef_ref[3, a] * qp
            + coef_ref[4, a] * qm
            + coef_ref[5, a] * pltpu.roll(qa, levels - 1, 0)
            + coef_ref[6, a] * pltpu.roll(qa, 1, 0)
        )
        surface = result[0:1] + src_ref[0, a : a + 1, :]
        targets = [o_ref.at[0, a]]
        if edges and a == 0:
            targets.append(edges[0].at[0])
        if edges and a == lat_rows - 1:
            targets.append(edges[1].at[0])
        for target in targets:
            target[...] = result
            target[0:1, :] = surface


def advance(state, south, north, weather, emission, north_open, with_edges):
    tracers, lat_rows, levels, lon = state.shape
    row = pl.BlockSpec((1, lat_rows, levels, lon), lambda k: (k, 0, 0, 0))
    edge = pl.BlockSpec((1, levels, lon), lambda k: (k, 0, 0))
    out_specs = [row]
    out_shape = [jax.ShapeDtypeStruct(state.shape, state.dtype)]
    if with_edges:
        out_specs += [edge, edge]
        out_shape += [jax.ShapeDtypeStruct((tracers, levels, lon), state.dtype)] * 2
    grid_spec = pltpu.PrefetchScalarGridSpec(
        num_scalar_prefetch=0,
        grid=(tracers,),
        in_specs=[
            pl.BlockSpec(memory_space=pltpu.SMEM),
            row,
            edge,
            edge,
            pl.BlockSpec(weather.shape[:2] + (lon,), lambda k: (0, 0, 0)),
            pl.BlockSpec((1, lat_rows, lon), lambda k: (k, 0, 0)),
        ],
        out_specs=out_specs,
        scratch_shapes=[pltpu.VMEM((7, lat_rows, levels, lon), jnp.float32)],
    )
    return pl.pallas_call(
        step_kernel,
        grid_spec=grid_spec,
        out_shape=out_shape,
        compiler_params=pltpu.CompilerParams(dimension_semantics=("arbitrary",)),
    )(north_open, state, south, north, weather, emission)


def interior_step(state, weather, emission, north_open):
    tracers, lat_rows, levels, lon = state.shape
    row = pl.BlockSpec((1, lat_rows, levels, lon), lambda k: (k, 0, 0, 0))
    kernel = functools.partial(
        lambda n, q, w, e, o, c, rows: step_kernel(n, q, None, None, w, e, o, c, rows=rows),
        rows=range(1, lat_rows - 1),
    )
    grid_spec = pltpu.PrefetchScalarGridSpec(
        num_scalar_prefetch=0,
        grid=(tracers,),
        in_specs=[
            pl.BlockSpec(memory_space=pltpu.SMEM),
            row,
            pl.BlockSpec(weather.shape[:2] + (lon,), lambda k: (0, 0, 0)),
            pl.BlockSpec((1, lat_rows, lon), lambda k: (k, 0, 0)),
        ],
        out_specs=row,
        scratch_shapes=[pltpu.VMEM((7, lat_rows, levels, lon), jnp.float32)],
    )
    return pl.pallas_call(
        kernel,
        grid_spec=grid_spec,
        out_shape=jax.ShapeDtypeStruct(state.shape, state.dtype),
        compiler_params=pltpu.CompilerParams(dimension_semantics=("arbitrary",)),
    )(north_open, state, weather, emission)


def edge_kernel(north_ref, lo_ref, hi_ref, lo_in_ref, hi_in_ref, qs_ref, qn_ref, wx_ref, src_ref, *outs):
    split = len(outs) == 2
    if not split:
        o_hbm, stage, sems = outs
    tracers, lat_rows = src_ref.shape[0], src_ref.shape[1]
    levels, lon = lo_ref.shape[1], lo_ref.shape[2]
    level = lax.broadcasted_iota(jnp.int32, (levels, lon), 0)
    not_top = level < levels - 1
    not_bottom = level > 0
    last = lat_rows - 1
    for top in (0, 1):
        a = top * last
        u = wx_ref[a]
        uw = pltpu.roll(u, 1, 1)
        v = wx_ref[lat_rows + a] * north_ref[a]
        vm = wx_ref[3 * lat_rows] if top == 0 else wx_ref[lat_rows + a - 1]
        w = wx_ref[2 * lat_rows + a]
        w_up = jnp.where(not_top, w, 0.0)
        w_down = jnp.where(not_bottom, pltpu.roll(w, 1, 0), 0.0)
        c_self = (
            1.0
            - jnp.maximum(u, 0.0)
            + jnp.minimum(uw, 0.0)
            - jnp.maximum(v, 0.0)
            + jnp.minimum(vm, 0.0)
            - w_up
            - w_down
        )
        c_east = -jnp.minimum(u, 0.0)
        c_west = jnp.maximum(uw, 0.0)
        c_north = -jnp.minimum(v, 0.0)
        c_south = jnp.maximum(vm, 0.0)
        for k in range(tracers):
            qa = hi_ref[k] if top else lo_ref[k]
            inner = hi_in_ref[k] if top else lo_in_ref[k]
            qm = inner if top else qs_ref[k]
            qp = qn_ref[k] if top else inner
            result = (
                c_self * qa
                + c_east * pltpu.roll(qa, lon - 1, 1)
                + c_west * pltpu.roll(qa, 1, 1)
                + c_north * qp
                + c_south * qm
                + w_up * pltpu.roll(qa, levels - 1, 0)
                + w_down * pltpu.roll(qa, 1, 0)
            )
            surface = result[0:1] + src_ref[k, a : a + 1, :]
            target = outs[top].at[k] if split else stage.at[top, k, 0]
            target[...] = result
            target[0:1, :] = surface
    if not split:
        copies = [
            pltpu.make_async_copy(stage.at[top], o_hbm.at[:, pl.ds(top * last, 1)], sems.at[top])
            for top in (0, 1)
        ]
        for copy in copies:
            copy.start()
        for copy in copies:
            copy.wait()


def edge_step(rows, base, south, north, weather, emission, north_open):
    tracers, levels, lon = rows[0].shape
    lat_rows = emission.shape[1]
    vmem = pl.BlockSpec(memory_space=pltpu.VMEM)
    in_specs = [pl.BlockSpec(memory_space=pltpu.SMEM)] + [vmem] * 6
    in_specs += [pl.BlockSpec(weather.shape[:2] + (lon,), lambda i: (0, 0, 0)), vmem]
    args = [north_open, *rows, south, north, weather, emission]
    edge = pl.BlockSpec((tracers, levels, lon), lambda i: (0, 0, 0))
    scratch = []
    if base is None:
        out_specs = [edge, edge]
        out_shape = [jax.ShapeDtypeStruct((tracers, levels, lon), jnp.float32)] * 2
        aliases = {}
        kernel = edge_kernel
    else:
        in_specs.append(pl.BlockSpec(memory_space=pl.ANY))
        args.append(base)
        out_specs = pl.BlockSpec(memory_space=pl.ANY)
        out_shape = jax.ShapeDtypeStruct(base.shape, base.dtype)
        aliases = {len(args) - 1: 0}
        scratch = [pltpu.VMEM((2, tracers, 1, levels, lon), jnp.float32), pltpu.SemaphoreType.DMA((2,))]
        kernel = lambda *refs: edge_kernel(*refs[:9], *refs[10:])
    grid_spec = pltpu.PrefetchScalarGridSpec(
        num_scalar_prefetch=0, grid=(1,), in_specs=in_specs, out_specs=out_specs, scratch_shapes=scratch
    )
    return pl.pallas_call(
        kernel,
        grid_spec=grid_spec,
        out_shape=out_shape,
        input_output_aliases=aliases,
    )(*args)


def fused_kernel(north_ref, q_ref, lo_ref, hi_ref, wx_ref, src_ref, o_ref, lo_in_ref, hi_in_ref, coef_ref, mid_ref):
    lat_rows = q_ref.shape[1]
    levels, lon = q_ref.shape[2], q_ref.shape[3]

    @pl.when(pl.program_id(0) == 0)
    def _():
        fill_coefficients(north_ref, wx_ref, coef_ref)

    def stencil(a, qa, qm, qp):
        result = (
            coef_ref[0, a] * qa
            + coef_ref[1, a] * pltpu.roll(qa, lon - 1, 1)
            + coef_ref[2, a] * pltpu.roll(qa, 1, 1)
            + coef_ref[3, a] * qp
            + coef_ref[4, a] * qm
            + coef_ref[5, a] * pltpu.roll(qa, levels - 1, 0)
            + coef_ref[6, a] * pltpu.roll(qa, 1, 0)
        )
        return result, result[0:1] + src_ref[0, a : a + 1, :]

    mid_ref[0] = lo_ref[0]
    mid_ref[lat_rows - 1] = hi_ref[0]
    for a in range(1, lat_rows - 1):
        result, surface = stencil(a, q_ref[0, a], q_ref[0, a - 1], q_ref[0, a + 1])
        mid_ref[a] = result
        mid_ref[a, 0:1, :] = surface
        if a == 1:
            lo_in_ref[0] = mid_ref[a]
        if a == lat_rows - 2:
            hi_in_ref[0] = mid_ref[a]
    for a in range(1, lat_rows - 1):
        result, surface = stencil(a, mid_ref[a], mid_ref[a - 1], mid_ref[a + 1])
        o_ref[0, a] = result
        o_ref[0, a, 0:1, :] = surface


def fused_steps(state, lo, hi, weather, emission, north_open):
    tracers, lat_rows, levels, lon = state.shape
    row = pl.BlockSpec((1, lat_rows, levels, lon), lambda k: (k, 0, 0, 0))
    edge = pl.BlockSpec((1, levels, lon), lambda k: (k, 0, 0))
    grid_spec = pltpu.PrefetchScalarGridSpec(
        num_scalar_prefetch=0,
        grid=(tracers,),
        in_specs=[
            pl.BlockSpec(memory_space=pltpu.SMEM),
            row,
            edge,
            edge,
            pl.BlockSpec(weather.shape[:2] + (lon,), lambda k: (0, 0, 0)),
            pl.BlockSpec((1, lat_rows, lon), lambda k: (k, 0, 0)),
        ],
        out_specs=[row, edge, edge],
        scratch_shapes=[
            pltpu.VMEM((7, lat_rows, levels, lon), jnp.float32),
            pltpu.VMEM((lat_rows, levels, lon), jnp.float32),
        ],
    )
    return pl.pallas_call(
        fused_kernel,
        grid_spec=grid_spec,
        out_shape=[jax.ShapeDtypeStruct(state.shape, state.dtype)]
        + [jax.ShapeDtypeStruct((tracers, levels, lon), state.dtype)] * 2,
        compiler_params=pltpu.CompilerParams(dimension_semantics=("arbitrary",)),
    )(north_open, state, lo, hi, weather, emission)


def on_device(
    tracer_state,
    control,
    prior_tiles,
    tile_index,
    region_map,
    region_sigma,
    zonal_courant,
    meridional_courant,
    vertical_diffusion,
):
    band_count = lax.axis_size("band")
    band_index = lax.axis_index("band")
    tiles_count = prior_tiles.shape[0]
    lat_rows = control.shape[1]

    latitude = band_index * lat_rows + jnp.arange(lat_rows, dtype=jnp.int32)
    north_open = (latitude < band_count * lat_rows - 1).astype(jnp.float32)
    choose = (
        tile_index[:, :, None] == lax.broadcasted_iota(jnp.int32, (1, 1, tiles_count), 2)
    ).astype(jnp.float32)
    own_row = lax.dynamic_slice_in_dim(choose, band_index, 1, 0)[0]
    row_tiles = jnp.einsum("bt,tmn->bmn", own_row, prior_tiles, precision=exact_dot)
    own_tile = lax.dynamic_index_in_dim(row_tiles, band_index, 0, keepdims=False)
    prior_field = jnp.einsum("jm,kmn->kjn", own_tile, control, precision=exact_dot)
    south_v = passed_along(meridional_courant[-1:], "band", 1)
    parts, (north_open, row_tiles, prior_field) = lax.optimization_barrier(
        ((zonal_courant, meridional_courant, vertical_diffusion, south_v), (north_open, row_tiles, prior_field))
    )
    pack = packed(list(parts))
    weather = relay_gather(pack, "tracer")
    held_state, held_control, _ = lax.optimization_barrier((tracer_state, control, pack))
    q_south = passed_along(held_state[:, -1], "band", 1)
    q_north = passed_along(held_state[:, 0], "band", -1)
    for s in range(1, band_count):
        pairs = [(i, (i + s) % band_count) for i in range(band_count)]
        part = lax.ppermute(held_control, "band", pairs)
        source_band = (band_index - s) % band_count
        tile = lax.dynamic_index_in_dim(row_tiles, source_band, 0, keepdims=False)
        prior_field = prior_field + jnp.einsum("jm,kmn->kjn", tile, part, precision=exact_dot)
    regions = region_sigma.shape[1]
    onehot = (region_map[:, :, None] == lax.broadcasted_iota(jnp.int32, (1, 1, regions), 2)).astype(
        jnp.float32
    )
    cell_sigma = jnp.einsum("kr,jnr->kjn", region_sigma, onehot, precision=exact_dot)
    emission = cell_sigma * prior_field

    rim = (tracer_state[:, 0], tracer_state[:, lat_rows - 1], tracer_state[:, 1], tracer_state[:, lat_rows - 2])
    bottom_row, top_row = edge_step(rim, None, q_south, q_north, weather, emission, north_open)
    s1_south = passed_along(top_row, "band", 1)
    s1_north = passed_along(bottom_row, "band", -1)
    inside, bottom_in, top_in = fused_steps(tracer_state, bottom_row, top_row, weather, emission, north_open)
    rim = (bottom_row, top_row, bottom_in, top_in)
    tracer_field = edge_step(rim, inside, s1_south, s1_north, weather, emission, north_open)
    return (tracer_field, emission)


def solution(mesh):
    in_specs = (
        P(("inv", "tracer"), "band", None, None),
        P(("inv", "tracer"), "band", None),
        P(),
        P(),
        P("band", None),
        P("tracer", None),
        P(("inv", "band"), None, "tracer"),
        P(("inv", "band"), None, "tracer"),
        P(("inv", "band"), None, "tracer"),
    )
    out_specs = (P(("inv", "tracer"), "band", None, None), P(("inv", "tracer"), "band", None))
    return jax.shard_map(
        on_device, mesh=mesh, in_specs=in_specs, out_specs=out_specs, check_vma=False
    )
```

```python
import functools

import jax
import jax.numpy as jnp
from jax import lax
from jax.experimental import pallas as pl
from jax.experimental.pallas import tpu as pltpu
from jax.sharding import PartitionSpec as P

exact_dot = lax.Precision.HIGHEST


def passed_along(value, axis, by):
    count = lax.axis_size(axis)
    pairs = [(i, i + by) for i in range(count) if 0 <= i + by < count]
    return lax.ppermute(value, axis, pairs)


def pack_kernel(*refs):
    parts, out_ref = refs[:-1], refs[-1]
    row = 0
    for part in parts:
        rows = part.shape[0]
        out_ref[row : row + rows] = part[...]
        row += rows


def packed(parts):
    rows = sum(part.shape[0] for part in parts)
    return pl.pallas_call(
        pack_kernel,
        out_shape=jax.ShapeDtypeStruct((rows,) + parts[0].shape[1:], parts[0].dtype),
    )(*parts)


def relay_gather(x, axis):
    count = lax.axis_size(axis)
    me = lax.axis_index(axis)
    rows, levels, width = x.shape
    buf = jnp.zeros((rows, levels, (count + 1) * width), x.dtype)
    buf = lax.dynamic_update_slice(buf, x, (0, 0, me * width))
    right = left = x
    for r in range(1, count):
        right = lax.ppermute(right, axis, [(i, i + 1) for i in range(r - 1, count - 1)])
        left = lax.ppermute(left, axis, [(j, j - 1) for j in range(1, count - r + 1)])
        slot = jnp.where(me - r >= 0, me - r, count)
        buf = lax.dynamic_update_slice(buf, right, (0, 0, slot * width))
        slot = jnp.where(me + r < count, me + r, count)
        buf = lax.dynamic_update_slice(buf, left, (0, 0, slot * width))
    return buf


def fill_coefficients(north_ref, wx_ref, coef_ref):
    lat_rows = coef_ref.shape[1]
    levels, lon = coef_ref.shape[2], coef_ref.shape[3]
    level = lax.broadcasted_iota(jnp.int32, (levels, lon), 0)
    not_top = level < levels - 1
    not_bottom = level > 0
    for a in range(lat_rows):
        u = wx_ref[a]
        uw = pltpu.roll(u, 1, 1)
        v = wx_ref[lat_rows + a] * north_ref[a]
        vm = wx_ref[3 * lat_rows] if a == 0 else wx_ref[lat_rows + a - 1]
        w = wx_ref[2 * lat_rows + a]
        w_up = jnp.where(not_top, w, 0.0)
        w_down = jnp.where(not_bottom, pltpu.roll(w, 1, 0), 0.0)
        coef_ref[0, a] = (
            1.0
            - jnp.maximum(u, 0.0)
            + jnp.minimum(uw, 0.0)
            - jnp.maximum(v, 0.0)
            + jnp.minimum(vm, 0.0)
            - w_up
            - w_down
        )
        coef_ref[1, a] = -jnp.minimum(u, 0.0)
        coef_ref[2, a] = jnp.maximum(uw, 0.0)
        coef_ref[3, a] = -jnp.minimum(v, 0.0)
        coef_ref[4, a] = jnp.maximum(vm, 0.0)
        coef_ref[5, a] = w_up
        coef_ref[6, a] = w_down


def step_kernel(north_ref, q_ref, qs_ref, qn_ref, wx_ref, src_ref, *rest, rows=None):
    o_ref = rest[0]
    edges = rest[1:-1]
    coef_ref = rest[-1]
    lat_rows = q_ref.shape[1]
    rows = range(lat_rows) if rows is None else rows
    levels, lon = q_ref.shape[2], q_ref.shape[3]
    level = lax.broadcasted_iota(jnp.int32, (levels, lon), 0)
    not_top = level < levels - 1
    not_bottom = level > 0

    @pl.when(pl.program_id(0) == 0)
    def _():
        fill_coefficients(north_ref, wx_ref, coef_ref)

    for a in rows:
        qa = q_ref[0, a]
        qm = qs_ref[0] if a == 0 else q_ref[0, a - 1]
        qp = qn_ref[0] if a == lat_rows - 1 else q_ref[0, a + 1]
        result = (
            coef_ref[0, a] * qa
            + coef_ref[1, a] * pltpu.roll(qa, lon - 1, 1)
            + coef_ref[2, a] * pltpu.roll(qa, 1, 1)
            + coef_ref[3, a] * qp
            + coef_ref[4, a] * qm
            + coef_ref[5, a] * pltpu.roll(qa, levels - 1, 0)
            + coef_ref[6, a] * pltpu.roll(qa, 1, 0)
        )
        surface = result[0:1] + src_ref[0, a : a + 1, :]
        targets = [o_ref.at[0, a]]
        if edges and a == 0:
            targets.append(edges[0].at[0])
        if edges and a == lat_rows - 1:
            targets.append(edges[1].at[0])
        for target in targets:
            target[...] = result
            target[0:1, :] = surface


def advance(state, south, north, weather, emission, north_open, with_edges):
    tracers, lat_rows, levels, lon = state.shape
    row = pl.BlockSpec((1, lat_rows, levels, lon), lambda k: (k, 0, 0, 0))
    edge = pl.BlockSpec((1, levels, lon), lambda k: (k, 0, 0))
    out_specs = [row]
    out_shape = [jax.ShapeDtypeStruct(state.shape, state.dtype)]
    if with_edges:
        out_specs += [edge, edge]
        out_shape += [jax.ShapeDtypeStruct((tracers, levels, lon), state.dtype)] * 2
    grid_spec = pltpu.PrefetchScalarGridSpec(
        num_scalar_prefetch=0,
        grid=(tracers,),
        in_specs=[
            pl.BlockSpec(memory_space=pltpu.SMEM),
            row,
            edge,
            edge,
            pl.BlockSpec(weather.shape[:2] + (lon,), lambda k: (0, 0, 0)),
            pl.BlockSpec((1, lat_rows, lon), lambda k: (k, 0, 0)),
        ],
        out_specs=out_specs,
        scratch_shapes=[pltpu.VMEM((7, lat_rows, levels, lon), jnp.float32)],
    )
    return pl.pallas_call(
        step_kernel,
        grid_spec=grid_spec,
        out_shape=out_shape,
        compiler_params=pltpu.CompilerParams(dimension_semantics=("arbitrary",)),
    )(north_open, state, south, north, weather, emission)


def interior_step(state, weather, emission, north_open):
    tracers, lat_rows, levels, lon = state.shape
    row = pl.BlockSpec((1, lat_rows, levels, lon), lambda k: (k, 0, 0, 0))
    kernel = functools.partial(
        lambda n, q, w, e, o, c, rows: step_kernel(n, q, None, None, w, e, o, c, rows=rows),
        rows=range(1, lat_rows - 1),
    )
    grid_spec = pltpu.PrefetchScalarGridSpec(
        num_scalar_prefetch=0,
        grid=(tracers,),
        in_specs=[
            pl.BlockSpec(memory_space=pltpu.SMEM),
            row,
            pl.BlockSpec(weather.shape[:2] + (lon,), lambda k: (0, 0, 0)),
            pl.BlockSpec((1, lat_rows, lon), lambda k: (k, 0, 0)),
        ],
        out_specs=row,
        scratch_shapes=[pltpu.VMEM((7, lat_rows, levels, lon), jnp.float32)],
    )
    return pl.pallas_call(
        kernel,
        grid_spec=grid_spec,
        out_shape=jax.ShapeDtypeStruct(state.shape, state.dtype),
        compiler_params=pltpu.CompilerParams(dimension_semantics=("arbitrary",)),
    )(north_open, state, weather, emission)


def edge_kernel(north_ref, lo_ref, hi_ref, lo_in_ref, hi_in_ref, qs_ref, qn_ref, *rest):
    met_refs, src_ref, outs = rest[:8], rest[8], rest[9:]
    split = len(outs) == 2
    if not split:
        o_hbm, stage, sems = outs
    tracers, lat_rows = src_ref.shape[0], src_ref.shape[1]
    levels, lon = lo_ref.shape[1], lo_ref.shape[2]
    level = lax.broadcasted_iota(jnp.int32, (levels, lon), 0)
    not_top = level < levels - 1
    not_bottom = level > 0
    last = lat_rows - 1
    for top in (0, 1):
        a = top * last
        u_ref, v_ref, vm_ref, w_ref = met_refs[4 * top : 4 * top + 4]
        u = u_ref[0]
        uw = pltpu.roll(u, 1, 1)
        v = v_ref[0] * north_ref[a]
        vm = vm_ref[0]
        w = w_ref[0]
        w_up = jnp.where(not_top, w, 0.0)
        w_down = jnp.where(not_bottom, pltpu.roll(w, 1, 0), 0.0)
        c_self = (
            1.0
            - jnp.maximum(u, 0.0)
            + jnp.minimum(uw, 0.0)
            - jnp.maximum(v, 0.0)
            + jnp.minimum(vm, 0.0)
            - w_up
            - w_down
        )
        c_east = -jnp.minimum(u, 0.0)
        c_west = jnp.maximum(uw, 0.0)
        c_north = -jnp.minimum(v, 0.0)
        c_south = jnp.maximum(vm, 0.0)
        for k in range(tracers):
            qa = hi_ref[k] if top else lo_ref[k]
            inner = hi_in_ref[k] if top else lo_in_ref[k]
            qm = inner if top else qs_ref[k]
            qp = qn_ref[k] if top else inner
            result = (
                c_self * qa
                + c_east * pltpu.roll(qa, lon - 1, 1)
                + c_west * pltpu.roll(qa, 1, 1)
                + c_north * qp
                + c_south * qm
                + w_up * pltpu.roll(qa, levels - 1, 0)
                + w_down * pltpu.roll(qa, 1, 0)
            )
            surface = result[0:1] + src_ref[k, a : a + 1, :]
            target = outs[top].at[k] if split else stage.at[top, k, 0]
            target[...] = result
            target[0:1, :] = surface
    if not split:
        copies = [
            pltpu.make_async_copy(stage.at[top], o_hbm.at[:, pl.ds(top * last, 1)], sems.at[top])
            for top in (0, 1)
        ]
        for copy in copies:
            copy.start()
        for copy in copies:
            copy.wait()


def edge_step(rows, base, south, north, weather, emission, north_open):
    tracers, levels, lon = rows[0].shape
    lat_rows = emission.shape[1]
    vmem = pl.BlockSpec(memory_space=pltpu.VMEM)
    in_specs = [pl.BlockSpec(memory_space=pltpu.SMEM)] + [vmem] * 6
    last = lat_rows - 1
    met_rows = []
    for a, below in ((0, 3 * lat_rows), (last, lat_rows + last - 1)):
        met_rows += [a, lat_rows + a, below, 2 * lat_rows + a]
    in_specs += [pl.BlockSpec((1, levels, lon), lambda i, r=r: (r, 0, 0)) for r in met_rows] + [vmem]
    args = [north_open, *rows, south, north] + [weather] * len(met_rows) + [emission]
    edge = pl.BlockSpec((tracers, levels, lon), lambda i: (0, 0, 0))
    scratch = []
    if base is None:
        out_specs = [edge, edge]
        out_shape = [jax.ShapeDtypeStruct((tracers, levels, lon), jnp.float32)] * 2
        aliases = {}
        kernel = edge_kernel
    else:
        in_specs.append(pl.BlockSpec(memory_space=pl.ANY))
        args.append(base)
        out_specs = pl.BlockSpec(memory_space=pl.ANY)
        out_shape = jax.ShapeDtypeStruct(base.shape, base.dtype)
        aliases = {len(args) - 1: 0}
        scratch = [pltpu.VMEM((2, tracers, 1, levels, lon), jnp.float32), pltpu.SemaphoreType.DMA((2,))]
        kernel = lambda *refs: edge_kernel(*refs[:16], *refs[17:])
    grid_spec = pltpu.PrefetchScalarGridSpec(
        num_scalar_prefetch=0, grid=(1,), in_specs=in_specs, out_specs=out_specs, scratch_shapes=scratch
    )
    return pl.pallas_call(
        kernel,
        grid_spec=grid_spec,
        out_shape=out_shape,
        input_output_aliases=aliases,
    )(*args)


def fused_kernel(north_ref, q_ref, lo_ref, hi_ref, wx_ref, src_ref, o_ref, lo_in_ref, hi_in_ref, coef_ref, mid_ref):
    lat_rows = q_ref.shape[1]
    levels, lon = q_ref.shape[2], q_ref.shape[3]

    @pl.when(pl.program_id(0) == 0)
    def _():
        fill_coefficients(north_ref, wx_ref, coef_ref)

    def stencil(a, qa, qm, qp):
        result = (
            coef_ref[0, a] * qa
            + coef_ref[1, a] * pltpu.roll(qa, lon - 1, 1)
            + coef_ref[2, a] * pltpu.roll(qa, 1, 1)
            + coef_ref[3, a] * qp
            + coef_ref[4, a] * qm
            + coef_ref[5, a] * pltpu.roll(qa, levels - 1, 0)
            + coef_ref[6, a] * pltpu.roll(qa, 1, 0)
        )
        return result, result[0:1] + src_ref[0, a : a + 1, :]

    mid_ref[0] = lo_ref[0]
    mid_ref[lat_rows - 1] = hi_ref[0]
    for a in range(1, lat_rows - 1):
        result, surface = stencil(a, q_ref[0, a], q_ref[0, a - 1], q_ref[0, a + 1])
        mid_ref[a] = result
        mid_ref[a, 0:1, :] = surface
        if a == 1:
            lo_in_ref[0] = mid_ref[a]
        if a == lat_rows - 2:
            hi_in_ref[0] = mid_ref[a]
    for a in range(1, lat_rows - 1):
        result, surface = stencil(a, mid_ref[a], mid_ref[a - 1], mid_ref[a + 1])
        o_ref[0, a] = result
        o_ref[0, a, 0:1, :] = surface


def fused_steps(state, lo, hi, weather, emission, north_open):
    tracers, lat_rows, levels, lon = state.shape
    row = pl.BlockSpec((1, lat_rows, levels, lon), lambda k: (k, 0, 0, 0))
    edge = pl.BlockSpec((1, levels, lon), lambda k: (k, 0, 0))
    grid_spec = pltpu.PrefetchScalarGridSpec(
        num_scalar_prefetch=0,
        grid=(tracers,),
        in_specs=[
            pl.BlockSpec(memory_space=pltpu.SMEM),
            row,
            edge,
            edge,
            pl.BlockSpec(weather.shape[:2] + (lon,), lambda k: (0, 0, 0)),
            pl.BlockSpec((1, lat_rows, lon), lambda k: (k, 0, 0)),
        ],
        out_specs=[row, edge, edge],
        scratch_shapes=[
            pltpu.VMEM((7, lat_rows, levels, lon), jnp.float32),
            pltpu.VMEM((lat_rows, levels, lon), jnp.float32),
        ],
    )
    return pl.pallas_call(
        fused_kernel,
        grid_spec=grid_spec,
        out_shape=[jax.ShapeDtypeStruct(state.shape, state.dtype)]
        + [jax.ShapeDtypeStruct((tracers, levels, lon), state.dtype)] * 2,
        compiler_params=pltpu.CompilerParams(dimension_semantics=("arbitrary",)),
    )(north_open, state, lo, hi, weather, emission)


def on_device(
    tracer_state,
    control,
    prior_tiles,
    tile_index,
    region_map,
    region_sigma,
    zonal_courant,
    meridional_courant,
    vertical_diffusion,
):
    band_count = lax.axis_size("band")
    band_index = lax.axis_index("band")
    tiles_count = prior_tiles.shape[0]
    lat_rows = control.shape[1]

    latitude = band_index * lat_rows + jnp.arange(lat_rows, dtype=jnp.int32)
    north_open = (latitude < band_count * lat_rows - 1).astype(jnp.float32)
    choose = (
        tile_index[:, :, None] == lax.broadcasted_iota(jnp.int32, (1, 1, tiles_count), 2)
    ).astype(jnp.float32)
    own_row = lax.dynamic_slice_in_dim(choose, band_index, 1, 0)[0]
    row_tiles = jnp.einsum("bt,tmn->bmn", own_row, prior_tiles, precision=exact_dot)
    own_tile = lax.dynamic_index_in_dim(row_tiles, band_index, 0, keepdims=False)
    prior_field = jnp.einsum("jm,kmn->kjn", own_tile, control, precision=exact_dot)
    south_v = passed_along(meridional_courant[-1:], "band", 1)
    parts, (north_open, row_tiles, prior_field) = lax.optimization_barrier(
        ((zonal_courant, meridional_courant, vertical_diffusion, south_v), (north_open, row_tiles, prior_field))
    )
    pack = packed(list(parts))
    weather = relay_gather(pack, "tracer")
    held_state, held_control, _ = lax.optimization_barrier((tracer_state, control, pack))
    q_south = passed_along(held_state[:, -1], "band", 1)
    q_north = passed_along(held_state[:, 0], "band", -1)
    for s in range(1, band_count):
        pairs = [(i, (i + s) % band_count) for i in range(band_count)]
        part = lax.ppermute(held_control, "band", pairs)
        source_band = (band_index - s) % band_count
        tile = lax.dynamic_index_in_dim(row_tiles, source_band, 0, keepdims=False)
        prior_field = prior_field + jnp.einsum("jm,kmn->kjn", tile, part, precision=exact_dot)
    regions = region_sigma.shape[1]
    onehot = (region_map[:, :, None] == lax.broadcasted_iota(jnp.int32, (1, 1, regions), 2)).astype(
        jnp.float32
    )
    cell_sigma = jnp.einsum("kr,jnr->kjn", region_sigma, onehot, precision=exact_dot)
    emission = cell_sigma * prior_field

    rim = (tracer_state[:, 0], tracer_state[:, lat_rows - 1], tracer_state[:, 1], tracer_state[:, lat_rows - 2])
    bottom_row, top_row = edge_step(rim, None, q_south, q_north, weather, emission, north_open)
    s1_south = passed_along(top_row, "band", 1)
    s1_north = passed_along(bottom_row, "band", -1)
    inside, bottom_in, top_in = fused_steps(tracer_state, bottom_row, top_row, weather, emission, north_open)
    rim = (bottom_row, top_row, bottom_in, top_in)
    tracer_field = edge_step(rim, inside, s1_south, s1_north, weather, emission, north_open)
    return (tracer_field, emission)


def solution(mesh):
    in_specs = (
        P(("inv", "tracer"), "band", None, None),
        P(("inv", "tracer"), "band", None),
        P(),
        P(),
        P("band", None),
        P("tracer", None),
        P(("inv", "band"), None, "tracer"),
        P(("inv", "band"), None, "tracer"),
        P(("inv", "band"), None, "tracer"),
    )
    out_specs = (P(("inv", "tracer"), "band", None, None), P(("inv", "tracer"), "band", None))
    return jax.shard_map(
        on_device, mesh=mesh, in_specs=in_specs, out_specs=out_specs, check_vma=False
    )
```

```python
import functools

import jax
import jax.numpy as jnp
from jax import lax
from jax.experimental import pallas as pl
from jax.experimental.pallas import tpu as pltpu
from jax.sharding import PartitionSpec as P

exact_dot = lax.Precision.HIGHEST


def passed_along(value, axis, by):
    count = lax.axis_size(axis)
    pairs = [(i, i + by) for i in range(count) if 0 <= i + by < count]
    return lax.ppermute(value, axis, pairs)


def pack_kernel(*refs):
    parts, out_ref = refs[:-1], refs[-1]
    row = 0
    for part in parts:
        rows = part.shape[0]
        out_ref[row : row + rows] = part[...]
        row += rows


def packed(parts):
    rows = sum(part.shape[0] for part in parts)
    return pl.pallas_call(
        pack_kernel,
        out_shape=jax.ShapeDtypeStruct((rows,) + parts[0].shape[1:], parts[0].dtype),
    )(*parts)


def relay_gather(x, axis):
    count = lax.axis_size(axis)
    me = lax.axis_index(axis)
    rows, levels, width = x.shape
    buf = jnp.zeros((rows, levels, (count + 1) * width), x.dtype)
    buf = lax.dynamic_update_slice(buf, x, (0, 0, me * width))
    right = left = x
    for r in range(1, count):
        right = lax.ppermute(right, axis, [(i, i + 1) for i in range(r - 1, count - 1)])
        left = lax.ppermute(left, axis, [(j, j - 1) for j in range(1, count - r + 1)])
        slot = jnp.where(me - r >= 0, me - r, count)
        buf = lax.dynamic_update_slice(buf, right, (0, 0, slot * width))
        slot = jnp.where(me + r < count, me + r, count)
        buf = lax.dynamic_update_slice(buf, left, (0, 0, slot * width))
    return buf


def fill_coefficients(north_ref, wx_ref, coef_ref, ready=None):
    lat_rows = coef_ref.shape[1]
    levels, lon = coef_ref.shape[2], coef_ref.shape[3]
    level = lax.broadcasted_iota(jnp.int32, (levels, lon), 0)
    not_top = level < levels - 1
    not_bottom = level > 0
    for a in range(lat_rows):
        if ready is not None:
            ready(a)
        u = wx_ref[a]
        uw = pltpu.roll(u, 1, 1)
        v = wx_ref[lat_rows + a] * north_ref[a]
        vm = wx_ref[3 * lat_rows] if a == 0 else wx_ref[lat_rows + a - 1]
        w = wx_ref[2 * lat_rows + a]
        w_up = jnp.where(not_top, w, 0.0)
        w_down = jnp.where(not_bottom, pltpu.roll(w, 1, 0), 0.0)
        coef_ref[0, a] = (
            1.0
            - jnp.maximum(u, 0.0)
            + jnp.minimum(uw, 0.0)
            - jnp.maximum(v, 0.0)
            + jnp.minimum(vm, 0.0)
            - w_up
            - w_down
        )
        coef_ref[1, a] = -jnp.minimum(u, 0.0)
        coef_ref[2, a] = jnp.maximum(uw, 0.0)
        coef_ref[3, a] = -jnp.minimum(v, 0.0)
        coef_ref[4, a] = jnp.maximum(vm, 0.0)
        coef_ref[5, a] = w_up
        coef_ref[6, a] = w_down


def step_kernel(north_ref, q_ref, qs_ref, qn_ref, wx_ref, src_ref, *rest, rows=None):
    o_ref = rest[0]
    edges = rest[1:-1]
    coef_ref = rest[-1]
    lat_rows = q_ref.shape[1]
    rows = range(lat_rows) if rows is None else rows
    levels, lon = q_ref.shape[2], q_ref.shape[3]
    level = lax.broadcasted_iota(jnp.int32, (levels, lon), 0)
    not_top = level < levels - 1
    not_bottom = level > 0

    @pl.when(pl.program_id(0) == 0)
    def _():
        fill_coefficients(north_ref, wx_ref, coef_ref)

    for a in rows:
        qa = q_ref[0, a]
        qm = qs_ref[0] if a == 0 else q_ref[0, a - 1]
        qp = qn_ref[0] if a == lat_rows - 1 else q_ref[0, a + 1]
        result = (
            coef_ref[0, a] * qa
            + coef_ref[1, a] * pltpu.roll(qa, lon - 1, 1)
            + coef_ref[2, a] * pltpu.roll(qa, 1, 1)
            + coef_ref[3, a] * qp
            + coef_ref[4, a] * qm
            + coef_ref[5, a] * pltpu.roll(qa, levels - 1, 0)
            + coef_ref[6, a] * pltpu.roll(qa, 1, 0)
        )
        surface = result[0:1] + src_ref[0, a : a + 1, :]
        targets = [o_ref.at[0, a]]
        if edges and a == 0:
            targets.append(edges[0].at[0])
        if edges and a == lat_rows - 1:
            targets.append(edges[1].at[0])
        for target in targets:
            target[...] = result
            target[0:1, :] = surface


def advance(state, south, north, weather, emission, north_open, with_edges):
    tracers, lat_rows, levels, lon = state.shape
    row = pl.BlockSpec((1, lat_rows, levels, lon), lambda k: (k, 0, 0, 0))
    edge = pl.BlockSpec((1, levels, lon), lambda k: (k, 0, 0))
    out_specs = [row]
    out_shape = [jax.ShapeDtypeStruct(state.shape, state.dtype)]
    if with_edges:
        out_specs += [edge, edge]
        out_shape += [jax.ShapeDtypeStruct((tracers, levels, lon), state.dtype)] * 2
    grid_spec = pltpu.PrefetchScalarGridSpec(
        num_scalar_prefetch=0,
        grid=(tracers,),
        in_specs=[
            pl.BlockSpec(memory_space=pltpu.SMEM),
            row,
            edge,
            edge,
            pl.BlockSpec(weather.shape[:2] + (lon,), lambda k: (0, 0, 0)),
            pl.BlockSpec((1, lat_rows, lon), lambda k: (k, 0, 0)),
        ],
        out_specs=out_specs,
        scratch_shapes=[pltpu.VMEM((7, lat_rows, levels, lon), jnp.float32)],
    )
    return pl.pallas_call(
        step_kernel,
        grid_spec=grid_spec,
        out_shape=out_shape,
        compiler_params=pltpu.CompilerParams(dimension_semantics=("arbitrary",)),
    )(north_open, state, south, north, weather, emission)


def interior_step(state, weather, emission, north_open):
    tracers, lat_rows, levels, lon = state.shape
    row = pl.BlockSpec((1, lat_rows, levels, lon), lambda k: (k, 0, 0, 0))
    kernel = functools.partial(
        lambda n, q, w, e, o, c, rows: step_kernel(n, q, None, None, w, e, o, c, rows=rows),
        rows=range(1, lat_rows - 1),
    )
    grid_spec = pltpu.PrefetchScalarGridSpec(
        num_scalar_prefetch=0,
        grid=(tracers,),
        in_specs=[
            pl.BlockSpec(memory_space=pltpu.SMEM),
            row,
            pl.BlockSpec(weather.shape[:2] + (lon,), lambda k: (0, 0, 0)),
            pl.BlockSpec((1, lat_rows, lon), lambda k: (k, 0, 0)),
        ],
        out_specs=row,
        scratch_shapes=[pltpu.VMEM((7, lat_rows, levels, lon), jnp.float32)],
    )
    return pl.pallas_call(
        kernel,
        grid_spec=grid_spec,
        out_shape=jax.ShapeDtypeStruct(state.shape, state.dtype),
        compiler_params=pltpu.CompilerParams(dimension_semantics=("arbitrary",)),
    )(north_open, state, weather, emission)


def edge_kernel(north_ref, lo_ref, hi_ref, lo_in_ref, hi_in_ref, qs_ref, qn_ref, *rest):
    met_refs, src_ref, outs = rest[:8], rest[8], rest[9:]
    split = len(outs) == 2
    if not split:
        o_hbm, stage, sems = outs
    tracers, lat_rows = src_ref.shape[0], src_ref.shape[1]
    levels, lon = lo_ref.shape[1], lo_ref.shape[2]
    level = lax.broadcasted_iota(jnp.int32, (levels, lon), 0)
    not_top = level < levels - 1
    not_bottom = level > 0
    last = lat_rows - 1
    for top in (0, 1):
        a = top * last
        u_ref, v_ref, vm_ref, w_ref = met_refs[4 * top : 4 * top + 4]
        u = u_ref[0]
        uw = pltpu.roll(u, 1, 1)
        v = v_ref[0] * north_ref[a]
        vm = vm_ref[0]
        w = w_ref[0]
        w_up = jnp.where(not_top, w, 0.0)
        w_down = jnp.where(not_bottom, pltpu.roll(w, 1, 0), 0.0)
        c_self = (
            1.0
            - jnp.maximum(u, 0.0)
            + jnp.minimum(uw, 0.0)
            - jnp.maximum(v, 0.0)
            + jnp.minimum(vm, 0.0)
            - w_up
            - w_down
        )
        c_east = -jnp.minimum(u, 0.0)
        c_west = jnp.maximum(uw, 0.0)
        c_north = -jnp.minimum(v, 0.0)
        c_south = jnp.maximum(vm, 0.0)
        for k in range(tracers):
            qa = hi_ref[k] if top else lo_ref[k]
            inner = hi_in_ref[k] if top else lo_in_ref[k]
            qm = inner if top else qs_ref[k]
            qp = qn_ref[k] if top else inner
            result = (
                c_self * qa
                + c_east * pltpu.roll(qa, lon - 1, 1)
                + c_west * pltpu.roll(qa, 1, 1)
                + c_north * qp
                + c_south * qm
                + w_up * pltpu.roll(qa, levels - 1, 0)
                + w_down * pltpu.roll(qa, 1, 0)
            )
            surface = result[0:1] + src_ref[k, a : a + 1, :]
            target = outs[top].at[k] if split else stage.at[top, k, 0]
            target[...] = result
            target[0:1, :] = surface
    if not split:
        copies = [
            pltpu.make_async_copy(stage.at[top], o_hbm.at[:, pl.ds(top * last, 1)], sems.at[top])
            for top in (0, 1)
        ]
        for copy in copies:
            copy.start()
        for copy in copies:
            copy.wait()


def edge_step(rows, base, south, north, weather, emission, north_open):
    tracers, levels, lon = rows[0].shape
    lat_rows = emission.shape[1]
    vmem = pl.BlockSpec(memory_space=pltpu.VMEM)
    in_specs = [pl.BlockSpec(memory_space=pltpu.SMEM)] + [vmem] * 6
    last = lat_rows - 1
    met_rows = []
    for a, below in ((0, 3 * lat_rows), (last, lat_rows + last - 1)):
        met_rows += [a, lat_rows + a, below, 2 * lat_rows + a]
    in_specs += [pl.BlockSpec((1, levels, lon), lambda i, r=r: (r, 0, 0)) for r in met_rows] + [vmem]
    args = [north_open, *rows, south, north] + [weather] * len(met_rows) + [emission]
    edge = pl.BlockSpec((tracers, levels, lon), lambda i: (0, 0, 0))
    scratch = []
    if base is None:
        out_specs = [edge, edge]
        out_shape = [jax.ShapeDtypeStruct((tracers, levels, lon), jnp.float32)] * 2
        aliases = {}
        kernel = edge_kernel
    else:
        in_specs.append(pl.BlockSpec(memory_space=pl.ANY))
        args.append(base)
        out_specs = pl.BlockSpec(memory_space=pl.ANY)
        out_shape = jax.ShapeDtypeStruct(base.shape, base.dtype)
        aliases = {len(args) - 1: 0}
        scratch = [pltpu.VMEM((2, tracers, 1, levels, lon), jnp.float32), pltpu.SemaphoreType.DMA((2,))]
        kernel = lambda *refs: edge_kernel(*refs[:16], *refs[17:])
    grid_spec = pltpu.PrefetchScalarGridSpec(
        num_scalar_prefetch=0, grid=(1,), in_specs=in_specs, out_specs=out_specs, scratch_shapes=scratch
    )
    return pl.pallas_call(
        kernel,
        grid_spec=grid_spec,
        out_shape=out_shape,
        input_output_aliases=aliases,
    )(*args)


def fused_kernel(north_ref, q_ref, lo_ref, hi_ref, wx_hbm, src_ref, o_ref, lo_in_ref, hi_in_ref, coef_ref, mid_ref, wx_ref, sems):
    lat_rows = q_ref.shape[1]
    levels, lon = q_ref.shape[2], q_ref.shape[3]

    @pl.when(pl.program_id(0) == 0)
    def _():
        copies = [
            pltpu.make_async_copy(wx_hbm.at[pl.ds(r, 1), :, pl.ds(0, lon)], wx_ref.at[pl.ds(r, 1)], sems.at[r])
            for r in range(wx_ref.shape[0])
        ]
        order = []
        for a in range(lat_rows):
            for r in (a, lat_rows + a, 2 * lat_rows + a, 3 * lat_rows if a == 0 else lat_rows + a - 1):
                if r not in order:
                    order.append(r)
        for r in order:
            copies[r].start()
        waited = set()

        def ready(a):
            for r in (a, lat_rows + a, 2 * lat_rows + a, 3 * lat_rows if a == 0 else lat_rows + a - 1):
                if r not in waited:
                    copies[r].wait()
                    waited.add(r)

        fill_coefficients(north_ref, wx_ref, coef_ref, ready)

    def stencil(a, qa, qm, qp):
        result = (
            coef_ref[0, a] * qa
            + coef_ref[1, a] * pltpu.roll(qa, lon - 1, 1)
            + coef_ref[2, a] * pltpu.roll(qa, 1, 1)
            + coef_ref[3, a] * qp
            + coef_ref[4, a] * qm
            + coef_ref[5, a] * pltpu.roll(qa, levels - 1, 0)
            + coef_ref[6, a] * pltpu.roll(qa, 1, 0)
        )
        return result, result[0:1] + src_ref[0, a : a + 1, :]

    mid_ref[0] = lo_ref[0]
    mid_ref[lat_rows - 1] = hi_ref[0]
    for a in range(1, lat_rows - 1):
        result, surface = stencil(a, q_ref[0, a], q_ref[0, a - 1], q_ref[0, a + 1])
        mid_ref[a] = result
        mid_ref[a, 0:1, :] = surface
        if a == 1:
            lo_in_ref[0] = mid_ref[a]
        if a == lat_rows - 2:
            hi_in_ref[0] = mid_ref[a]
    for a in range(1, lat_rows - 1):
        result, surface = stencil(a, mid_ref[a], mid_ref[a - 1], mid_ref[a + 1])
        o_ref[0, a] = result
        o_ref[0, a, 0:1, :] = surface


def fused_steps(state, lo, hi, weather, emission, north_open):
    tracers, lat_rows, levels, lon = state.shape
    row = pl.BlockSpec((1, lat_rows, levels, lon), lambda k: (k, 0, 0, 0))
    edge = pl.BlockSpec((1, levels, lon), lambda k: (k, 0, 0))
    grid_spec = pltpu.PrefetchScalarGridSpec(
        num_scalar_prefetch=0,
        grid=(tracers,),
        in_specs=[
            pl.BlockSpec(memory_space=pltpu.SMEM),
            row,
            edge,
            edge,
            pl.BlockSpec(memory_space=pl.ANY),
            pl.BlockSpec((1, lat_rows, lon), lambda k: (k, 0, 0)),
        ],
        out_specs=[row, edge, edge],
        scratch_shapes=[
            pltpu.VMEM((7, lat_rows, levels, lon), jnp.float32),
            pltpu.VMEM((lat_rows, levels, lon), jnp.float32),
            pltpu.VMEM((weather.shape[0], levels, lon), jnp.float32),
            pltpu.SemaphoreType.DMA((weather.shape[0],)),
        ],
    )
    return pl.pallas_call(
        fused_kernel,
        grid_spec=grid_spec,
        out_shape=[jax.ShapeDtypeStruct(state.shape, state.dtype)]
        + [jax.ShapeDtypeStruct((tracers, levels, lon), state.dtype)] * 2,
        compiler_params=pltpu.CompilerParams(dimension_semantics=("arbitrary",)),
    )(north_open, state, lo, hi, weather, emission)


def on_device(
    tracer_state,
    control,
    prior_tiles,
    tile_index,
    region_map,
    region_sigma,
    zonal_courant,
    meridional_courant,
    vertical_diffusion,
):
    band_count = lax.axis_size("band")
    band_index = lax.axis_index("band")
    tiles_count = prior_tiles.shape[0]
    lat_rows = control.shape[1]

    latitude = band_index * lat_rows + jnp.arange(lat_rows, dtype=jnp.int32)
    north_open = (latitude < band_count * lat_rows - 1).astype(jnp.float32)
    choose = (
        tile_index[:, :, None] == lax.broadcasted_iota(jnp.int32, (1, 1, tiles_count), 2)
    ).astype(jnp.float32)
    own_row = lax.dynamic_slice_in_dim(choose, band_index, 1, 0)[0]
    row_tiles = jnp.einsum("bt,tmn->bmn", own_row, prior_tiles, precision=exact_dot)
    own_tile = lax.dynamic_index_in_dim(row_tiles, band_index, 0, keepdims=False)
    prior_field = jnp.einsum("jm,kmn->kjn", own_tile, control, precision=exact_dot)
    south_v = passed_along(meridional_courant[-1:], "band", 1)
    parts, (north_open, row_tiles, prior_field) = lax.optimization_barrier(
        ((zonal_courant, meridional_courant, vertical_diffusion, south_v), (north_open, row_tiles, prior_field))
    )
    pack = packed(list(parts))
    weather = relay_gather(pack, "tracer")
    held_state, held_control, _ = lax.optimization_barrier((tracer_state, control, pack))
    q_south = passed_along(held_state[:, -1], "band", 1)
    q_north = passed_along(held_state[:, 0], "band", -1)
    for s in range(1, band_count):
        pairs = [(i, (i + s) % band_count) for i in range(band_count)]
        part = lax.ppermute(held_control, "band", pairs)
        source_band = (band_index - s) % band_count
        tile = lax.dynamic_index_in_dim(row_tiles, source_band, 0, keepdims=False)
        prior_field = prior_field + jnp.einsum("jm,kmn->kjn", tile, part, precision=exact_dot)
    regions = region_sigma.shape[1]
    onehot = (region_map[:, :, None] == lax.broadcasted_iota(jnp.int32, (1, 1, regions), 2)).astype(
        jnp.float32
    )
    cell_sigma = jnp.einsum("kr,jnr->kjn", region_sigma, onehot, precision=exact_dot)
    emission = cell_sigma * prior_field

    rim = (tracer_state[:, 0], tracer_state[:, lat_rows - 1], tracer_state[:, 1], tracer_state[:, lat_rows - 2])
    bottom_row, top_row = edge_step(rim, None, q_south, q_north, weather, emission, north_open)
    s1_south = passed_along(top_row, "band", 1)
    s1_north = passed_along(bottom_row, "band", -1)
    inside, bottom_in, top_in = fused_steps(tracer_state, bottom_row, top_row, weather, emission, north_open)
    rim = (bottom_row, top_row, bottom_in, top_in)
    tracer_field = edge_step(rim, inside, s1_south, s1_north, weather, emission, north_open)
    return (tracer_field, emission)


def solution(mesh):
    in_specs = (
        P(("inv", "tracer"), "band", None, None),
        P(("inv", "tracer"), "band", None),
        P(),
        P(),
        P("band", None),
        P("tracer", None),
        P(("inv", "band"), None, "tracer"),
        P(("inv", "band"), None, "tracer"),
        P(("inv", "band"), None, "tracer"),
    )
    out_specs = (P(("inv", "tracer"), "band", None, None), P(("inv", "tracer"), "band", None))
    return jax.shard_map(
        on_device, mesh=mesh, in_specs=in_specs, out_specs=out_specs, check_vma=False
    )
```

```python
import functools

import jax
import jax.numpy as jnp
from jax import lax
from jax.experimental import pallas as pl
from jax.experimental.pallas import tpu as pltpu
from jax.sharding import PartitionSpec as P

exact_dot = lax.Precision.HIGHEST


def passed_along(value, axis, by):
    count = lax.axis_size(axis)
    pairs = [(i, i + by) for i in range(count) if 0 <= i + by < count]
    return lax.ppermute(value, axis, pairs)


def pack_kernel(*refs):
    parts, out_ref = refs[:-1], refs[-1]
    row = 0
    for part in parts:
        rows = part.shape[0]
        out_ref[row : row + rows] = part[...]
        row += rows


def packed(parts):
    rows = sum(part.shape[0] for part in parts)
    return pl.pallas_call(
        pack_kernel,
        out_shape=jax.ShapeDtypeStruct((rows,) + parts[0].shape[1:], parts[0].dtype),
    )(*parts)


def relay_gather(x, axis):
    count = lax.axis_size(axis)
    me = lax.axis_index(axis)
    rows, levels, width = x.shape
    buf = jnp.zeros((rows, levels, (count + 1) * width), x.dtype)
    buf = lax.dynamic_update_slice(buf, x, (0, 0, me * width))
    right = left = x
    for r in range(1, count):
        right = lax.ppermute(right, axis, [(i, i + 1) for i in range(r - 1, count - 1)])
        left = lax.ppermute(left, axis, [(j, j - 1) for j in range(1, count - r + 1)])
        slot = jnp.where(me - r >= 0, me - r, count)
        buf = lax.dynamic_update_slice(buf, right, (0, 0, slot * width))
        slot = jnp.where(me + r < count, me + r, count)
        buf = lax.dynamic_update_slice(buf, left, (0, 0, slot * width))
    return buf


def fill_coefficients(north_ref, wx_ref, coef_ref):
    lat_rows = coef_ref.shape[1]
    levels, lon = coef_ref.shape[2], coef_ref.shape[3]
    level = lax.broadcasted_iota(jnp.int32, (levels, lon), 0)
    not_top = level < levels - 1
    not_bottom = level > 0
    for a in range(lat_rows):
        u = wx_ref[a]
        uw = pltpu.roll(u, 1, 1)
        v = wx_ref[lat_rows + a] * north_ref[a]
        vm = wx_ref[3 * lat_rows] if a == 0 else wx_ref[lat_rows + a - 1]
        w = wx_ref[2 * lat_rows + a]
        w_up = jnp.where(not_top, w, 0.0)
        w_down = jnp.where(not_bottom, pltpu.roll(w, 1, 0), 0.0)
        coef_ref[0, a] = (
            1.0
            - jnp.maximum(u, 0.0)
            + jnp.minimum(uw, 0.0)
            - jnp.maximum(v, 0.0)
            + jnp.minimum(vm, 0.0)
            - w_up
            - w_down
        )
        coef_ref[1, a] = -jnp.minimum(u, 0.0)
        coef_ref[2, a] = jnp.maximum(uw, 0.0)
        coef_ref[3, a] = -jnp.minimum(v, 0.0)
        coef_ref[4, a] = jnp.maximum(vm, 0.0)
        coef_ref[5, a] = w_up
        coef_ref[6, a] = w_down


def step_kernel(north_ref, q_ref, qs_ref, qn_ref, wx_ref, src_ref, *rest, rows=None):
    o_ref = rest[0]
    edges = rest[1:-1]
    coef_ref = rest[-1]
    lat_rows = q_ref.shape[1]
    rows = range(lat_rows) if rows is None else rows
    levels, lon = q_ref.shape[2], q_ref.shape[3]
    level = lax.broadcasted_iota(jnp.int32, (levels, lon), 0)
    not_top = level < levels - 1
    not_bottom = level > 0

    @pl.when(pl.program_id(0) == 0)
    def _():
        fill_coefficients(north_ref, wx_ref, coef_ref)

    for a in rows:
        qa = q_ref[0, a]
        qm = qs_ref[0] if a == 0 else q_ref[0, a - 1]
        qp = qn_ref[0] if a == lat_rows - 1 else q_ref[0, a + 1]
        result = (
            coef_ref[0, a] * qa
            + coef_ref[1, a] * pltpu.roll(qa, lon - 1, 1)
            + coef_ref[2, a] * pltpu.roll(qa, 1, 1)
            + coef_ref[3, a] * qp
            + coef_ref[4, a] * qm
            + coef_ref[5, a] * pltpu.roll(qa, levels - 1, 0)
            + coef_ref[6, a] * pltpu.roll(qa, 1, 0)
        )
        surface = result[0:1] + src_ref[0, a : a + 1, :]
        targets = [o_ref.at[0, a]]
        if edges and a == 0:
            targets.append(edges[0].at[0])
        if edges and a == lat_rows - 1:
            targets.append(edges[1].at[0])
        for target in targets:
            target[...] = result
            target[0:1, :] = surface


def advance(state, south, north, weather, emission, north_open, with_edges):
    tracers, lat_rows, levels, lon = state.shape
    row = pl.BlockSpec((1, lat_rows, levels, lon), lambda k: (k, 0, 0, 0))
    edge = pl.BlockSpec((1, levels, lon), lambda k: (k, 0, 0))
    out_specs = [row]
    out_shape = [jax.ShapeDtypeStruct(state.shape, state.dtype)]
    if with_edges:
        out_specs += [edge, edge]
        out_shape += [jax.ShapeDtypeStruct((tracers, levels, lon), state.dtype)] * 2
    grid_spec = pltpu.PrefetchScalarGridSpec(
        num_scalar_prefetch=0,
        grid=(tracers,),
        in_specs=[
            pl.BlockSpec(memory_space=pltpu.SMEM),
            row,
            edge,
            edge,
            pl.BlockSpec(weather.shape[:2] + (lon,), lambda k: (0, 0, 0)),
            pl.BlockSpec((1, lat_rows, lon), lambda k: (k, 0, 0)),
        ],
        out_specs=out_specs,
        scratch_shapes=[pltpu.VMEM((7, lat_rows, levels, lon), jnp.float32)],
    )
    return pl.pallas_call(
        step_kernel,
        grid_spec=grid_spec,
        out_shape=out_shape,
        compiler_params=pltpu.CompilerParams(dimension_semantics=("arbitrary",)),
    )(north_open, state, south, north, weather, emission)


def interior_step(state, weather, emission, north_open):
    tracers, lat_rows, levels, lon = state.shape
    row = pl.BlockSpec((1, lat_rows, levels, lon), lambda k: (k, 0, 0, 0))
    kernel = functools.partial(
        lambda n, q, w, e, o, c, rows: step_kernel(n, q, None, None, w, e, o, c, rows=rows),
        rows=range(1, lat_rows - 1),
    )
    grid_spec = pltpu.PrefetchScalarGridSpec(
        num_scalar_prefetch=0,
        grid=(tracers,),
        in_specs=[
            pl.BlockSpec(memory_space=pltpu.SMEM),
            row,
            pl.BlockSpec(weather.shape[:2] + (lon,), lambda k: (0, 0, 0)),
            pl.BlockSpec((1, lat_rows, lon), lambda k: (k, 0, 0)),
        ],
        out_specs=row,
        scratch_shapes=[pltpu.VMEM((7, lat_rows, levels, lon), jnp.float32)],
    )
    return pl.pallas_call(
        kernel,
        grid_spec=grid_spec,
        out_shape=jax.ShapeDtypeStruct(state.shape, state.dtype),
        compiler_params=pltpu.CompilerParams(dimension_semantics=("arbitrary",)),
    )(north_open, state, weather, emission)


def edge_kernel(north_ref, lo_ref, hi_ref, lo_in_ref, hi_in_ref, qs_ref, qn_ref, *rest):
    met_refs, src_ref, outs = rest[:8], rest[8], rest[9:]
    split = len(outs) == 2
    if not split:
        o_hbm, stage, sems = outs
    tracers, lat_rows = src_ref.shape[0], src_ref.shape[1]
    levels, lon = lo_ref.shape[1], lo_ref.shape[2]
    level = lax.broadcasted_iota(jnp.int32, (levels, lon), 0)
    not_top = level < levels - 1
    not_bottom = level > 0
    last = lat_rows - 1
    for top in (0, 1):
        a = top * last
        u_ref, v_ref, vm_ref, w_ref = met_refs[4 * top : 4 * top + 4]
        u = u_ref[0]
        uw = pltpu.roll(u, 1, 1)
        v = v_ref[0] * north_ref[a]
        vm = vm_ref[0]
        w = w_ref[0]
        w_up = jnp.where(not_top, w, 0.0)
        w_down = jnp.where(not_bottom, pltpu.roll(w, 1, 0), 0.0)
        c_self = (
            1.0
            - jnp.maximum(u, 0.0)
            + jnp.minimum(uw, 0.0)
            - jnp.maximum(v, 0.0)
            + jnp.minimum(vm, 0.0)
            - w_up
            - w_down
        )
        c_east = -jnp.minimum(u, 0.0)
        c_west = jnp.maximum(uw, 0.0)
        c_north = -jnp.minimum(v, 0.0)
        c_south = jnp.maximum(vm, 0.0)
        for k in range(tracers):
            qa = hi_ref[k] if top else lo_ref[k]
            inner = hi_in_ref[k] if top else lo_in_ref[k]
            qm = inner if top else qs_ref[k]
            qp = qn_ref[k] if top else inner
            result = (
                c_self * qa
                + c_east * pltpu.roll(qa, lon - 1, 1)
                + c_west * pltpu.roll(qa, 1, 1)
                + c_north * qp
                + c_south * qm
                + w_up * pltpu.roll(qa, levels - 1, 0)
                + w_down * pltpu.roll(qa, 1, 0)
            )
            surface = result[0:1] + src_ref[k, a : a + 1, :]
            target = outs[top].at[k] if split else stage.at[top, k, 0]
            target[...] = result
            target[0:1, :] = surface
    if not split:
        copies = [
            pltpu.make_async_copy(stage.at[top], o_hbm.at[:, pl.ds(top * last, 1)], sems.at[top])
            for top in (0, 1)
        ]
        for copy in copies:
            copy.start()
        for copy in copies:
            copy.wait()


def edge_step(rows, base, south, north, weather, emission, north_open):
    tracers, levels, lon = rows[0].shape
    lat_rows = emission.shape[1]
    whole = pl.BlockSpec((tracers, levels, lon), lambda i: (0, 0, 0))
    in_specs = [pl.BlockSpec(memory_space=pltpu.SMEM)] + [whole] * 6
    last = lat_rows - 1
    met_rows = []
    for a, below in ((0, 3 * lat_rows), (last, lat_rows + last - 1)):
        met_rows += [a, lat_rows + a, below, 2 * lat_rows + a]
    in_specs += [pl.BlockSpec((1, levels, lon), lambda i, r=r: (r, 0, 0)) for r in met_rows]
    in_specs += [pl.BlockSpec(emission.shape, lambda i: (0, 0, 0))]
    args = [north_open, *rows, south, north] + [weather] * len(met_rows) + [emission]
    edge = pl.BlockSpec((tracers, levels, lon), lambda i: (0, 0, 0))
    scratch = []
    if base is None:
        out_specs = [edge, edge]
        out_shape = [jax.ShapeDtypeStruct((tracers, levels, lon), jnp.float32)] * 2
        aliases = {}
        kernel = edge_kernel
    else:
        in_specs.append(pl.BlockSpec(memory_space=pl.ANY))
        args.append(base)
        out_specs = pl.BlockSpec(memory_space=pl.ANY)
        out_shape = jax.ShapeDtypeStruct(base.shape, base.dtype)
        aliases = {len(args) - 1: 0}
        scratch = [pltpu.VMEM((2, tracers, 1, levels, lon), jnp.float32), pltpu.SemaphoreType.DMA((2,))]
        kernel = lambda *refs: edge_kernel(*refs[:16], *refs[17:])
    grid_spec = pltpu.PrefetchScalarGridSpec(
        num_scalar_prefetch=0, grid=(1,), in_specs=in_specs, out_specs=out_specs, scratch_shapes=scratch
    )
    return pl.pallas_call(
        kernel,
        grid_spec=grid_spec,
        out_shape=out_shape,
        input_output_aliases=aliases,
    )(*args)


def fused_kernel(north_ref, q_ref, lo_ref, hi_ref, wx_ref, src_ref, o_ref, lo_in_ref, hi_in_ref, coef_ref, mid_ref):
    lat_rows = q_ref.shape[1]
    levels, lon = q_ref.shape[2], q_ref.shape[3]

    @pl.when(pl.program_id(0) == 0)
    def _():
        fill_coefficients(north_ref, wx_ref, coef_ref)

    def stencil(a, qa, qm, qp):
        result = (
            coef_ref[0, a] * qa
            + coef_ref[1, a] * pltpu.roll(qa, lon - 1, 1)
            + coef_ref[2, a] * pltpu.roll(qa, 1, 1)
            + coef_ref[3, a] * qp
            + coef_ref[4, a] * qm
            + coef_ref[5, a] * pltpu.roll(qa, levels - 1, 0)
            + coef_ref[6, a] * pltpu.roll(qa, 1, 0)
        )
        return result, result[0:1] + src_ref[0, a : a + 1, :]

    mid_ref[0] = lo_ref[0]
    mid_ref[lat_rows - 1] = hi_ref[0]
    for a in range(1, lat_rows - 1):
        result, surface = stencil(a, q_ref[0, a], q_ref[0, a - 1], q_ref[0, a + 1])
        mid_ref[a] = result
        mid_ref[a, 0:1, :] = surface
        if a == 1:
            lo_in_ref[0] = mid_ref[a]
        if a == lat_rows - 2:
            hi_in_ref[0] = mid_ref[a]
    for a in range(1, lat_rows - 1):
        result, surface = stencil(a, mid_ref[a], mid_ref[a - 1], mid_ref[a + 1])
        o_ref[0, a] = result
        o_ref[0, a, 0:1, :] = surface


def fused_steps(state, lo, hi, weather, emission, north_open):
    tracers, lat_rows, levels, lon = state.shape
    row = pl.BlockSpec((1, lat_rows, levels, lon), lambda k: (k, 0, 0, 0))
    edge = pl.BlockSpec((1, levels, lon), lambda k: (k, 0, 0))
    grid_spec = pltpu.PrefetchScalarGridSpec(
        num_scalar_prefetch=0,
        grid=(tracers,),
        in_specs=[
            pl.BlockSpec(memory_space=pltpu.SMEM),
            row,
            edge,
            edge,
            pl.BlockSpec(weather.shape[:2] + (lon,), lambda k: (0, 0, 0)),
            pl.BlockSpec((1, lat_rows, lon), lambda k: (k, 0, 0)),
        ],
        out_specs=[row, edge, edge],
        scratch_shapes=[
            pltpu.VMEM((7, lat_rows, levels, lon), jnp.float32),
            pltpu.VMEM((lat_rows, levels, lon), jnp.float32),
        ],
    )
    return pl.pallas_call(
        fused_kernel,
        grid_spec=grid_spec,
        out_shape=[jax.ShapeDtypeStruct(state.shape, state.dtype)]
        + [jax.ShapeDtypeStruct((tracers, levels, lon), state.dtype)] * 2,
        compiler_params=pltpu.CompilerParams(dimension_semantics=("arbitrary",)),
    )(north_open, state, lo, hi, weather, emission)


def on_device(
    tracer_state,
    control,
    prior_tiles,
    tile_index,
    region_map,
    region_sigma,
    zonal_courant,
    meridional_courant,
    vertical_diffusion,
):
    band_count = lax.axis_size("band")
    band_index = lax.axis_index("band")
    tiles_count = prior_tiles.shape[0]
    lat_rows = control.shape[1]

    latitude = band_index * lat_rows + jnp.arange(lat_rows, dtype=jnp.int32)
    north_open = (latitude < band_count * lat_rows - 1).astype(jnp.float32)
    choose = (
        tile_index[:, :, None] == lax.broadcasted_iota(jnp.int32, (1, 1, tiles_count), 2)
    ).astype(jnp.float32)
    own_row = lax.dynamic_slice_in_dim(choose, band_index, 1, 0)[0]
    row_tiles = jnp.einsum("bt,tmn->bmn", own_row, prior_tiles, precision=exact_dot)
    own_tile = lax.dynamic_index_in_dim(row_tiles, band_index, 0, keepdims=False)
    prior_field = jnp.einsum("jm,kmn->kjn", own_tile, control, precision=exact_dot)
    south_v = passed_along(meridional_courant[-1:], "band", 1)
    parts, (north_open, row_tiles, prior_field) = lax.optimization_barrier(
        ((zonal_courant, meridional_courant, vertical_diffusion, south_v), (north_open, row_tiles, prior_field))
    )
    pack = packed(list(parts))
    weather = relay_gather(pack, "tracer")
    held_state, held_control, _ = lax.optimization_barrier((tracer_state, control, pack))
    q_south = passed_along(held_state[:, -1], "band", 1)
    q_north = passed_along(held_state[:, 0], "band", -1)
    for s in range(1, band_count):
        pairs = [(i, (i + s) % band_count) for i in range(band_count)]
        part = lax.ppermute(held_control, "band", pairs)
        source_band = (band_index - s) % band_count
        tile = lax.dynamic_index_in_dim(row_tiles, source_band, 0, keepdims=False)
        prior_field = prior_field + jnp.einsum("jm,kmn->kjn", tile, part, precision=exact_dot)
    regions = region_sigma.shape[1]
    onehot = (region_map[:, :, None] == lax.broadcasted_iota(jnp.int32, (1, 1, regions), 2)).astype(
        jnp.float32
    )
    cell_sigma = jnp.einsum("kr,jnr->kjn", region_sigma, onehot, precision=exact_dot)
    emission = cell_sigma * prior_field

    rim = (tracer_state[:, 0], tracer_state[:, lat_rows - 1], tracer_state[:, 1], tracer_state[:, lat_rows - 2])
    bottom_row, top_row = edge_step(rim, None, q_south, q_north, weather, emission, north_open)
    s1_south = passed_along(top_row, "band", 1)
    s1_north = passed_along(bottom_row, "band", -1)
    inside, bottom_in, top_in = fused_steps(tracer_state, bottom_row, top_row, weather, emission, north_open)
    rim = (bottom_row, top_row, bottom_in, top_in)
    tracer_field = edge_step(rim, inside, s1_south, s1_north, weather, emission, north_open)
    return (tracer_field, emission)


def solution(mesh):
    in_specs = (
        P(("inv", "tracer"), "band", None, None),
        P(("inv", "tracer"), "band", None),
        P(),
        P(),
        P("band", None),
        P("tracer", None),
        P(("inv", "band"), None, "tracer"),
        P(("inv", "band"), None, "tracer"),
        P(("inv", "band"), None, "tracer"),
    )
    out_specs = (P(("inv", "tracer"), "band", None, None), P(("inv", "tracer"), "band", None))
    return jax.shard_map(
        on_device, mesh=mesh, in_specs=in_specs, out_specs=out_specs, check_vma=False
    )
```

```python
import functools

import jax
import jax.numpy as jnp
from jax import lax
from jax.experimental import pallas as pl
from jax.experimental.pallas import tpu as pltpu
from jax.sharding import PartitionSpec as P

exact_dot = lax.Precision.HIGHEST


def passed_along(value, axis, by):
    count = lax.axis_size(axis)
    pairs = [(i, i + by) for i in range(count) if 0 <= i + by < count]
    return lax.ppermute(value, axis, pairs)


def pack_kernel(*refs):
    parts, out_ref = refs[:-1], refs[-1]
    row = 0
    for part in parts:
        rows = part.shape[0]
        out_ref[row : row + rows] = part[...]
        row += rows


def packed(parts):
    rows = sum(part.shape[0] for part in parts)
    return pl.pallas_call(
        pack_kernel,
        out_shape=jax.ShapeDtypeStruct((rows,) + parts[0].shape[1:], parts[0].dtype),
    )(*parts)


def relay_gather(x, axis):
    count = lax.axis_size(axis)
    me = lax.axis_index(axis)
    rows, levels, width = x.shape
    buf = jnp.zeros((rows, levels, (count + 1) * width), x.dtype)
    buf = lax.dynamic_update_slice(buf, x, (0, 0, me * width))
    right = left = x
    for r in range(1, count):
        right = lax.ppermute(right, axis, [(i, i + 1) for i in range(r - 1, count - 1)])
        left = lax.ppermute(left, axis, [(j, j - 1) for j in range(1, count - r + 1)])
        slot = jnp.where(me - r >= 0, me - r, count)
        buf = lax.dynamic_update_slice(buf, right, (0, 0, slot * width))
        slot = jnp.where(me + r < count, me + r, count)
        buf = lax.dynamic_update_slice(buf, left, (0, 0, slot * width))
    return buf


def fill_coefficients(north_ref, wx_ref, coef_ref, rows=None):
    lat_rows = coef_ref.shape[1]
    levels, lon = coef_ref.shape[2], coef_ref.shape[3]
    level = lax.broadcasted_iota(jnp.int32, (levels, lon), 0)
    not_top = level < levels - 1
    not_bottom = level > 0
    for a in range(lat_rows) if rows is None else rows:
        u = wx_ref[a]
        uw = pltpu.roll(u, 1, 1)
        v = wx_ref[lat_rows + a] * north_ref[a]
        vm = wx_ref[3 * lat_rows] if a == 0 else wx_ref[lat_rows + a - 1]
        w = wx_ref[2 * lat_rows + a]
        w_up = jnp.where(not_top, w, 0.0)
        w_down = jnp.where(not_bottom, pltpu.roll(w, 1, 0), 0.0)
        coef_ref[0, a] = (
            1.0
            - jnp.maximum(u, 0.0)
            + jnp.minimum(uw, 0.0)
            - jnp.maximum(v, 0.0)
            + jnp.minimum(vm, 0.0)
            - w_up
            - w_down
        )
        coef_ref[1, a] = -jnp.minimum(u, 0.0)
        coef_ref[2, a] = jnp.maximum(uw, 0.0)
        coef_ref[3, a] = -jnp.minimum(v, 0.0)
        coef_ref[4, a] = jnp.maximum(vm, 0.0)
        coef_ref[5, a] = w_up
        coef_ref[6, a] = w_down


def step_kernel(north_ref, q_ref, qs_ref, qn_ref, wx_ref, src_ref, *rest, rows=None):
    o_ref = rest[0]
    edges = rest[1:-1]
    coef_ref = rest[-1]
    lat_rows = q_ref.shape[1]
    rows = range(lat_rows) if rows is None else rows
    levels, lon = q_ref.shape[2], q_ref.shape[3]
    level = lax.broadcasted_iota(jnp.int32, (levels, lon), 0)
    not_top = level < levels - 1
    not_bottom = level > 0

    @pl.when(pl.program_id(0) == 0)
    def _():
        fill_coefficients(north_ref, wx_ref, coef_ref)

    for a in rows:
        qa = q_ref[0, a]
        qm = qs_ref[0] if a == 0 else q_ref[0, a - 1]
        qp = qn_ref[0] if a == lat_rows - 1 else q_ref[0, a + 1]
        result = (
            coef_ref[0, a] * qa
            + coef_ref[1, a] * pltpu.roll(qa, lon - 1, 1)
            + coef_ref[2, a] * pltpu.roll(qa, 1, 1)
            + coef_ref[3, a] * qp
            + coef_ref[4, a] * qm
            + coef_ref[5, a] * pltpu.roll(qa, levels - 1, 0)
            + coef_ref[6, a] * pltpu.roll(qa, 1, 0)
        )
        surface = result[0:1] + src_ref[0, a : a + 1, :]
        targets = [o_ref.at[0, a]]
        if edges and a == 0:
            targets.append(edges[0].at[0])
        if edges and a == lat_rows - 1:
            targets.append(edges[1].at[0])
        for target in targets:
            target[...] = result
            target[0:1, :] = surface


def advance(state, south, north, weather, emission, north_open, with_edges):
    tracers, lat_rows, levels, lon = state.shape
    row = pl.BlockSpec((1, lat_rows, levels, lon), lambda k: (k, 0, 0, 0))
    edge = pl.BlockSpec((1, levels, lon), lambda k: (k, 0, 0))
    out_specs = [row]
    out_shape = [jax.ShapeDtypeStruct(state.shape, state.dtype)]
    if with_edges:
        out_specs += [edge, edge]
        out_shape += [jax.ShapeDtypeStruct((tracers, levels, lon), state.dtype)] * 2
    grid_spec = pltpu.PrefetchScalarGridSpec(
        num_scalar_prefetch=0,
        grid=(tracers,),
        in_specs=[
            pl.BlockSpec(memory_space=pltpu.SMEM),
            row,
            edge,
            edge,
            pl.BlockSpec(weather.shape[:2] + (lon,), lambda k: (0, 0, 0)),
            pl.BlockSpec((1, lat_rows, lon), lambda k: (k, 0, 0)),
        ],
        out_specs=out_specs,
        scratch_shapes=[pltpu.VMEM((7, lat_rows, levels, lon), jnp.float32)],
    )
    return pl.pallas_call(
        step_kernel,
        grid_spec=grid_spec,
        out_shape=out_shape,
        compiler_params=pltpu.CompilerParams(dimension_semantics=("arbitrary",)),
    )(north_open, state, south, north, weather, emission)


def interior_step(state, weather, emission, north_open):
    tracers, lat_rows, levels, lon = state.shape
    row = pl.BlockSpec((1, lat_rows, levels, lon), lambda k: (k, 0, 0, 0))
    kernel = functools.partial(
        lambda n, q, w, e, o, c, rows: step_kernel(n, q, None, None, w, e, o, c, rows=rows),
        rows=range(1, lat_rows - 1),
    )
    grid_spec = pltpu.PrefetchScalarGridSpec(
        num_scalar_prefetch=0,
        grid=(tracers,),
        in_specs=[
            pl.BlockSpec(memory_space=pltpu.SMEM),
            row,
            pl.BlockSpec(weather.shape[:2] + (lon,), lambda k: (0, 0, 0)),
            pl.BlockSpec((1, lat_rows, lon), lambda k: (k, 0, 0)),
        ],
        out_specs=row,
        scratch_shapes=[pltpu.VMEM((7, lat_rows, levels, lon), jnp.float32)],
    )
    return pl.pallas_call(
        kernel,
        grid_spec=grid_spec,
        out_shape=jax.ShapeDtypeStruct(state.shape, state.dtype),
        compiler_params=pltpu.CompilerParams(dimension_semantics=("arbitrary",)),
    )(north_open, state, weather, emission)


def edge_kernel(north_ref, lo_ref, hi_ref, lo_in_ref, hi_in_ref, qs_ref, qn_ref, *rest):
    met_refs, src_ref, outs = rest[:8], rest[8], rest[9:]
    split = len(outs) == 2
    if not split:
        o_hbm, stage, sems = outs
    tracers, lat_rows = src_ref.shape[0], src_ref.shape[1]
    levels, lon = lo_ref.shape[1], lo_ref.shape[2]
    level = lax.broadcasted_iota(jnp.int32, (levels, lon), 0)
    not_top = level < levels - 1
    not_bottom = level > 0
    last = lat_rows - 1
    for top in (0, 1):
        a = top * last
        u_ref, v_ref, vm_ref, w_ref = met_refs[4 * top : 4 * top + 4]
        u = u_ref[0]
        uw = pltpu.roll(u, 1, 1)
        v = v_ref[0] * north_ref[a]
        vm = vm_ref[0]
        w = w_ref[0]
        w_up = jnp.where(not_top, w, 0.0)
        w_down = jnp.where(not_bottom, pltpu.roll(w, 1, 0), 0.0)
        c_self = (
            1.0
            - jnp.maximum(u, 0.0)
            + jnp.minimum(uw, 0.0)
            - jnp.maximum(v, 0.0)
            + jnp.minimum(vm, 0.0)
            - w_up
            - w_down
        )
        c_east = -jnp.minimum(u, 0.0)
        c_west = jnp.maximum(uw, 0.0)
        c_north = -jnp.minimum(v, 0.0)
        c_south = jnp.maximum(vm, 0.0)
        for k in range(tracers):
            qa = hi_ref[k] if top else lo_ref[k]
            inner = hi_in_ref[k] if top else lo_in_ref[k]
            qm = inner if top else qs_ref[k]
            qp = qn_ref[k] if top else inner
            result = (
                c_self * qa
                + c_east * pltpu.roll(qa, lon - 1, 1)
                + c_west * pltpu.roll(qa, 1, 1)
                + c_north * qp
                + c_south * qm
                + w_up * pltpu.roll(qa, levels - 1, 0)
                + w_down * pltpu.roll(qa, 1, 0)
            )
            surface = result[0:1] + src_ref[k, a : a + 1, :]
            target = outs[top].at[k] if split else stage.at[top, k, 0]
            target[...] = result
            target[0:1, :] = surface
    if not split:
        copies = [
            pltpu.make_async_copy(stage.at[top], o_hbm.at[:, pl.ds(top * last, 1)], sems.at[top])
            for top in (0, 1)
        ]
        for copy in copies:
            copy.start()
        for copy in copies:
            copy.wait()


def edge_step(rows, base, south, north, weather, emission, north_open):
    tracers, levels, lon = rows[0].shape
    lat_rows = emission.shape[1]
    whole = pl.BlockSpec((tracers, levels, lon), lambda i: (0, 0, 0))
    in_specs = [pl.BlockSpec(memory_space=pltpu.SMEM)] + [whole] * 6
    last = lat_rows - 1
    met_rows = []
    for a, below in ((0, 3 * lat_rows), (last, lat_rows + last - 1)):
        met_rows += [a, lat_rows + a, below, 2 * lat_rows + a]
    in_specs += [pl.BlockSpec((1, levels, lon), lambda i, r=r: (r, 0, 0)) for r in met_rows]
    in_specs += [pl.BlockSpec(emission.shape, lambda i: (0, 0, 0))]
    args = [north_open, *rows, south, north] + [weather] * len(met_rows) + [emission]
    edge = pl.BlockSpec((tracers, levels, lon), lambda i: (0, 0, 0))
    scratch = []
    if base is None:
        out_specs = [edge, edge]
        out_shape = [jax.ShapeDtypeStruct((tracers, levels, lon), jnp.float32)] * 2
        aliases = {}
        kernel = edge_kernel
    else:
        in_specs.append(pl.BlockSpec(memory_space=pl.ANY))
        args.append(base)
        out_specs = pl.BlockSpec(memory_space=pl.ANY)
        out_shape = jax.ShapeDtypeStruct(base.shape, base.dtype)
        aliases = {len(args) - 1: 0}
        scratch = [pltpu.VMEM((2, tracers, 1, levels, lon), jnp.float32), pltpu.SemaphoreType.DMA((2,))]
        kernel = lambda *refs: edge_kernel(*refs[:16], *refs[17:])
    grid_spec = pltpu.PrefetchScalarGridSpec(
        num_scalar_prefetch=0, grid=(1,), in_specs=in_specs, out_specs=out_specs, scratch_shapes=scratch
    )
    return pl.pallas_call(
        kernel,
        grid_spec=grid_spec,
        out_shape=out_shape,
        input_output_aliases=aliases,
    )(*args)


def fused_kernel(north_ref, q_ref, lo_ref, hi_ref, wx_ref, src_ref, o_ref, lo_in_ref, hi_in_ref, coef_ref, mid_ref):
    lat_rows = q_ref.shape[1]
    levels, lon = q_ref.shape[2], q_ref.shape[3]

    @pl.when(pl.program_id(0) == 0)
    def _():
        fill_coefficients(north_ref, wx_ref, coef_ref, range(1, lat_rows - 1))

    def stencil(a, qa, qm, qp):
        result = (
            coef_ref[0, a] * qa
            + coef_ref[1, a] * pltpu.roll(qa, lon - 1, 1)
            + coef_ref[2, a] * pltpu.roll(qa, 1, 1)
            + coef_ref[3, a] * qp
            + coef_ref[4, a] * qm
            + coef_ref[5, a] * pltpu.roll(qa, levels - 1, 0)
            + coef_ref[6, a] * pltpu.roll(qa, 1, 0)
        )
        return result, result[0:1] + src_ref[0, a : a + 1, :]

    mid_ref[0] = lo_ref[0]
    mid_ref[lat_rows - 1] = hi_ref[0]
    for a in range(1, lat_rows - 1):
        result, surface = stencil(a, q_ref[0, a], q_ref[0, a - 1], q_ref[0, a + 1])
        mid_ref[a] = result
        mid_ref[a, 0:1, :] = surface
        if a == 1:
            lo_in_ref[0] = mid_ref[a]
        if a == lat_rows - 2:
            hi_in_ref[0] = mid_ref[a]
    for a in range(1, lat_rows - 1):
        result, surface = stencil(a, mid_ref[a], mid_ref[a - 1], mid_ref[a + 1])
        o_ref[0, a] = result
        o_ref[0, a, 0:1, :] = surface


def fused_steps(state, lo, hi, weather, emission, north_open):
    tracers, lat_rows, levels, lon = state.shape
    row = pl.BlockSpec((1, lat_rows, levels, lon), lambda k: (k, 0, 0, 0))
    edge = pl.BlockSpec((1, levels, lon), lambda k: (k, 0, 0))
    grid_spec = pltpu.PrefetchScalarGridSpec(
        num_scalar_prefetch=0,
        grid=(tracers,),
        in_specs=[
            pl.BlockSpec(memory_space=pltpu.SMEM),
            row,
            edge,
            edge,
            pl.BlockSpec(weather.shape[:2] + (lon,), lambda k: (0, 0, 0)),
            pl.BlockSpec((1, lat_rows, lon), lambda k: (k, 0, 0)),
        ],
        out_specs=[row, edge, edge],
        scratch_shapes=[
            pltpu.VMEM((7, lat_rows, levels, lon), jnp.float32),
            pltpu.VMEM((lat_rows, levels, lon), jnp.float32),
        ],
    )
    return pl.pallas_call(
        fused_kernel,
        grid_spec=grid_spec,
        out_shape=[jax.ShapeDtypeStruct(state.shape, state.dtype)]
        + [jax.ShapeDtypeStruct((tracers, levels, lon), state.dtype)] * 2,
        compiler_params=pltpu.CompilerParams(dimension_semantics=("arbitrary",)),
    )(north_open, state, lo, hi, weather, emission)


def on_device(
    tracer_state,
    control,
    prior_tiles,
    tile_index,
    region_map,
    region_sigma,
    zonal_courant,
    meridional_courant,
    vertical_diffusion,
):
    band_count = lax.axis_size("band")
    band_index = lax.axis_index("band")
    tiles_count = prior_tiles.shape[0]
    lat_rows = control.shape[1]

    latitude = band_index * lat_rows + jnp.arange(lat_rows, dtype=jnp.int32)
    north_open = (latitude < band_count * lat_rows - 1).astype(jnp.float32)
    choose = (
        tile_index[:, :, None] == lax.broadcasted_iota(jnp.int32, (1, 1, tiles_count), 2)
    ).astype(jnp.float32)
    own_row = lax.dynamic_slice_in_dim(choose, band_index, 1, 0)[0]
    row_tiles = jnp.einsum("bt,tmn->bmn", own_row, prior_tiles, precision=exact_dot)
    own_tile = lax.dynamic_index_in_dim(row_tiles, band_index, 0, keepdims=False)
    prior_field = jnp.einsum("jm,kmn->kjn", own_tile, control, precision=exact_dot)
    south_v = passed_along(meridional_courant[-1:], "band", 1)
    parts, (north_open, row_tiles, prior_field) = lax.optimization_barrier(
        ((zonal_courant, meridional_courant, vertical_diffusion, south_v), (north_open, row_tiles, prior_field))
    )
    pack = packed(list(parts))
    weather = relay_gather(pack, "tracer")
    held_state, held_control, _ = lax.optimization_barrier((tracer_state, control, pack))
    q_south = passed_along(held_state[:, -1], "band", 1)
    q_north = passed_along(held_state[:, 0], "band", -1)
    for s in range(1, band_count):
        pairs = [(i, (i + s) % band_count) for i in range(band_count)]
        part = lax.ppermute(held_control, "band", pairs)
        source_band = (band_index - s) % band_count
        tile = lax.dynamic_index_in_dim(row_tiles, source_band, 0, keepdims=False)
        prior_field = prior_field + jnp.einsum("jm,kmn->kjn", tile, part, precision=exact_dot)
    regions = region_sigma.shape[1]
    onehot = (region_map[:, :, None] == lax.broadcasted_iota(jnp.int32, (1, 1, regions), 2)).astype(
        jnp.float32
    )
    cell_sigma = jnp.einsum("kr,jnr->kjn", region_sigma, onehot, precision=exact_dot)
    emission = cell_sigma * prior_field

    rim = (tracer_state[:, 0], tracer_state[:, lat_rows - 1], tracer_state[:, 1], tracer_state[:, lat_rows - 2])
    bottom_row, top_row = edge_step(rim, None, q_south, q_north, weather, emission, north_open)
    s1_south = passed_along(top_row, "band", 1)
    s1_north = passed_along(bottom_row, "band", -1)
    inside, bottom_in, top_in = fused_steps(tracer_state, bottom_row, top_row, weather, emission, north_open)
    rim = (bottom_row, top_row, bottom_in, top_in)
    tracer_field = edge_step(rim, inside, s1_south, s1_north, weather, emission, north_open)
    return (tracer_field, emission)


def solution(mesh):
    in_specs = (
        P(("inv", "tracer"), "band", None, None),
        P(("inv", "tracer"), "band", None),
        P(),
        P(),
        P("band", None),
        P("tracer", None),
        P(("inv", "band"), None, "tracer"),
        P(("inv", "band"), None, "tracer"),
        P(("inv", "band"), None, "tracer"),
    )
    out_specs = (P(("inv", "tracer"), "band", None, None), P(("inv", "tracer"), "band", None))
    return jax.shard_map(
        on_device, mesh=mesh, in_specs=in_specs, out_specs=out_specs, check_vma=False
    )
```

```python
import functools

import jax
import jax.numpy as jnp
from jax import lax
from jax.experimental import pallas as pl
from jax.experimental.pallas import tpu as pltpu
from jax.sharding import PartitionSpec as P

exact_dot = lax.Precision.HIGHEST


def passed_along(value, axis, by):
    count = lax.axis_size(axis)
    pairs = [(i, i + by) for i in range(count) if 0 <= i + by < count]
    return lax.ppermute(value, axis, pairs)


def pack_kernel(*refs):
    parts, out_ref = refs[:-1], refs[-1]
    row = 0
    for part in parts:
        rows = part.shape[0]
        out_ref[row : row + rows] = part[...]
        row += rows


def packed(parts):
    rows = sum(part.shape[0] for part in parts)
    return pl.pallas_call(
        pack_kernel,
        out_shape=jax.ShapeDtypeStruct((rows,) + parts[0].shape[1:], parts[0].dtype),
    )(*parts)


def relay_gather(x, axis):
    count = lax.axis_size(axis)
    me = lax.axis_index(axis)
    rows, levels, width = x.shape
    buf = jnp.zeros((rows, levels, (count + 1) * width), x.dtype)
    buf = lax.dynamic_update_slice(buf, x, (0, 0, me * width))
    right = left = x
    for r in range(1, count):
        right = lax.ppermute(right, axis, [(i, i + 1) for i in range(r - 1, count - 1)])
        left = lax.ppermute(left, axis, [(j, j - 1) for j in range(1, count - r + 1)])
        slot = jnp.where(me - r >= 0, me - r, count)
        buf = lax.dynamic_update_slice(buf, right, (0, 0, slot * width))
        slot = jnp.where(me + r < count, me + r, count)
        buf = lax.dynamic_update_slice(buf, left, (0, 0, slot * width))
    return buf


def fill_coefficients(north_ref, wx_ref, coef_ref, rows=None):
    lat_rows = coef_ref.shape[1]
    levels, lon = coef_ref.shape[2], coef_ref.shape[3]
    level = lax.broadcasted_iota(jnp.int32, (levels, lon), 0)
    not_top = level < levels - 1
    not_bottom = level > 0
    for a in range(lat_rows) if rows is None else rows:
        u = wx_ref[a]
        uw = pltpu.roll(u, 1, 1)
        v = wx_ref[lat_rows + a] * north_ref[a]
        vm = wx_ref[3 * lat_rows] if a == 0 else wx_ref[lat_rows + a - 1]
        w = wx_ref[2 * lat_rows + a]
        w_up = jnp.where(not_top, w, 0.0)
        w_down = jnp.where(not_bottom, pltpu.roll(w, 1, 0), 0.0)
        coef_ref[0, a] = (
            1.0
            - jnp.maximum(u, 0.0)
            + jnp.minimum(uw, 0.0)
            - jnp.maximum(v, 0.0)
            + jnp.minimum(vm, 0.0)
            - w_up
            - w_down
        )
        coef_ref[1, a] = -jnp.minimum(u, 0.0)
        coef_ref[2, a] = jnp.maximum(uw, 0.0)
        coef_ref[3, a] = -jnp.minimum(v, 0.0)
        coef_ref[4, a] = jnp.maximum(vm, 0.0)
        coef_ref[5, a] = w_up
        coef_ref[6, a] = w_down


def step_kernel(north_ref, q_ref, qs_ref, qn_ref, wx_ref, src_ref, *rest, rows=None):
    o_ref = rest[0]
    edges = rest[1:-1]
    coef_ref = rest[-1]
    lat_rows = q_ref.shape[1]
    rows = range(lat_rows) if rows is None else rows
    levels, lon = q_ref.shape[2], q_ref.shape[3]
    level = lax.broadcasted_iota(jnp.int32, (levels, lon), 0)
    not_top = level < levels - 1
    not_bottom = level > 0

    @pl.when(pl.program_id(0) == 0)
    def _():
        fill_coefficients(north_ref, wx_ref, coef_ref)

    for a in rows:
        qa = q_ref[0, a]
        qm = qs_ref[0] if a == 0 else q_ref[0, a - 1]
        qp = qn_ref[0] if a == lat_rows - 1 else q_ref[0, a + 1]
        result = (
            coef_ref[0, a] * qa
            + coef_ref[1, a] * pltpu.roll(qa, lon - 1, 1)
            + coef_ref[2, a] * pltpu.roll(qa, 1, 1)
            + coef_ref[3, a] * qp
            + coef_ref[4, a] * qm
            + coef_ref[5, a] * pltpu.roll(qa, levels - 1, 0)
            + coef_ref[6, a] * pltpu.roll(qa, 1, 0)
        )
        surface = result[0:1] + src_ref[0, a : a + 1, :]
        targets = [o_ref.at[0, a]]
        if edges and a == 0:
            targets.append(edges[0].at[0])
        if edges and a == lat_rows - 1:
            targets.append(edges[1].at[0])
        for target in targets:
            target[...] = result
            target[0:1, :] = surface


def advance(state, south, north, weather, emission, north_open, with_edges):
    tracers, lat_rows, levels, lon = state.shape
    row = pl.BlockSpec((1, lat_rows, levels, lon), lambda k: (k, 0, 0, 0))
    edge = pl.BlockSpec((1, levels, lon), lambda k: (k, 0, 0))
    out_specs = [row]
    out_shape = [jax.ShapeDtypeStruct(state.shape, state.dtype)]
    if with_edges:
        out_specs += [edge, edge]
        out_shape += [jax.ShapeDtypeStruct((tracers, levels, lon), state.dtype)] * 2
    grid_spec = pltpu.PrefetchScalarGridSpec(
        num_scalar_prefetch=0,
        grid=(tracers,),
        in_specs=[
            pl.BlockSpec(memory_space=pltpu.SMEM),
            row,
            edge,
            edge,
            pl.BlockSpec(weather.shape[:2] + (lon,), lambda k: (0, 0, 0)),
            pl.BlockSpec((1, lat_rows, lon), lambda k: (k, 0, 0)),
        ],
        out_specs=out_specs,
        scratch_shapes=[pltpu.VMEM((7, lat_rows, levels, lon), jnp.float32)],
    )
    return pl.pallas_call(
        step_kernel,
        grid_spec=grid_spec,
        out_shape=out_shape,
        compiler_params=pltpu.CompilerParams(dimension_semantics=("arbitrary",)),
    )(north_open, state, south, north, weather, emission)


def interior_step(state, weather, emission, north_open):
    tracers, lat_rows, levels, lon = state.shape
    row = pl.BlockSpec((1, lat_rows, levels, lon), lambda k: (k, 0, 0, 0))
    kernel = functools.partial(
        lambda n, q, w, e, o, c, rows: step_kernel(n, q, None, None, w, e, o, c, rows=rows),
        rows=range(1, lat_rows - 1),
    )
    grid_spec = pltpu.PrefetchScalarGridSpec(
        num_scalar_prefetch=0,
        grid=(tracers,),
        in_specs=[
            pl.BlockSpec(memory_space=pltpu.SMEM),
            row,
            pl.BlockSpec(weather.shape[:2] + (lon,), lambda k: (0, 0, 0)),
            pl.BlockSpec((1, lat_rows, lon), lambda k: (k, 0, 0)),
        ],
        out_specs=row,
        scratch_shapes=[pltpu.VMEM((7, lat_rows, levels, lon), jnp.float32)],
    )
    return pl.pallas_call(
        kernel,
        grid_spec=grid_spec,
        out_shape=jax.ShapeDtypeStruct(state.shape, state.dtype),
        compiler_params=pltpu.CompilerParams(dimension_semantics=("arbitrary",)),
    )(north_open, state, weather, emission)


def edge_kernel(north_ref, lo_ref, hi_ref, lo_in_ref, hi_in_ref, qs_ref, qn_ref, *rest):
    met_refs, src_ref, outs = rest[:8], rest[8], rest[9:]
    split = len(outs) == 2
    if not split:
        o_hbm, stage, sems = outs
    tracers, lat_rows = src_ref.shape[0], src_ref.shape[1]
    levels, lon = lo_ref.shape[1], lo_ref.shape[2]
    level = lax.broadcasted_iota(jnp.int32, (levels, lon), 0)
    not_top = level < levels - 1
    not_bottom = level > 0
    last = lat_rows - 1
    for top in (0, 1):
        a = top * last
        u_ref, v_ref, vm_ref, w_ref = met_refs[4 * top : 4 * top + 4]
        u = u_ref[0]
        uw = pltpu.roll(u, 1, 1)
        v = v_ref[0] * north_ref[a]
        vm = vm_ref[0]
        w = w_ref[0]
        w_up = jnp.where(not_top, w, 0.0)
        w_down = jnp.where(not_bottom, pltpu.roll(w, 1, 0), 0.0)
        c_self = (
            1.0
            - jnp.maximum(u, 0.0)
            + jnp.minimum(uw, 0.0)
            - jnp.maximum(v, 0.0)
            + jnp.minimum(vm, 0.0)
            - w_up
            - w_down
        )
        c_east = -jnp.minimum(u, 0.0)
        c_west = jnp.maximum(uw, 0.0)
        c_north = -jnp.minimum(v, 0.0)
        c_south = jnp.maximum(vm, 0.0)
        for k in range(tracers):
            qa = hi_ref[k] if top else lo_ref[k]
            inner = hi_in_ref[k] if top else lo_in_ref[k]
            qm = inner if top else qs_ref[k]
            qp = qn_ref[k] if top else inner
            result = (
                c_self * qa
                + c_east * pltpu.roll(qa, lon - 1, 1)
                + c_west * pltpu.roll(qa, 1, 1)
                + c_north * qp
                + c_south * qm
                + w_up * pltpu.roll(qa, levels - 1, 0)
                + w_down * pltpu.roll(qa, 1, 0)
            )
            surface = result[0:1] + src_ref[k, a : a + 1, :]
            target = outs[top].at[k] if split else stage.at[top, k, 0]
            target[...] = result
            target[0:1, :] = surface
    if not split:
        copies = [
            pltpu.make_async_copy(stage.at[top], o_hbm.at[:, pl.ds(top * last, 1)], sems.at[top])
            for top in (0, 1)
        ]
        for copy in copies:
            copy.start()
        for copy in copies:
            copy.wait()


def edge_step(rows, base, south, north, weather, merid_south, emission, north_open):
    tracers, levels, lon = rows[0].shape
    lat_rows = emission.shape[1]
    whole = pl.BlockSpec((tracers, levels, lon), lambda i: (0, 0, 0))
    in_specs = [pl.BlockSpec(memory_space=pltpu.SMEM)] + [whole] * 6
    last = lat_rows - 1
    met_rows = []
    for a, below in ((0, (merid_south, 0)), (last, (weather, lat_rows + last - 1))):
        met_rows += [(weather, a), (weather, lat_rows + a), below, (weather, 2 * lat_rows + a)]
    in_specs += [pl.BlockSpec((1, levels, lon), lambda i, r=r: (r, 0, 0)) for _, r in met_rows]
    in_specs += [pl.BlockSpec(emission.shape, lambda i: (0, 0, 0))]
    args = [north_open, *rows, south, north] + [m for m, _ in met_rows] + [emission]
    edge = pl.BlockSpec((tracers, levels, lon), lambda i: (0, 0, 0))
    scratch = []
    if base is None:
        out_specs = [edge, edge]
        out_shape = [jax.ShapeDtypeStruct((tracers, levels, lon), jnp.float32)] * 2
        aliases = {}
        kernel = edge_kernel
    else:
        in_specs.append(pl.BlockSpec(memory_space=pl.ANY))
        args.append(base)
        out_specs = pl.BlockSpec(memory_space=pl.ANY)
        out_shape = jax.ShapeDtypeStruct(base.shape, base.dtype)
        aliases = {len(args) - 1: 0}
        scratch = [pltpu.VMEM((2, tracers, 1, levels, lon), jnp.float32), pltpu.SemaphoreType.DMA((2,))]
        kernel = lambda *refs: edge_kernel(*refs[:16], *refs[17:])
    grid_spec = pltpu.PrefetchScalarGridSpec(
        num_scalar_prefetch=0, grid=(1,), in_specs=in_specs, out_specs=out_specs, scratch_shapes=scratch
    )
    return pl.pallas_call(
        kernel,
        grid_spec=grid_spec,
        out_shape=out_shape,
        input_output_aliases=aliases,
    )(*args)


def fused_kernel(north_ref, q_ref, lo_ref, hi_ref, wx_ref, src_ref, o_ref, lo_in_ref, hi_in_ref, coef_ref, mid_ref):
    lat_rows = q_ref.shape[1]
    levels, lon = q_ref.shape[2], q_ref.shape[3]

    @pl.when(pl.program_id(0) == 0)
    def _():
        fill_coefficients(north_ref, wx_ref, coef_ref, range(1, lat_rows - 1))

    def stencil(a, qa, qm, qp):
        result = (
            coef_ref[0, a] * qa
            + coef_ref[1, a] * pltpu.roll(qa, lon - 1, 1)
            + coef_ref[2, a] * pltpu.roll(qa, 1, 1)
            + coef_ref[3, a] * qp
            + coef_ref[4, a] * qm
            + coef_ref[5, a] * pltpu.roll(qa, levels - 1, 0)
            + coef_ref[6, a] * pltpu.roll(qa, 1, 0)
        )
        return result, result[0:1] + src_ref[0, a : a + 1, :]

    mid_ref[0] = lo_ref[0]
    mid_ref[lat_rows - 1] = hi_ref[0]
    for a in range(1, lat_rows - 1):
        result, surface = stencil(a, q_ref[0, a], q_ref[0, a - 1], q_ref[0, a + 1])
        mid_ref[a] = result
        mid_ref[a, 0:1, :] = surface
        if a == 1:
            lo_in_ref[0] = mid_ref[a]
        if a == lat_rows - 2:
            hi_in_ref[0] = mid_ref[a]
    for a in range(1, lat_rows - 1):
        result, surface = stencil(a, mid_ref[a], mid_ref[a - 1], mid_ref[a + 1])
        o_ref[0, a] = result
        o_ref[0, a, 0:1, :] = surface


def fused_steps(state, lo, hi, weather, emission, north_open):
    tracers, lat_rows, levels, lon = state.shape
    row = pl.BlockSpec((1, lat_rows, levels, lon), lambda k: (k, 0, 0, 0))
    edge = pl.BlockSpec((1, levels, lon), lambda k: (k, 0, 0))
    grid_spec = pltpu.PrefetchScalarGridSpec(
        num_scalar_prefetch=0,
        grid=(tracers,),
        in_specs=[
            pl.BlockSpec(memory_space=pltpu.SMEM),
            row,
            edge,
            edge,
            pl.BlockSpec(weather.shape[:2] + (lon,), lambda k: (0, 0, 0)),
            pl.BlockSpec((1, lat_rows, lon), lambda k: (k, 0, 0)),
        ],
        out_specs=[row, edge, edge],
        scratch_shapes=[
            pltpu.VMEM((7, lat_rows, levels, lon), jnp.float32),
            pltpu.VMEM((lat_rows, levels, lon), jnp.float32),
        ],
    )
    return pl.pallas_call(
        fused_kernel,
        grid_spec=grid_spec,
        out_shape=[jax.ShapeDtypeStruct(state.shape, state.dtype)]
        + [jax.ShapeDtypeStruct((tracers, levels, lon), state.dtype)] * 2,
        compiler_params=pltpu.CompilerParams(dimension_semantics=("arbitrary",)),
    )(north_open, state, lo, hi, weather, emission)


def on_device(
    tracer_state,
    control,
    prior_tiles,
    tile_index,
    region_map,
    region_sigma,
    zonal_courant,
    meridional_courant,
    vertical_diffusion,
):
    band_count = lax.axis_size("band")
    band_index = lax.axis_index("band")
    tiles_count = prior_tiles.shape[0]
    lat_rows = control.shape[1]

    latitude = band_index * lat_rows + jnp.arange(lat_rows, dtype=jnp.int32)
    north_open = (latitude < band_count * lat_rows - 1).astype(jnp.float32)
    choose = (
        tile_index[:, :, None] == lax.broadcasted_iota(jnp.int32, (1, 1, tiles_count), 2)
    ).astype(jnp.float32)
    own_row = lax.dynamic_slice_in_dim(choose, band_index, 1, 0)[0]
    row_tiles = jnp.einsum("bt,tmn->bmn", own_row, prior_tiles, precision=exact_dot)
    own_tile = lax.dynamic_index_in_dim(row_tiles, band_index, 0, keepdims=False)
    prior_field = jnp.einsum("jm,kmn->kjn", own_tile, control, precision=exact_dot)
    parts, (north_open, row_tiles, prior_field) = lax.optimization_barrier(
        ((zonal_courant, meridional_courant, vertical_diffusion), (north_open, row_tiles, prior_field))
    )
    pack = packed(list(parts))
    weather = relay_gather(pack, "tracer")
    tracer_count = lax.axis_size("tracer")
    me = lax.axis_index("tracer")
    chunk = meridional_courant.shape[2]
    merid_south = jnp.zeros((1,) + meridional_courant.shape[1:2] + (tracer_count * chunk,), jnp.float32)
    for s in range(tracer_count):
        pairs = [
            (t * band_count + b, ((t + s) % tracer_count) * band_count + b + 1)
            for t in range(tracer_count)
            for b in range(band_count - 1)
        ]
        part = lax.ppermute(meridional_courant[-1:], ("tracer", "band"), pairs)
        merid_south = lax.dynamic_update_slice(merid_south, part, (0, 0, ((me - s) % tracer_count) * chunk))
    held_state, held_control, _ = lax.optimization_barrier((tracer_state, control, pack))
    q_south = passed_along(held_state[:, -1], "band", 1)
    q_north = passed_along(held_state[:, 0], "band", -1)
    for s in range(1, band_count):
        pairs = [(i, (i + s) % band_count) for i in range(band_count)]
        part = lax.ppermute(held_control, "band", pairs)
        source_band = (band_index - s) % band_count
        tile = lax.dynamic_index_in_dim(row_tiles, source_band, 0, keepdims=False)
        prior_field = prior_field + jnp.einsum("jm,kmn->kjn", tile, part, precision=exact_dot)
    regions = region_sigma.shape[1]
    onehot = (region_map[:, :, None] == lax.broadcasted_iota(jnp.int32, (1, 1, regions), 2)).astype(
        jnp.float32
    )
    cell_sigma = jnp.einsum("kr,jnr->kjn", region_sigma, onehot, precision=exact_dot)
    emission = cell_sigma * prior_field

    rim = (tracer_state[:, 0], tracer_state[:, lat_rows - 1], tracer_state[:, 1], tracer_state[:, lat_rows - 2])
    bottom_row, top_row = edge_step(rim, None, q_south, q_north, weather, merid_south, emission, north_open)
    s1_south = passed_along(top_row, "band", 1)
    s1_north = passed_along(bottom_row, "band", -1)
    inside, bottom_in, top_in = fused_steps(tracer_state, bottom_row, top_row, weather, emission, north_open)
    rim = (bottom_row, top_row, bottom_in, top_in)
    tracer_field = edge_step(rim, inside, s1_south, s1_north, weather, merid_south, emission, north_open)
    return (tracer_field, emission)


def solution(mesh):
    in_specs = (
        P(("inv", "tracer"), "band", None, None),
        P(("inv", "tracer"), "band", None),
        P(),
        P(),
        P("band", None),
        P("tracer", None),
        P(("inv", "band"), None, "tracer"),
        P(("inv", "band"), None, "tracer"),
        P(("inv", "band"), None, "tracer"),
    )
    out_specs = (P(("inv", "tracer"), "band", None, None), P(("inv", "tracer"), "band", None))
    return jax.shard_map(
        on_device, mesh=mesh, in_specs=in_specs, out_specs=out_specs, check_vma=False
    )
```

```python
import functools

import jax
import jax.numpy as jnp
from jax import lax
from jax.experimental import pallas as pl
from jax.experimental.pallas import tpu as pltpu
from jax.sharding import PartitionSpec as P

exact_dot = lax.Precision.HIGHEST


def passed_along(value, axis, by):
    count = lax.axis_size(axis)
    pairs = [(i, i + by) for i in range(count) if 0 <= i + by < count]
    return lax.ppermute(value, axis, pairs)


def pack_kernel(*refs):
    parts, out_ref = refs[:-1], refs[-1]
    row = 0
    for part in parts:
        rows = part.shape[0]
        out_ref[row : row + rows] = part[...]
        row += rows


def packed(parts):
    rows = sum(part.shape[0] for part in parts)
    return pl.pallas_call(
        pack_kernel,
        out_shape=jax.ShapeDtypeStruct((rows,) + parts[0].shape[1:], parts[0].dtype),
    )(*parts)


def relay_gather(x, axis):
    count = lax.axis_size(axis)
    me = lax.axis_index(axis)
    rows, levels, width = x.shape
    buf = jnp.zeros((rows, levels, (count + 1) * width), x.dtype)
    buf = lax.dynamic_update_slice(buf, x, (0, 0, me * width))
    right = left = x
    for r in range(1, count):
        right = lax.ppermute(right, axis, [(i, i + 1) for i in range(r - 1, count - 1)])
        left = lax.ppermute(left, axis, [(j, j - 1) for j in range(1, count - r + 1)])
        slot = jnp.where(me - r >= 0, me - r, count)
        buf = lax.dynamic_update_slice(buf, right, (0, 0, slot * width))
        slot = jnp.where(me + r < count, me + r, count)
        buf = lax.dynamic_update_slice(buf, left, (0, 0, slot * width))
    return buf


def fill_coefficients(north_ref, wx_ref, coef_ref):
    lat_rows = coef_ref.shape[1]
    levels, lon = coef_ref.shape[2], coef_ref.shape[3]
    level = lax.broadcasted_iota(jnp.int32, (levels, lon), 0)
    not_top = level < levels - 1
    not_bottom = level > 0
    for a in range(lat_rows):
        u = wx_ref[a]
        uw = pltpu.roll(u, 1, 1)
        v = wx_ref[lat_rows + a] * north_ref[a]
        vm = wx_ref[3 * lat_rows] if a == 0 else wx_ref[lat_rows + a - 1]
        w = wx_ref[2 * lat_rows + a]
        w_up = jnp.where(not_top, w, 0.0)
        w_down = jnp.where(not_bottom, pltpu.roll(w, 1, 0), 0.0)
        coef_ref[0, a] = (
            1.0
            - jnp.maximum(u, 0.0)
            + jnp.minimum(uw, 0.0)
            - jnp.maximum(v, 0.0)
            + jnp.minimum(vm, 0.0)
            - w_up
            - w_down
        )
        coef_ref[1, a] = -jnp.minimum(u, 0.0)
        coef_ref[2, a] = jnp.maximum(uw, 0.0)
        coef_ref[3, a] = -jnp.minimum(v, 0.0)
        coef_ref[4, a] = jnp.maximum(vm, 0.0)
        coef_ref[5, a] = w_up
        coef_ref[6, a] = w_down


def step_kernel(north_ref, q_ref, qs_ref, qn_ref, wx_ref, src_ref, *rest, rows=None):
    o_ref = rest[0]
    edges = rest[1:-1]
    coef_ref = rest[-1]
    lat_rows = q_ref.shape[1]
    rows = range(lat_rows) if rows is None else rows
    levels, lon = q_ref.shape[2], q_ref.shape[3]
    level = lax.broadcasted_iota(jnp.int32, (levels, lon), 0)
    not_top = level < levels - 1
    not_bottom = level > 0

    @pl.when(pl.program_id(0) == 0)
    def _():
        fill_coefficients(north_ref, wx_ref, coef_ref)

    for a in rows:
        qa = q_ref[0, a]
        qm = qs_ref[0] if a == 0 else q_ref[0, a - 1]
        qp = qn_ref[0] if a == lat_rows - 1 else q_ref[0, a + 1]
        result = (
            coef_ref[0, a] * qa
            + coef_ref[1, a] * pltpu.roll(qa, lon - 1, 1)
            + coef_ref[2, a] * pltpu.roll(qa, 1, 1)
            + coef_ref[3, a] * qp
            + coef_ref[4, a] * qm
            + coef_ref[5, a] * pltpu.roll(qa, levels - 1, 0)
            + coef_ref[6, a] * pltpu.roll(qa, 1, 0)
        )
        surface = result[0:1] + src_ref[0, a : a + 1, :]
        targets = [o_ref.at[0, a]]
        if edges and a == 0:
            targets.append(edges[0].at[0])
        if edges and a == lat_rows - 1:
            targets.append(edges[1].at[0])
        for target in targets:
            target[...] = result
            target[0:1, :] = surface


def advance(state, south, north, weather, emission, north_open, with_edges):
    tracers, lat_rows, levels, lon = state.shape
    row = pl.BlockSpec((1, lat_rows, levels, lon), lambda k: (k, 0, 0, 0))
    edge = pl.BlockSpec((1, levels, lon), lambda k: (k, 0, 0))
    out_specs = [row]
    out_shape = [jax.ShapeDtypeStruct(state.shape, state.dtype)]
    if with_edges:
        out_specs += [edge, edge]
        out_shape += [jax.ShapeDtypeStruct((tracers, levels, lon), state.dtype)] * 2
    grid_spec = pltpu.PrefetchScalarGridSpec(
        num_scalar_prefetch=0,
        grid=(tracers,),
        in_specs=[
            pl.BlockSpec(memory_space=pltpu.SMEM),
            row,
            edge,
            edge,
            pl.BlockSpec(weather.shape[:2] + (lon,), lambda k: (0, 0, 0)),
            pl.BlockSpec((1, lat_rows, lon), lambda k: (k, 0, 0)),
        ],
        out_specs=out_specs,
        scratch_shapes=[pltpu.VMEM((7, lat_rows, levels, lon), jnp.float32)],
    )
    return pl.pallas_call(
        step_kernel,
        grid_spec=grid_spec,
        out_shape=out_shape,
        compiler_params=pltpu.CompilerParams(dimension_semantics=("arbitrary",)),
    )(north_open, state, south, north, weather, emission)


def interior_step(state, weather, emission, north_open):
    tracers, lat_rows, levels, lon = state.shape
    row = pl.BlockSpec((1, lat_rows, levels, lon), lambda k: (k, 0, 0, 0))
    kernel = functools.partial(
        lambda n, q, w, e, o, c, rows: step_kernel(n, q, None, None, w, e, o, c, rows=rows),
        rows=range(1, lat_rows - 1),
    )
    grid_spec = pltpu.PrefetchScalarGridSpec(
        num_scalar_prefetch=0,
        grid=(tracers,),
        in_specs=[
            pl.BlockSpec(memory_space=pltpu.SMEM),
            row,
            pl.BlockSpec(weather.shape[:2] + (lon,), lambda k: (0, 0, 0)),
            pl.BlockSpec((1, lat_rows, lon), lambda k: (k, 0, 0)),
        ],
        out_specs=row,
        scratch_shapes=[pltpu.VMEM((7, lat_rows, levels, lon), jnp.float32)],
    )
    return pl.pallas_call(
        kernel,
        grid_spec=grid_spec,
        out_shape=jax.ShapeDtypeStruct(state.shape, state.dtype),
        compiler_params=pltpu.CompilerParams(dimension_semantics=("arbitrary",)),
    )(north_open, state, weather, emission)


def edge_kernel(north_ref, lo_ref, hi_ref, lo_in_ref, hi_in_ref, qs_ref, qn_ref, *rest):
    met_refs, src_ref, outs = rest[:8], rest[8], rest[9:]
    split = len(outs) == 2
    if not split:
        o_hbm, stage, sems = outs
    tracers, lat_rows = src_ref.shape[0], src_ref.shape[1]
    levels, lon = lo_ref.shape[1], lo_ref.shape[2]
    level = lax.broadcasted_iota(jnp.int32, (levels, lon), 0)
    not_top = level < levels - 1
    not_bottom = level > 0
    last = lat_rows - 1
    for top in (0, 1):
        a = top * last
        u_ref, v_ref, vm_ref, w_ref = met_refs[4 * top : 4 * top + 4]
        u = u_ref[0]
        uw = pltpu.roll(u, 1, 1)
        v = v_ref[0] * north_ref[a]
        vm = vm_ref[0]
        w = w_ref[0]
        w_up = jnp.where(not_top, w, 0.0)
        w_down = jnp.where(not_bottom, pltpu.roll(w, 1, 0), 0.0)
        c_self = (
            1.0
            - jnp.maximum(u, 0.0)
            + jnp.minimum(uw, 0.0)
            - jnp.maximum(v, 0.0)
            + jnp.minimum(vm, 0.0)
            - w_up
            - w_down
        )
        c_east = -jnp.minimum(u, 0.0)
        c_west = jnp.maximum(uw, 0.0)
        c_north = -jnp.minimum(v, 0.0)
        c_south = jnp.maximum(vm, 0.0)
        for k in range(tracers):
            qa = hi_ref[k] if top else lo_ref[k]
            inner = hi_in_ref[k] if top else lo_in_ref[k]
            qm = inner if top else qs_ref[k]
            qp = qn_ref[k] if top else inner
            result = (
                c_self * qa
                + c_east * pltpu.roll(qa, lon - 1, 1)
                + c_west * pltpu.roll(qa, 1, 1)
                + c_north * qp
                + c_south * qm
                + w_up * pltpu.roll(qa, levels - 1, 0)
                + w_down * pltpu.roll(qa, 1, 0)
            )
            surface = result[0:1] + src_ref[k, a : a + 1, :]
            target = outs[top].at[k] if split else stage.at[top, k, 0]
            target[...] = result
            target[0:1, :] = surface
    if not split:
        copies = [
            pltpu.make_async_copy(stage.at[top], o_hbm.at[:, pl.ds(top * last, 1)], sems.at[top])
            for top in (0, 1)
        ]
        for copy in copies:
            copy.start()
        for copy in copies:
            copy.wait()


def edge_step(rows, base, south, north, weather, emission, north_open):
    tracers, levels, lon = rows[0].shape
    lat_rows = emission.shape[1]
    whole = pl.BlockSpec((tracers, levels, lon), lambda i: (0, 0, 0))
    in_specs = [pl.BlockSpec(memory_space=pltpu.SMEM)] + [whole] * 6
    last = lat_rows - 1
    met_rows = []
    for a, below in ((0, 3 * lat_rows), (last, lat_rows + last - 1)):
        met_rows += [a, lat_rows + a, below, 2 * lat_rows + a]
    in_specs += [pl.BlockSpec((1, levels, lon), lambda i, r=r: (r, 0, 0)) for r in met_rows]
    in_specs += [pl.BlockSpec(emission.shape, lambda i: (0, 0, 0))]
    args = [north_open, *rows, south, north] + [weather] * len(met_rows) + [emission]
    edge = pl.BlockSpec((tracers, levels, lon), lambda i: (0, 0, 0))
    scratch = []
    if base is None:
        out_specs = [edge, edge]
        out_shape = [jax.ShapeDtypeStruct((tracers, levels, lon), jnp.float32)] * 2
        aliases = {}
        kernel = edge_kernel
    else:
        in_specs.append(pl.BlockSpec(memory_space=pl.ANY))
        args.append(base)
        out_specs = pl.BlockSpec(memory_space=pl.ANY)
        out_shape = jax.ShapeDtypeStruct(base.shape, base.dtype)
        aliases = {len(args) - 1: 0}
        scratch = [pltpu.VMEM((2, tracers, 1, levels, lon), jnp.float32), pltpu.SemaphoreType.DMA((2,))]
        kernel = lambda *refs: edge_kernel(*refs[:16], *refs[17:])
    grid_spec = pltpu.PrefetchScalarGridSpec(
        num_scalar_prefetch=0, grid=(1,), in_specs=in_specs, out_specs=out_specs, scratch_shapes=scratch
    )
    return pl.pallas_call(
        kernel,
        grid_spec=grid_spec,
        out_shape=out_shape,
        input_output_aliases=aliases,
    )(*args)


def fused_kernel(north_ref, q_ref, lo_ref, hi_ref, wx_ref, src_ref, o_ref, lo_in_ref, hi_in_ref, coef_ref, mid_ref):
    lat_rows = q_ref.shape[1]
    levels, lon = q_ref.shape[2], q_ref.shape[3]
    group = q_ref.shape[0]

    @pl.when(pl.program_id(0) == 0)
    def _():
        fill_coefficients(north_ref, wx_ref, coef_ref)

    def stencil(t, a, qa, qm, qp):
        result = (
            coef_ref[0, a] * qa
            + coef_ref[1, a] * pltpu.roll(qa, lon - 1, 1)
            + coef_ref[2, a] * pltpu.roll(qa, 1, 1)
            + coef_ref[3, a] * qp
            + coef_ref[4, a] * qm
            + coef_ref[5, a] * pltpu.roll(qa, levels - 1, 0)
            + coef_ref[6, a] * pltpu.roll(qa, 1, 0)
        )
        return result, result[0:1] + src_ref[t, a : a + 1, :]

    for t in range(group):
        mid_ref[0] = lo_ref[t]
        mid_ref[lat_rows - 1] = hi_ref[t]
        for a in range(1, lat_rows - 1):
            result, surface = stencil(t, a, q_ref[t, a], q_ref[t, a - 1], q_ref[t, a + 1])
            mid_ref[a] = result
            mid_ref[a, 0:1, :] = surface
            if a == 1:
                lo_in_ref[t] = mid_ref[a]
            if a == lat_rows - 2:
                hi_in_ref[t] = mid_ref[a]
        for a in range(1, lat_rows - 1):
            result, surface = stencil(t, a, mid_ref[a], mid_ref[a - 1], mid_ref[a + 1])
            o_ref[t, a] = result
            o_ref[t, a, 0:1, :] = surface


def fused_steps(state, lo, hi, weather, emission, north_open):
    tracers, lat_rows, levels, lon = state.shape
    group = 2 if tracers % 2 == 0 else 1
    row = pl.BlockSpec((group, lat_rows, levels, lon), lambda k: (k, 0, 0, 0))
    edge = pl.BlockSpec((group, levels, lon), lambda k: (k, 0, 0))
    grid_spec = pltpu.PrefetchScalarGridSpec(
        num_scalar_prefetch=0,
        grid=(tracers // group,),
        in_specs=[
            pl.BlockSpec(memory_space=pltpu.SMEM),
            row,
            edge,
            edge,
            pl.BlockSpec(weather.shape[:2] + (lon,), lambda k: (0, 0, 0)),
            pl.BlockSpec((group, lat_rows, lon), lambda k: (k, 0, 0)),
        ],
        out_specs=[row, edge, edge],
        scratch_shapes=[
            pltpu.VMEM((7, lat_rows, levels, lon), jnp.float32),
            pltpu.VMEM((lat_rows, levels, lon), jnp.float32),
        ],
    )
    return pl.pallas_call(
        fused_kernel,
        grid_spec=grid_spec,
        out_shape=[jax.ShapeDtypeStruct(state.shape, state.dtype)]
        + [jax.ShapeDtypeStruct((tracers, levels, lon), state.dtype)] * 2,
        compiler_params=pltpu.CompilerParams(dimension_semantics=("arbitrary",)),
    )(north_open, state, lo, hi, weather, emission)


def on_device(
    tracer_state,
    control,
    prior_tiles,
    tile_index,
    region_map,
    region_sigma,
    zonal_courant,
    meridional_courant,
    vertical_diffusion,
):
    band_count = lax.axis_size("band")
    band_index = lax.axis_index("band")
    tiles_count = prior_tiles.shape[0]
    lat_rows = control.shape[1]

    latitude = band_index * lat_rows + jnp.arange(lat_rows, dtype=jnp.int32)
    north_open = (latitude < band_count * lat_rows - 1).astype(jnp.float32)
    choose = (
        tile_index[:, :, None] == lax.broadcasted_iota(jnp.int32, (1, 1, tiles_count), 2)
    ).astype(jnp.float32)
    own_row = lax.dynamic_slice_in_dim(choose, band_index, 1, 0)[0]
    row_tiles = jnp.einsum("bt,tmn->bmn", own_row, prior_tiles, precision=exact_dot)
    own_tile = lax.dynamic_index_in_dim(row_tiles, band_index, 0, keepdims=False)
    prior_field = jnp.einsum("jm,kmn->kjn", own_tile, control, precision=exact_dot)
    south_v = passed_along(meridional_courant[-1:], "band", 1)
    parts, (north_open, row_tiles, prior_field) = lax.optimization_barrier(
        ((zonal_courant, meridional_courant, vertical_diffusion, south_v), (north_open, row_tiles, prior_field))
    )
    pack = packed(list(parts))
    weather = relay_gather(pack, "tracer")
    held_state, held_control, _ = lax.optimization_barrier((tracer_state, control, pack))
    q_south = passed_along(held_state[:, -1], "band", 1)
    q_north = passed_along(held_state[:, 0], "band", -1)
    for s in range(1, band_count):
        pairs = [(i, (i + s) % band_count) for i in range(band_count)]
        part = lax.ppermute(held_control, "band", pairs)
        source_band = (band_index - s) % band_count
        tile = lax.dynamic_index_in_dim(row_tiles, source_band, 0, keepdims=False)
        prior_field = prior_field + jnp.einsum("jm,kmn->kjn", tile, part, precision=exact_dot)
    regions = region_sigma.shape[1]
    onehot = (region_map[:, :, None] == lax.broadcasted_iota(jnp.int32, (1, 1, regions), 2)).astype(
        jnp.float32
    )
    cell_sigma = jnp.einsum("kr,jnr->kjn", region_sigma, onehot, precision=exact_dot)
    emission = cell_sigma * prior_field

    rim = (tracer_state[:, 0], tracer_state[:, lat_rows - 1], tracer_state[:, 1], tracer_state[:, lat_rows - 2])
    bottom_row, top_row = edge_step(rim, None, q_south, q_north, weather, emission, north_open)
    s1_south = passed_along(top_row, "band", 1)
    s1_north = passed_along(bottom_row, "band", -1)
    inside, bottom_in, top_in = fused_steps(tracer_state, bottom_row, top_row, weather, emission, north_open)
    rim = (bottom_row, top_row, bottom_in, top_in)
    tracer_field = edge_step(rim, inside, s1_south, s1_north, weather, emission, north_open)
    return (tracer_field, emission)


def solution(mesh):
    in_specs = (
        P(("inv", "tracer"), "band", None, None),
        P(("inv", "tracer"), "band", None),
        P(),
        P(),
        P("band", None),
        P("tracer", None),
        P(("inv", "band"), None, "tracer"),
        P(("inv", "band"), None, "tracer"),
        P(("inv", "band"), None, "tracer"),
    )
    out_specs = (P(("inv", "tracer"), "band", None, None), P(("inv", "tracer"), "band", None))
    return jax.shard_map(
        on_device, mesh=mesh, in_specs=in_specs, out_specs=out_specs, check_vma=False
    )
```
